512 devices in a mesh: grp: 32 (over x, y), tp: 16 (over z, core).
Axes of the slice: x: 4, y: 8, z: 8, core: 2. Of those that a mesh axis runs over, the one named last changes fastest.
Arguments:
- patches: bfloat16 [16384, 1664], P('grp'), may hold values from -6 to 6
- patch_image: int32 [16384], P('grp'), may hold values from 0 to 4095, as said below
- vis_gain: float32 [1664], replicated, may hold values from 0.25 to 1.75
- vis_bias: float32 [1664], replicated, may hold values from -3 to 3
- vis_qkv: bfloat16 [3, 1664, 1664], P(None, None, 'tp'), may hold values from -2 to 2
- vis_out: bfloat16 [1664, 1664], P('tp'), may hold values from -0.15625 to 0.15625
- merge_weight: bfloat16 [4, 1664, 1024], P(None, 'tp'), may hold values from -0.078125 to 0.078125
- positions: int32 [4096], P('grp'), may hold values from 0 to 12287, as said below
- text: bfloat16 [8192, 1024], P('grp'), may hold values from -6 to 6
- dec_gain: float32 [1024], replicated, may hold values from 0.25 to 1.75
- dec_bias: float32 [1024], replicated, may hold values from -3 to 3
- dec_qkv: bfloat16 [3, 1024, 1024], P(None, None, 'tp'), may hold values from -2 to 2
Outputs:
- dec_attn: bfloat16 [12288, 1024], P('grp', 'tp')
The draws below stay inside these ranges and needn't reach their ends.
Inputs may be any that keep to these rules, and one draw needn't show every extreme that they name: `patch_image`: each aligned run of four patches belongs to one image. Groups 2j and 2j+1 are partners: the last image of group 2j continues as the first image of group 2j+1; no other image is shared between groups. All positions are distinct; each group's block of 384 positions holds exactly 128 of them; the 128 merged rows of one group put at most 8 positions into any one group's block.
All inputs are finite; a program needn't handle non-finite values.
Results may differ from the reference program's by a relative error of at most 0.025.
Values may be sent and summed in bfloat16 or wider, within the bound.
No kernel may reach another device: no remote copies, remote signals or barrier semaphores. Data moves between devices by JAX's collectives and lax.ppermute only.
A program may use at most 128 MiB of HBM per device.

```python
import jax
import jax.numpy as jnp
from jax import lax

D = 1664
HEADS = 16
HD = 104
DEC = 1024
DHEADS = 16
DH = 64
P_GRP = 512
TXT_GRP = 256
M_GRP = 128
TOK_GRP = 384
SEQ = 12288
CAP = 8
N_GRP = 32


def drawn_rows(key, salt, rows, width):
    own = jax.random.fold_in(key, salt)
    values = jnp.clip(jax.random.normal(own, (rows, width), jnp.float32), -6.0, 6.0)
    return values.astype(jnp.bfloat16)


def drawn_weights(key, salt, width, heads, head):
    own = jax.random.fold_in(key, salt)
    base = jnp.clip(jax.random.normal(own, (3, width, heads * head), jnp.float32), -4.0, 4.0) * width ** (-0.5)
    return base.astype(jnp.bfloat16)


def draw_patches(key, part):
    return drawn_rows(key, 11, N_GRP * P_GRP, D)


def draw_text(key, part):
    return drawn_rows(key, 12, N_GRP * TXT_GRP, DEC)


def draw_vis_qkv(key, part):
    return drawn_weights(key, 31, D, HEADS, HD)


def draw_dec_qkv(key, part):
    return drawn_weights(key, 32, DEC, DHEADS, DH)


def draw_patch_image(key, part):
    pairs = N_GRP // 2
    rolls = jax.random.randint(key, (pairs, 2 * M_GRP), 0, 12)
    starts = (rolls == 0).astype(jnp.int32)
    reach = jax.random.randint(jax.random.fold_in(key, 5), (pairs, 1), 0, M_GRP - 1)
    column = jnp.arange(2 * M_GRP)[None, :]
    inside = (column >= M_GRP) & (column <= M_GRP + reach)
    fresh = column == M_GRP + 1 + reach
    starts = jnp.where(column == 0, 1, jnp.where(fresh, 1, jnp.where(inside, 0, starts)))
    local = jnp.cumsum(starts, axis=1) - 1
    total = jnp.sum(starts, axis=1, keepdims=True)
    base = (jnp.arange(pairs) * (2 * M_GRP))[:, None]
    ident = jnp.where(local == total - 1, base + 2 * M_GRP - 1, base + local)
    return jnp.repeat(ident.reshape(-1), 4).astype(jnp.int32)


def draw_positions(key, part):
    spread = min(N_GRP, 16)
    shifts = jax.random.permutation(jax.random.fold_in(key, 1), N_GRP)[:spread]
    slot_key = jax.random.fold_in(key, 2)
    order_key = jax.random.fold_in(key, 3)
    slots = jax.vmap(lambda d: jax.random.permutation(jax.random.fold_in(slot_key, d), TOK_GRP)[:M_GRP])(jnp.arange(N_GRP))
    order = jax.vmap(lambda g: jax.random.permutation(jax.random.fold_in(order_key, g), M_GRP))(jnp.arange(N_GRP))
    block = jnp.arange(M_GRP) // CAP
    target = (jnp.arange(N_GRP)[:, None] + shifts[block][None, :]) % N_GRP
    within = jnp.broadcast_to(jnp.arange(M_GRP)[None, :], (N_GRP, M_GRP))
    values = target * TOK_GRP + slots[target, within]
    result = jnp.take_along_axis(values, order, axis=1)
    return result.reshape(-1).astype(jnp.int32)


def level_of(key, shape, cuts, smallest, top_value):
    factor_of, own = 1.0, jax.random.fold_in(key, 6)
    for position, shards_of in cuts:
        draws = jnp.exp(jax.random.uniform(jax.random.fold_in(own, position), (shards_of,), jnp.float32, smallest / len(cuts), top_value / len(cuts)))
        factor_of = factor_of * jnp.repeat(draws, shape[position] // shards_of).reshape([-1 if axis == position else 1 for axis in range(len(shape))])
    return factor_of


def scatter_about(rng, dims, scale, most, shards=(), held_as=jnp.bfloat16):
    values = jax.random.normal(rng, dims, jnp.float32) * scale
    if len(shards) > 0:
        values = level_of(rng, dims, shards, -0.22, 0.18) * values
    return jnp.clip(values, min=-most, max=most).astype(held_as)


def setup_inputs(seed: int = 0) -> dict:
    streams_of = jax.random.split(jax.random.key(seed), 13)
    patches = draw_patches(jax.random.fold_in(streams_of[12], 71), 0)
    patch_image = draw_patch_image(jax.random.fold_in(streams_of[12], 71), 0)
    vis_gain = jnp.clip(1.0 + 0.15 * jax.random.normal(streams_of[2], (D,), jnp.float32), 0.25, 1.75)
    vis_bias = scatter_about(streams_of[3], (D,), 0.3, 3.0, (), jnp.float32)
    vis_qkv = draw_vis_qkv(jax.random.fold_in(streams_of[12], 71), 0)
    vis_out = scatter_about(streams_of[5], (HEADS * HD, D), (HEADS * HD) ** -0.5, 0.15625, ((0, 16),))
    merge_weight = scatter_about(streams_of[6], (4, D, DEC), (4 * D) ** -0.5, 0.078125, ((1, 16),))
    positions = draw_positions(jax.random.fold_in(streams_of[12], 71), 0)
    text = draw_text(jax.random.fold_in(streams_of[12], 71), 0)
    dec_gain = jnp.clip(1.0 + 0.15 * jax.random.normal(streams_of[9], (DEC,), jnp.float32), 0.25, 1.75)
    dec_bias = scatter_about(streams_of[10], (DEC,), 0.3, 3.0, (), jnp.float32)
    dec_qkv = draw_dec_qkv(jax.random.fold_in(streams_of[12], 71), 0)
    return {"patches": patches, "patch_image": patch_image, "vis_gain": vis_gain, "vis_bias": vis_bias, "vis_qkv": vis_qkv, "vis_out": vis_out, "merge_weight": merge_weight, "positions": positions, "text": text, "dec_gain": dec_gain, "dec_bias": dec_bias, "dec_qkv": dec_qkv}


layer_eps = 1e-05

def normalize(values, gain, bias):
    mean = lax.optimization_barrier(jnp.mean(values, axis=-1, keepdims=True))
    centred = values - mean
    spread = lax.optimization_barrier(jnp.mean(centred * centred, axis=-1, keepdims=True))
    return centred * lax.rsqrt(spread + layer_eps) * gain + bias

def reference(patches, patch_image, vis_gain, vis_bias, vis_qkv, vis_out, merge_weight, positions, text, dec_gain, dec_bias, dec_qkv):
    pairs = N_GRP // 2
    pair_rows = patches.reshape(pairs, 2 * P_GRP, D)
    pair_ids = patch_image.reshape(pairs, 2 * P_GRP)
    qkv_wide = vis_qkv.astype(jnp.float32)

    def one_pair(item):
        rows, ident = item
        rows_f = rows.astype(jnp.float32)
        normed = normalize(rows_f, vis_gain, vis_bias).astype(jnp.bfloat16)
        proj = jnp.einsum('pd,sde->spe', normed.astype(jnp.float32), qkv_wide).astype(jnp.bfloat16)
        query = proj[0].reshape(-1, HEADS, HD).astype(jnp.float32)
        keys = proj[1].reshape(-1, HEADS, HD).astype(jnp.float32)
        values = proj[2].reshape(-1, HEADS, HD).astype(jnp.float32)
        scores = jnp.einsum('phe,khe->hpk', query, keys) * HD ** (-0.5)
        same = ident[:, None] == ident[None, :]
        top = lax.optimization_barrier(jnp.max(jnp.where(same, scores, -1e+30), axis=2, keepdims=True))
        expo = jnp.where(same, jnp.exp(scores - top), 0.0)
        weights = (expo / lax.optimization_barrier(jnp.sum(expo, axis=2, keepdims=True))).astype(jnp.bfloat16)
        attended = jnp.einsum('hpk,khe->phe', weights.astype(jnp.float32), values).astype(jnp.bfloat16)
        attended = attended.reshape(-1, HEADS * HD)
        mixed = jnp.dot(attended, vis_out, preferred_element_type=jnp.float32)
        return (rows_f + mixed).astype(jnp.bfloat16)
    visual = lax.map(one_pair, (pair_rows, pair_ids)).reshape(N_GRP * P_GRP, D)
    merged = jnp.dot(visual.reshape(N_GRP * M_GRP, 4 * D), merge_weight.reshape(4 * D, DEC), preferred_element_type=jnp.float32).astype(jnp.bfloat16)
    prompt = jnp.zeros((SEQ, DEC), jnp.bfloat16).at[positions].set(merged)
    image_flag = jnp.zeros((SEQ,), jnp.int32).at[positions].set(1).reshape(N_GRP, TOK_GRP)
    text_slots = jnp.argsort(image_flag, axis=1, stable=True)[:, :TXT_GRP].astype(jnp.int32)
    text_slots = text_slots + (jnp.arange(N_GRP, dtype=jnp.int32) * TOK_GRP)[:, None]
    prompt = prompt.at[text_slots.reshape(-1)].set(text)
    dnorm = normalize(prompt.astype(jnp.float32), dec_gain, dec_bias).astype(jnp.bfloat16)
    dproj = jnp.einsum('td,sde->ste', dnorm.astype(jnp.float32), dec_qkv.astype(jnp.float32)).astype(jnp.bfloat16)
    dquery = dproj[0].reshape(SEQ, DHEADS, DH).transpose(1, 0, 2)
    dkeys = dproj[1].reshape(SEQ, DHEADS, DH).transpose(1, 0, 2)
    dvalues = dproj[2].reshape(SEQ, DHEADS, DH).transpose(1, 0, 2)
    order = jnp.arange(SEQ, dtype=jnp.int32)
    allowed = order[None, :] <= order[:, None]

    def one_head(item):
        query, keys, values = item
        scores = jnp.dot(query, keys.T, preferred_element_type=jnp.float32) * DH ** (-0.5)
        top = lax.optimization_barrier(jnp.max(jnp.where(allowed, scores, -1e+30), axis=1, keepdims=True))
        expo = jnp.where(allowed, jnp.exp(scores - top), 0.0)
        summed = jnp.dot(expo.astype(jnp.bfloat16), values, preferred_element_type=jnp.float32)
        return (summed / lax.optimization_barrier(jnp.sum(expo, axis=1, keepdims=True))).astype(jnp.bfloat16)
    heads_out = lax.map(one_head, (dquery, dkeys, dvalues))
    return heads_out.transpose(1, 0, 2).reshape(SEQ, DHEADS * DH)
```

```python
import jax
import jax.numpy as jnp
from jax import lax
from jax.sharding import PartitionSpec as P

HD = 104
DH = 64


layer_eps = 1e-05


def swapped(value, axis, stride):
    return lax.ppermute(value, axis, [(i, i ^ 1 << stride) for i in range(lax.axis_size(axis))])


def a2a_gather(value, axis):
    n = lax.axis_size(axis)
    spread = jnp.broadcast_to(value[None], (n,) + value.shape)
    got = lax.all_to_all(spread, axis, 0, 0, tiled=True)
    return got.reshape((n * value.shape[0],) + value.shape[1:])


def a2a_reduce_scatter(value, axis):
    n = lax.axis_size(axis)
    parts = value.reshape((n, value.shape[0] // n) + value.shape[1:])
    got = lax.all_to_all(parts, axis, 0, 0, tiled=True)
    return jnp.sum(got.astype(jnp.float32), axis=0)


def normalize(values, gain, bias):
    mean = jnp.mean(values, axis=-1, keepdims=True)
    centred = values - mean
    spread = jnp.mean(centred * centred, axis=-1, keepdims=True)
    return centred * lax.rsqrt(spread + layer_eps) * gain + bias


def body(
    patches,
    patch_image,
    vis_gain,
    vis_bias,
    vis_qkv,
    vis_out,
    merge_weight,
    positions,
    text,
    dec_gain,
    dec_bias,
    dec_qkv,
):
    rows = patches.shape[0]
    heads = vis_qkv.shape[2] // HD
    patches_f = patches.astype(jnp.float32)
    normed = normalize(patches_f, vis_gain, vis_bias).astype(jnp.bfloat16)
    proj = jnp.einsum("pd,sde->spe", normed, vis_qkv, preferred_element_type=jnp.float32).astype(
        jnp.bfloat16
    )
    query = proj[0].reshape(rows, heads, HD)
    partner_kv, partner_ids = swapped((proj[1:], patch_image), "grp", 0)
    both_kv = jnp.concatenate([proj[1:], partner_kv], axis=1)
    both_ids = jnp.concatenate([patch_image, partner_ids], axis=0)
    keys = both_kv[0].reshape(2 * rows, heads, HD)
    values = both_kv[1].reshape(2 * rows, heads, HD)
    scores = jnp.einsum("phe,khe->hpk", query, keys, preferred_element_type=jnp.float32) * HD ** (
        -0.5
    )
    same = patch_image[:, None] == both_ids[None, :]
    top = jnp.max(jnp.where(same, scores, -1e30), axis=2, keepdims=True)
    expo = jnp.where(same, jnp.exp(scores - top), 0.0)
    weights = (expo / jnp.sum(expo, axis=2, keepdims=True)).astype(jnp.bfloat16)
    attended = jnp.einsum(
        "hpk,khe->phe", weights, values, preferred_element_type=jnp.float32
    ).astype(jnp.bfloat16)
    attended = attended.reshape(rows, heads * HD)
    width = patches.shape[1] // lax.axis_size("tp")
    mixed = a2a_reduce_scatter(
        lax.dot_general(
            vis_out, attended, (((0,), (1,)), ((), ())), preferred_element_type=jnp.float32
        ).astype(jnp.bfloat16),
        "tp",
    )
    own_cols = lax.dynamic_slice_in_dim(patches_f, lax.axis_index("tp") * width, width, 1)
    visual = (mixed + own_cols.T).astype(jnp.bfloat16)
    windows = visual.reshape(width, rows // 4, 4)
    partial_rows = jnp.einsum(
        "cmk,kce->me", windows, merge_weight, preferred_element_type=jnp.float32
    )
    groups = lax.axis_size("grp")
    here = lax.axis_index("grp")
    merged_count = rows // 4
    text_count = text.shape[0]
    tok = text_count + merged_count
    cap = merged_count // min(groups, 16)
    target = positions // tok
    member = (target[:, None] == jnp.arange(groups, dtype=jnp.int32)[None, :]).astype(jnp.int32)
    rank = jnp.sum(jnp.cumsum(member, axis=0) * member, axis=1) - 1
    slot = target * cap + rank
    select = slot[None, :] == jnp.arange(groups * cap, dtype=jnp.int32)[:, None]
    select_bf = select.astype(jnp.bfloat16)
    bucket_pos = jnp.sum(jnp.where(select, positions[None, :] + 1, 0), axis=1) - 1
    merged = a2a_gather(
        a2a_reduce_scatter(partial_rows.astype(jnp.bfloat16), "tp").astype(jnp.bfloat16), "tp"
    )
    packed = jnp.dot(select_bf, merged, preferred_element_type=jnp.float32).astype(jnp.bfloat16)
    got_rows, got_pos = (
        lax.all_to_all(packed, "grp", split_axis=0, concat_axis=0, tiled=True),
        lax.all_to_all(bucket_pos, "grp", split_axis=0, concat_axis=0, tiled=True),
    )
    local_pos = got_pos - here * tok
    place = jnp.arange(tok, dtype=jnp.int32)
    landing = (local_pos[None, :] == place[:, None]) & (got_pos[None, :] >= 0)
    image_here = jnp.any(landing, axis=1).astype(jnp.int32)
    text_index = place - (jnp.cumsum(image_here) - image_here)
    text_pick = (image_here[:, None] == 0) & (
        text_index[:, None] == jnp.arange(text_count, dtype=jnp.int32)[None, :]
    )
    prompt = jnp.dot(landing.astype(jnp.bfloat16), got_rows, preferred_element_type=jnp.float32)
    prompt = prompt + jnp.dot(
        text_pick.astype(jnp.bfloat16), text, preferred_element_type=jnp.float32
    )
    dnorm = normalize(prompt, dec_gain, dec_bias).astype(jnp.bfloat16)
    dproj = jnp.einsum("td,sde->ste", dnorm, dec_qkv, preferred_element_type=jnp.float32).astype(
        jnp.bfloat16
    )
    dheads = dec_qkv.shape[2] // DH
    dquery = dproj[0].reshape(tok, dheads, DH)
    query_pos = here * tok + place
    best = jnp.full((dheads, tok), -1e30, jnp.float32)
    kv_rows = a2a_gather(jnp.swapaxes(dproj[1:], 0, 1), "grp")
    key_rows = kv_rows[:, 0].reshape(-1, dheads, DH)
    value_rows = kv_rows[:, 1].reshape(-1, dheads, DH)
    key_pos = jnp.arange(key_rows.shape[0], dtype=jnp.int32)
    score = jnp.einsum(
        "the,rhe->htr", dquery, key_rows, preferred_element_type=jnp.float32
    ) * DH ** (-0.5)
    allowed = key_pos[None, :] <= query_pos[:, None]
    new_best = jnp.maximum(best, jnp.max(jnp.where(allowed[None], score, -1e30), axis=2))
    expo_d = jnp.where(allowed[None], jnp.exp(score - new_best[:, :, None]), 0.0)
    total = jnp.sum(expo_d, axis=2)
    acc = jnp.einsum(
        "htr,rhe->hte", expo_d.astype(jnp.bfloat16), value_rows, preferred_element_type=jnp.float32
    )
    best, total, acc = (new_best, total, acc)
    result = acc / total[:, :, None]
    return result.transpose(1, 0, 2).reshape(tok, dheads * DH).astype(jnp.bfloat16)


def solution(mesh):
    in_specs = (
        P("grp", None),
        P("grp"),
        P(),
        P(),
        P(None, None, "tp"),
        P("tp", None),
        P(None, "tp", None),
        P("grp"),
        P("grp", None),
        P(),
        P(),
        P(None, None, "tp"),
    )
    out_specs = P("grp", "tp")
    return jax.shard_map(body, mesh=mesh, in_specs=in_specs, out_specs=out_specs, check_vma=False)
```

```python
import jax
import jax.numpy as jnp
from jax import lax
from jax.sharding import Mesh
from jax.sharding import PartitionSpec as P

HD = 104
DH = 64

layer_eps = 1e-05

GRP = ("gx", "gy")
TP = ("z", "core")


def normalize(values, gain, bias):
    mean = jnp.mean(values, axis=-1, keepdims=True)
    centred = values - mean
    spread = jnp.mean(centred * centred, axis=-1, keepdims=True)
    return centred * lax.rsqrt(spread + layer_eps) * gain + bias


def a2a_gather(value, axis):
    n = lax.axis_size(axis)
    spread = jnp.broadcast_to(value[None], (n,) + value.shape)
    got = lax.all_to_all(spread, axis, 0, 0, tiled=True)
    return got.reshape((n * value.shape[0],) + value.shape[1:])


def grp_gather(value):
    return a2a_gather(a2a_gather(value, "gy"), "gx")


def a2a_sum(parts, axis):
    got = lax.all_to_all(parts, axis, 0, 0, tiled=True)
    return jnp.sum(got.astype(jnp.float32), axis=0)


def attend_part(query, qpos, keys, kpos, values):
    score = jnp.dot(query, keys.T, preferred_element_type=jnp.float32) * DH ** (-0.5)
    allowed = kpos[None, :] <= qpos[:, None]
    top = jnp.max(jnp.where(allowed, score, -1e30), axis=1)
    expo = jnp.where(allowed, jnp.exp(score - top[:, None]), 0.0)
    total = jnp.sum(expo, axis=1)
    acc = jnp.dot(expo.astype(jnp.bfloat16), values, preferred_element_type=jnp.float32)
    return top, total, acc


def body(
    patches,
    patch_image,
    vis_gain,
    vis_bias,
    vis_qkv,
    vis_out,
    merge_weight,
    positions,
    text,
    dec_gain,
    dec_bias,
    dec_qkv,
):
    groups = lax.axis_size(GRP)
    here = lax.axis_index(GRP)
    rows = patches.shape[0]
    merged_count = rows // 4
    text_count = text.shape[0]
    tok = text_count + merged_count
    cap = merged_count // min(groups, 16)

    tnorm = normalize(text.astype(jnp.float32), dec_gain, dec_bias).astype(jnp.bfloat16)
    tproj = jnp.einsum("td,sde->ste", tnorm, dec_qkv, preferred_element_type=jnp.float32).astype(
        jnp.bfloat16
    )
    text_kv = grp_gather(jnp.stack([tproj[1], tproj[2]], axis=1))

    all_pos = a2a_gather(positions, GRP)
    flags = jnp.zeros((groups * tok,), jnp.int32).at[all_pos].add(1).reshape(groups, tok)
    free = 1 - flags
    text_rank = jnp.cumsum(free, axis=1) - 1
    place = jnp.arange(tok, dtype=jnp.int32)
    pick = (free[:, :, None] == 1) & (
        text_rank[:, :, None] == jnp.arange(text_count, dtype=jnp.int32)[None, None, :]
    )
    text_pos = jnp.sum(jnp.where(pick, place[None, :, None], 0), axis=1) + (
        jnp.arange(groups, dtype=jnp.int32) * tok
    )[:, None]

    heads = vis_qkv.shape[2] // HD
    patches_f = patches.astype(jnp.float32)
    normed = normalize(patches_f, vis_gain, vis_bias).astype(jnp.bfloat16)
    proj = jnp.einsum("pd,sde->spe", normed, vis_qkv, preferred_element_type=jnp.float32).astype(
        jnp.bfloat16
    )
    query = proj[0].reshape(rows, heads, HD)
    swap = [(i, i ^ 1) for i in range(lax.axis_size("gy"))]
    partner_kv, partner_ids = lax.ppermute((proj[1:], patch_image), "gy", swap)
    both_kv = jnp.concatenate([proj[1:], partner_kv], axis=1)
    both_ids = jnp.concatenate([patch_image, partner_ids], axis=0)
    keys = both_kv[0].reshape(2 * rows, heads, HD)
    values = both_kv[1].reshape(2 * rows, heads, HD)
    scores = jnp.einsum("phe,khe->hpk", query, keys, preferred_element_type=jnp.float32) * HD ** (
        -0.5
    )
    same = patch_image[:, None] == both_ids[None, :]
    top = jnp.max(jnp.where(same, scores, -1e30), axis=2, keepdims=True)
    expo = jnp.where(same, jnp.exp(scores - top), 0.0)
    weights = (expo / jnp.sum(expo, axis=2, keepdims=True)).astype(jnp.bfloat16)
    attended = jnp.einsum(
        "hpk,khe->phe", weights, values, preferred_element_type=jnp.float32
    ).astype(jnp.bfloat16)
    attended = attended.reshape(rows, heads * HD)

    nz = lax.axis_size("z")
    ncore = lax.axis_size("core")
    width = patches.shape[1] // (nz * ncore)
    mixed_parts = lax.dot_general(
        vis_out, attended, (((0,), (1,)), ((), ())), preferred_element_type=jnp.float32
    ).astype(jnp.bfloat16)
    mixed_parts = mixed_parts.reshape(nz, ncore, width, rows).transpose(1, 0, 2, 3)
    half = a2a_sum(mixed_parts, "core").astype(jnp.bfloat16)
    mixed = a2a_sum(half, "z")
    own_cols = lax.dynamic_slice_in_dim(patches_f, lax.axis_index(TP) * width, width, 1)
    visual = (mixed + own_cols.T).astype(jnp.bfloat16)
    windows = visual.reshape(width, merged_count, 4)
    partial_rows = jnp.einsum(
        "cmk,kce->me", windows, merge_weight, preferred_element_type=jnp.float32
    ).astype(jnp.bfloat16)
    ntp = nz * ncore
    merged = a2a_gather(
        a2a_sum(partial_rows.reshape(ntp, merged_count // ntp, -1), TP).astype(jnp.bfloat16), TP
    )

    mnorm = normalize(merged.astype(jnp.float32), dec_gain, dec_bias).astype(jnp.bfloat16)
    mproj = jnp.einsum("td,sde->ste", mnorm, dec_qkv, preferred_element_type=jnp.float32).astype(
        jnp.bfloat16
    )
    merged_kv = grp_gather(jnp.stack([mproj[1], mproj[2]], axis=1))

    own_text_pos = lax.dynamic_index_in_dim(text_pos, here, 0, keepdims=False)
    dquery = jnp.concatenate([tproj[0], mproj[0]], axis=0)
    query_pos = jnp.concatenate([own_text_pos, positions], axis=0)
    top_t, total_t, acc_t = attend_part(
        dquery, query_pos, text_kv[:, 0], text_pos.reshape(-1), text_kv[:, 1]
    )
    top_m, total_m, acc_m = attend_part(dquery, query_pos, merged_kv[:, 0], all_pos, merged_kv[:, 1])
    best = jnp.maximum(top_t, top_m)
    scale_t = jnp.exp(top_t - best)
    scale_m = jnp.exp(top_m - best)
    total = total_t * scale_t + total_m * scale_m
    acc = acc_t * scale_t[:, None] + acc_m * scale_m[:, None]
    result = (acc / total[:, None]).astype(jnp.bfloat16)
    text_out = result[:text_count]
    merged_out = result[text_count:]

    target = positions // tok
    member = (target[:, None] == jnp.arange(groups, dtype=jnp.int32)[None, :]).astype(jnp.int32)
    rank = jnp.sum(jnp.cumsum(member, axis=0) * member, axis=1) - 1
    slot = target * cap + rank
    select = slot[None, :] == jnp.arange(groups * cap, dtype=jnp.int32)[:, None]
    packed = jnp.dot(
        select.astype(jnp.bfloat16), merged_out, preferred_element_type=jnp.float32
    ).astype(jnp.bfloat16)
    got = lax.all_to_all(packed, GRP, 0, 0, tiled=True)

    src_pos = all_pos.reshape(groups, merged_count)
    to_me = (src_pos // tok) == here
    src_rank = jnp.cumsum(to_me.astype(jnp.int32), axis=1) - 1
    slot_hit = to_me[:, :, None] & (
        src_rank[:, :, None] == jnp.arange(cap, dtype=jnp.int32)[None, None, :]
    )
    got_pos = jnp.sum(jnp.where(slot_hit, src_pos[:, :, None] + 1, 0), axis=1).reshape(-1) - 1
    local = got_pos - here * tok
    landing = (local[None, :] == place[:, None]) & (got_pos[None, :] >= 0)
    text_land = own_text_pos[None, :] - here * tok == place[:, None]
    out = jnp.dot(landing.astype(jnp.bfloat16), got, preferred_element_type=jnp.float32)
    out = out + jnp.dot(
        text_land.astype(jnp.bfloat16), text_out, preferred_element_type=jnp.float32
    )
    return out.astype(jnp.bfloat16)


def solution(mesh):
    grid = mesh.devices.reshape(4, mesh.devices.shape[0] // 4, mesh.devices.shape[1] // 2, 2)
    mesh4 = Mesh(grid, GRP + TP)
    in_specs = (
        P(GRP, None),
        P(GRP),
        P(),
        P(),
        P(None, None, TP),
        P(TP, None),
        P(None, TP, None),
        P(GRP),
        P(GRP, None),
        P(),
        P(),
        P(None, None, TP),
    )
    out_specs = P(GRP, TP)
    return jax.shard_map(body, mesh=mesh4, in_specs=in_specs, out_specs=out_specs, check_vma=False)
```

```python
import jax
import jax.numpy as jnp
from jax import lax
from jax.sharding import Mesh
from jax.sharding import PartitionSpec as P

HD = 104
DH = 64

layer_eps = 1e-05

GRP = ("gx", "gy")
TP = ("z", "core")


def normalize(values, gain, bias):
    mean = jnp.mean(values, axis=-1, keepdims=True)
    centred = values - mean
    spread = jnp.mean(centred * centred, axis=-1, keepdims=True)
    return centred * lax.rsqrt(spread + layer_eps) * gain + bias


def a2a_gather(value, axis):
    n = lax.axis_size(axis)
    spread = jnp.broadcast_to(value[None], (n,) + value.shape)
    got = lax.all_to_all(spread, axis, 0, 0, tiled=True)
    return got.reshape((n * value.shape[0],) + value.shape[1:])


def grp_gather(value):
    return a2a_gather(a2a_gather(value, "gy"), "gx")


def a2a_sum(parts, axis):
    got = lax.all_to_all(parts, axis, 0, 0, tiled=True)
    return jnp.sum(got.astype(jnp.float32), axis=0)


def attend_part(query, allowed, keys, values):
    score = jnp.dot(query, keys.T, preferred_element_type=jnp.float32) * DH ** (-0.5)
    top = jnp.max(jnp.where(allowed, score, -1e30), axis=1)
    expo = jnp.where(allowed, jnp.exp(score - top[:, None]), 0.0)
    total = jnp.sum(expo, axis=1)
    acc = jnp.dot(expo.astype(jnp.bfloat16), values, preferred_element_type=jnp.float32)
    return top, total, acc


def body(
    patches,
    patch_image,
    vis_gain,
    vis_bias,
    vis_qkv,
    vis_out,
    merge_weight,
    positions,
    text,
    dec_gain,
    dec_bias,
    dec_qkv,
):
    groups = lax.axis_size(GRP)
    here = lax.axis_index(GRP)
    rows = patches.shape[0]
    merged_count = rows // 4
    text_count = text.shape[0]
    tok = text_count + merged_count
    cap = merged_count // min(groups, 16)

    tnorm = normalize(text.astype(jnp.float32), dec_gain, dec_bias).astype(jnp.bfloat16)
    tproj = jnp.einsum("td,sde->ste", tnorm, dec_qkv, preferred_element_type=jnp.float32).astype(
        jnp.bfloat16
    )
    text_kv = lax.all_gather(jnp.stack([tproj[1], tproj[2]], axis=1), GRP, axis=0, tiled=True)

    all_pos = lax.all_gather(positions, GRP, axis=0, tiled=True)
    place = jnp.arange(tok, dtype=jnp.int32)
    flags = jnp.sum((all_pos[None, :] == (here * tok + place)[:, None]).astype(jnp.int32), axis=1)
    free = 1 - flags
    text_rank = jnp.cumsum(free) - 1
    pick = (free[:, None] == 1) & (text_rank[:, None] == jnp.arange(text_count, dtype=jnp.int32)[None, :])
    own_text_pos = jnp.sum(jnp.where(pick, place[:, None], 0), axis=0) + here * tok

    heads = vis_qkv.shape[2] // HD
    patches_f = patches.astype(jnp.float32)
    normed = normalize(patches_f, vis_gain, vis_bias).astype(jnp.bfloat16)
    proj = jnp.einsum("pd,sde->spe", normed, vis_qkv, preferred_element_type=jnp.float32).astype(
        jnp.bfloat16
    )
    query = proj[0].reshape(rows, heads, HD)
    swap = [(i, i ^ 1) for i in range(lax.axis_size("gy"))]
    partner_kv, partner_ids = lax.ppermute((proj[1:], patch_image), "gy", swap)
    both_kv = jnp.concatenate([proj[1:], partner_kv], axis=1)
    both_ids = jnp.concatenate([patch_image, partner_ids], axis=0)
    keys = both_kv[0].reshape(2 * rows, heads, HD)
    values = both_kv[1].reshape(2 * rows, heads, HD)
    scores = jnp.einsum("phe,khe->hpk", query, keys, preferred_element_type=jnp.float32) * HD ** (
        -0.5
    )
    same = patch_image[:, None] == both_ids[None, :]
    top = jnp.max(jnp.where(same, scores, -1e30), axis=2, keepdims=True)
    expo = jnp.where(same, jnp.exp(scores - top), 0.0)
    weights = (expo / jnp.sum(expo, axis=2, keepdims=True)).astype(jnp.bfloat16)
    attended = jnp.einsum(
        "hpk,khe->phe", weights, values, preferred_element_type=jnp.float32
    ).astype(jnp.bfloat16)
    attended = attended.reshape(rows, heads * HD)

    nz = lax.axis_size("z")
    ncore = lax.axis_size("core")
    width = patches.shape[1] // (nz * ncore)
    mixed_parts = lax.dot_general(
        vis_out, attended, (((0,), (1,)), ((), ())), preferred_element_type=jnp.float32
    ).astype(jnp.bfloat16)
    mixed_parts = mixed_parts.reshape(nz, ncore, width, rows).transpose(1, 0, 2, 3)
    half = a2a_sum(mixed_parts, "core").astype(jnp.bfloat16)
    mixed = a2a_sum(half, "z")
    own_cols = lax.dynamic_slice_in_dim(patches_f, lax.axis_index(TP) * width, width, 1)
    visual = (mixed + own_cols.T).astype(jnp.bfloat16)
    windows = visual.reshape(width, merged_count, 4)
    partial_rows = jnp.einsum(
        "cmk,kce->me", windows, merge_weight, preferred_element_type=jnp.float32
    ).astype(jnp.bfloat16)
    ntp = nz * ncore
    merged = a2a_gather(
        a2a_sum(partial_rows.reshape(ntp, merged_count // ntp, -1), TP).astype(jnp.bfloat16), TP
    )

    mnorm = normalize(merged.astype(jnp.float32), dec_gain, dec_bias).astype(jnp.bfloat16)
    mproj = jnp.einsum("td,sde->ste", mnorm, dec_qkv, preferred_element_type=jnp.float32).astype(
        jnp.bfloat16
    )
    merged_kv = grp_gather(jnp.stack([mproj[1], mproj[2]], axis=1))

    dquery = jnp.concatenate([tproj[0], mproj[0]], axis=0)
    query_pos = jnp.concatenate([own_text_pos, positions], axis=0)
    block = positions // tok
    seen = jnp.sum(
        ((all_pos[None, :] >= (block * tok)[:, None]) & (all_pos[None, :] <= positions[:, None])).astype(
            jnp.int32
        ),
        axis=1,
    )
    merged_limit = block * text_count + (positions - block * tok + 1 - seen)
    text_limit = here * text_count + jnp.arange(text_count, dtype=jnp.int32) + 1
    limit = jnp.concatenate([text_limit, merged_limit], axis=0)
    text_key = jnp.arange(groups * text_count, dtype=jnp.int32)
    top_t, total_t, acc_t = attend_part(
        dquery, text_key[None, :] < limit[:, None], text_kv[:, 0], text_kv[:, 1]
    )
    top_m, total_m, acc_m = attend_part(
        dquery, all_pos[None, :] <= query_pos[:, None], merged_kv[:, 0], merged_kv[:, 1]
    )
    best = jnp.maximum(top_t, top_m)
    scale_t = jnp.exp(top_t - best)
    scale_m = jnp.exp(top_m - best)
    total = total_t * scale_t + total_m * scale_m
    acc = acc_t * scale_t[:, None] + acc_m * scale_m[:, None]
    result = (acc / total[:, None]).astype(jnp.bfloat16)
    text_out = result[:text_count]
    merged_out = result[text_count:]

    target = positions // tok
    member = (target[:, None] == jnp.arange(groups, dtype=jnp.int32)[None, :]).astype(jnp.int32)
    rank = jnp.sum(jnp.cumsum(member, axis=0) * member, axis=1) - 1
    slot = target * cap + rank
    select = slot[None, :] == jnp.arange(groups * cap, dtype=jnp.int32)[:, None]
    packed = jnp.dot(
        select.astype(jnp.bfloat16), merged_out, preferred_element_type=jnp.float32
    ).astype(jnp.bfloat16)
    got = lax.all_to_all(packed, GRP, 0, 0, tiled=True)

    src_pos = all_pos.reshape(groups, merged_count)
    to_me = (src_pos // tok) == here
    src_rank = jnp.cumsum(to_me.astype(jnp.int32), axis=1) - 1
    slot_hit = to_me[:, :, None] & (
        src_rank[:, :, None] == jnp.arange(cap, dtype=jnp.int32)[None, None, :]
    )
    got_pos = jnp.sum(jnp.where(slot_hit, src_pos[:, :, None] + 1, 0), axis=1).reshape(-1) - 1
    local = got_pos - here * tok
    landing = (local[None, :] == place[:, None]) & (got_pos[None, :] >= 0)
    text_land = own_text_pos[None, :] - here * tok == place[:, None]
    out = jnp.dot(landing.astype(jnp.bfloat16), got, preferred_element_type=jnp.float32)
    out = out + jnp.dot(
        text_land.astype(jnp.bfloat16), text_out, preferred_element_type=jnp.float32
    )
    return out.astype(jnp.bfloat16)


def solution(mesh):
    grid = mesh.devices.reshape(4, mesh.devices.shape[0] // 4, mesh.devices.shape[1] // 2, 2)
    mesh4 = Mesh(grid, GRP + TP)
    in_specs = (
        P(GRP, None),
        P(GRP),
        P(),
        P(),
        P(None, None, TP),
        P(TP, None),
        P(None, TP, None),
        P(GRP),
        P(GRP, None),
        P(),
        P(),
        P(None, None, TP),
    )
    out_specs = P(GRP, TP)
    return jax.shard_map(body, mesh=mesh4, in_specs=in_specs, out_specs=out_specs, check_vma=False)
```

```python
import jax
import jax.numpy as jnp
from jax import lax
from jax.sharding import Mesh
from jax.sharding import PartitionSpec as P

HD = 104
DH = 64

layer_eps = 1e-05

GRP = ("gx", "gy")
TP = ("z", "core")


def normalize(values, gain, bias):
    mean = jnp.mean(values, axis=-1, keepdims=True)
    centred = values - mean
    spread = jnp.mean(centred * centred, axis=-1, keepdims=True)
    return centred * lax.rsqrt(spread + layer_eps) * gain + bias


def a2a_gather(value, axis):
    n = lax.axis_size(axis)
    spread = jnp.broadcast_to(value[None], (n,) + value.shape)
    got = lax.all_to_all(spread, axis, 0, 0, tiled=True)
    return got.reshape((n * value.shape[0],) + value.shape[1:])


def grp_gather(value):
    return a2a_gather(a2a_gather(value, "gy"), "gx")


def a2a_sum(parts, axis):
    got = lax.all_to_all(parts, axis, 0, 0, tiled=True)
    return jnp.sum(got.astype(jnp.float32), axis=0)


def attend_part(query, allowed, keys, values):
    score = jnp.dot(query, keys.T, preferred_element_type=jnp.float32) * DH ** (-0.5)
    top = jnp.max(jnp.where(allowed, score, -1e30), axis=1)
    expo = jnp.where(allowed, jnp.exp(score - top[:, None]), 0.0)
    total = jnp.sum(expo, axis=1)
    acc = jnp.dot(expo.astype(jnp.bfloat16), values, preferred_element_type=jnp.float32)
    return top, total, acc


def body(
    patches,
    patch_image,
    vis_gain,
    vis_bias,
    vis_qkv,
    vis_out,
    merge_weight,
    positions,
    text,
    dec_gain,
    dec_bias,
    dec_qkv,
):
    groups = lax.axis_size(GRP)
    here = lax.axis_index(GRP)
    rows = patches.shape[0]
    merged_count = rows // 4
    text_count = text.shape[0]
    tok = text_count + merged_count
    cap = merged_count // min(groups, 16)

    tnorm = normalize(text.astype(jnp.float32), dec_gain, dec_bias).astype(jnp.bfloat16)
    tproj = jnp.einsum("td,sde->ste", tnorm, dec_qkv, preferred_element_type=jnp.float32).astype(
        jnp.bfloat16
    )
    digit = 128
    pos_rows = jnp.stack([positions // digit, positions % digit]).astype(jnp.bfloat16)
    extra = jnp.zeros((8, 2, DH), jnp.bfloat16).at[:2].set(pos_rows.reshape(2, 2, DH))
    payload = jnp.concatenate([jnp.stack([tproj[1], tproj[2]], axis=1), extra], axis=0)
    gathered = lax.all_gather(payload, GRP, axis=0, tiled=True).reshape(
        groups, text_count + 8, 2, DH
    )
    text_kv = gathered[:, :text_count].reshape(groups * text_count, 2, DH)
    digits = gathered[:, text_count : text_count + 2].reshape(groups, 2, 2 * DH).astype(jnp.int32)
    all_pos = (digits[:, 0] * digit + digits[:, 1]).reshape(-1)

    place = jnp.arange(tok, dtype=jnp.int32)
    flags = jnp.sum((all_pos[None, :] == (here * tok + place)[:, None]).astype(jnp.int32), axis=1)
    free = 1 - flags
    text_rank = jnp.cumsum(free) - 1
    pick = (free[:, None] == 1) & (text_rank[:, None] == jnp.arange(text_count, dtype=jnp.int32)[None, :])
    own_text_pos = jnp.sum(jnp.where(pick, place[:, None], 0), axis=0) + here * tok

    heads = vis_qkv.shape[2] // HD
    patches_f = patches.astype(jnp.float32)
    normed = normalize(patches_f, vis_gain, vis_bias).astype(jnp.bfloat16)
    proj = jnp.einsum("pd,sde->spe", normed, vis_qkv, preferred_element_type=jnp.float32).astype(
        jnp.bfloat16
    )
    query = proj[0].reshape(rows, heads, HD)
    swap = [(i, i ^ 1) for i in range(lax.axis_size("gy"))]
    partner_kv, partner_ids = lax.ppermute((proj[1:], patch_image), "gy", swap)
    both_kv = jnp.concatenate([proj[1:], partner_kv], axis=1)
    both_ids = jnp.concatenate([patch_image, partner_ids], axis=0)
    keys = both_kv[0].reshape(2 * rows, heads, HD)
    values = both_kv[1].reshape(2 * rows, heads, HD)
    scores = jnp.einsum("phe,khe->hpk", query, keys, preferred_element_type=jnp.float32) * HD ** (
        -0.5
    )
    same = patch_image[:, None] == both_ids[None, :]
    top = jnp.max(jnp.where(same, scores, -1e30), axis=2, keepdims=True)
    expo = jnp.where(same, jnp.exp(scores - top), 0.0)
    weights = (expo / jnp.sum(expo, axis=2, keepdims=True)).astype(jnp.bfloat16)
    attended = jnp.einsum(
        "hpk,khe->phe", weights, values, preferred_element_type=jnp.float32
    ).astype(jnp.bfloat16)
    attended = attended.reshape(rows, heads * HD)

    nz = lax.axis_size("z")
    ncore = lax.axis_size("core")
    width = patches.shape[1] // (nz * ncore)
    mixed_parts = lax.dot_general(
        vis_out, attended, (((0,), (1,)), ((), ())), preferred_element_type=jnp.float32
    ).astype(jnp.bfloat16)
    mixed_parts = mixed_parts.reshape(nz, ncore, width, rows).transpose(1, 0, 2, 3)
    half = a2a_sum(mixed_parts, "core").astype(jnp.bfloat16)
    mixed = a2a_sum(half, "z")
    own_cols = lax.dynamic_slice_in_dim(patches_f, lax.axis_index(TP) * width, width, 1)
    visual = (mixed + own_cols.T).astype(jnp.bfloat16)
    windows = visual.reshape(width, merged_count, 4)
    partial_rows = jnp.einsum(
        "cmk,kce->me", windows, merge_weight, preferred_element_type=jnp.float32
    ).astype(jnp.bfloat16)
    ntp = nz * ncore
    merged = a2a_gather(
        a2a_sum(partial_rows.reshape(ntp, merged_count // ntp, -1), TP).astype(jnp.bfloat16), TP
    )

    mnorm = normalize(merged.astype(jnp.float32), dec_gain, dec_bias).astype(jnp.bfloat16)
    mproj = jnp.einsum("td,sde->ste", mnorm, dec_qkv, preferred_element_type=jnp.float32).astype(
        jnp.bfloat16
    )
    merged_kv = grp_gather(jnp.stack([mproj[1], mproj[2]], axis=1))

    dquery = jnp.concatenate([tproj[0], mproj[0]], axis=0)
    query_pos = jnp.concatenate([own_text_pos, positions], axis=0)
    block = positions // tok
    seen = jnp.sum(
        ((all_pos[None, :] >= (block * tok)[:, None]) & (all_pos[None, :] <= positions[:, None])).astype(
            jnp.int32
        ),
        axis=1,
    )
    merged_limit = block * text_count + (positions - block * tok + 1 - seen)
    text_limit = here * text_count + jnp.arange(text_count, dtype=jnp.int32) + 1
    limit = jnp.concatenate([text_limit, merged_limit], axis=0)
    text_key = jnp.arange(groups * text_count, dtype=jnp.int32)
    top_t, total_t, acc_t = attend_part(
        dquery, text_key[None, :] < limit[:, None], text_kv[:, 0], text_kv[:, 1]
    )
    top_m, total_m, acc_m = attend_part(
        dquery, all_pos[None, :] <= query_pos[:, None], merged_kv[:, 0], merged_kv[:, 1]
    )
    best = jnp.maximum(top_t, top_m)
    scale_t = jnp.exp(top_t - best)
    scale_m = jnp.exp(top_m - best)
    total = total_t * scale_t + total_m * scale_m
    acc = acc_t * scale_t[:, None] + acc_m * scale_m[:, None]
    result = (acc / total[:, None]).astype(jnp.bfloat16)
    text_out = result[:text_count]
    merged_out = result[text_count:]

    target = positions // tok
    member = (target[:, None] == jnp.arange(groups, dtype=jnp.int32)[None, :]).astype(jnp.int32)
    rank = jnp.sum(jnp.cumsum(member, axis=0) * member, axis=1) - 1
    slot = target * cap + rank
    select = slot[None, :] == jnp.arange(groups * cap, dtype=jnp.int32)[:, None]
    packed = jnp.dot(
        select.astype(jnp.bfloat16), merged_out, preferred_element_type=jnp.float32
    ).astype(jnp.bfloat16)
    got = lax.all_to_all(packed, GRP, 0, 0, tiled=True)

    src_pos = all_pos.reshape(groups, merged_count)
    to_me = (src_pos // tok) == here
    src_rank = jnp.cumsum(to_me.astype(jnp.int32), axis=1) - 1
    slot_hit = to_me[:, :, None] & (
        src_rank[:, :, None] == jnp.arange(cap, dtype=jnp.int32)[None, None, :]
    )
    got_pos = jnp.sum(jnp.where(slot_hit, src_pos[:, :, None] + 1, 0), axis=1).reshape(-1) - 1
    local = got_pos - here * tok
    landing = (local[None, :] == place[:, None]) & (got_pos[None, :] >= 0)
    text_land = own_text_pos[None, :] - here * tok == place[:, None]
    out = jnp.dot(landing.astype(jnp.bfloat16), got, preferred_element_type=jnp.float32)
    out = out + jnp.dot(
        text_land.astype(jnp.bfloat16), text_out, preferred_element_type=jnp.float32
    )
    return out.astype(jnp.bfloat16)


def solution(mesh):
    grid = mesh.devices.reshape(4, mesh.devices.shape[0] // 4, mesh.devices.shape[1] // 2, 2)
    mesh4 = Mesh(grid, GRP + TP)
    in_specs = (
        P(GRP, None),
        P(GRP),
        P(),
        P(),
        P(None, None, TP),
        P(TP, None),
        P(None, TP, None),
        P(GRP),
        P(GRP, None),
        P(),
        P(),
        P(None, None, TP),
    )
    out_specs = P(GRP, TP)
    return jax.shard_map(body, mesh=mesh4, in_specs=in_specs, out_specs=out_specs, check_vma=False)
```

```python
import jax
import jax.numpy as jnp
from jax import lax
from jax.sharding import Mesh
from jax.sharding import PartitionSpec as P

HD = 104
DH = 64

layer_eps = 1e-05

GRP = ("gx", "gy")
TP = ("z", "core")


def normalize(values, gain, bias):
    mean = jnp.mean(values, axis=-1, keepdims=True)
    centred = values - mean
    spread = jnp.mean(centred * centred, axis=-1, keepdims=True)
    return centred * lax.rsqrt(spread + layer_eps) * gain + bias


def a2a_gather(value, axis):
    n = lax.axis_size(axis)
    spread = jnp.broadcast_to(value[None], (n,) + value.shape)
    got = lax.all_to_all(spread, axis, 0, 0, tiled=True)
    return got.reshape((n * value.shape[0],) + value.shape[1:])


def grp_gather(value):
    return a2a_gather(a2a_gather(value, "gy"), "gx")


def a2a_sum(parts, axis):
    got = lax.all_to_all(parts, axis, 0, 0, tiled=True)
    return jnp.sum(got.astype(jnp.float32), axis=0)


def attend_part(query, allowed, keys, values):
    score = jnp.dot(query, keys.T, preferred_element_type=jnp.float32) * DH ** (-0.5)
    top = jnp.max(jnp.where(allowed, score, -1e30), axis=1)
    expo = jnp.where(allowed, jnp.exp(score - top[:, None]), 0.0)
    total = jnp.sum(expo, axis=1)
    acc = jnp.dot(expo.astype(jnp.bfloat16), values, preferred_element_type=jnp.float32)
    return top, total, acc


def body(
    patches,
    patch_image,
    vis_gain,
    vis_bias,
    vis_qkv,
    vis_out,
    merge_weight,
    positions,
    text,
    dec_gain,
    dec_bias,
    dec_qkv,
):
    groups = lax.axis_size(GRP)
    here = lax.axis_index(GRP)
    rows = patches.shape[0]
    merged_count = rows // 4
    text_count = text.shape[0]
    tok = text_count + merged_count
    cap = merged_count // min(groups, 16)

    tnorm = normalize(text.astype(jnp.float32), dec_gain, dec_bias).astype(jnp.bfloat16)
    tproj = jnp.einsum("td,sde->ste", tnorm, dec_qkv, preferred_element_type=jnp.float32).astype(
        jnp.bfloat16
    )
    digit = 128
    pad_rows = 8
    lanes = 2 * DH
    pos_rows = jnp.stack([positions // digit, positions % digit]).astype(jnp.bfloat16)
    extra = jnp.zeros((pad_rows, lanes), jnp.bfloat16).at[:2].set(pos_rows.reshape(2, lanes))
    payload = jnp.concatenate([jnp.concatenate([tproj[1], tproj[2]], axis=1), extra], axis=0)
    text_kv = lax.all_gather(payload, GRP, axis=0, tiled=True)
    digits = text_kv.reshape(groups, text_count + pad_rows, lanes)[:, text_count : text_count + 2]
    digits = digits.astype(jnp.int32)
    all_pos = (digits[:, 0] * digit + digits[:, 1]).reshape(-1)

    place = jnp.arange(tok, dtype=jnp.int32)
    flags = jnp.sum((all_pos[None, :] == (here * tok + place)[:, None]).astype(jnp.int32), axis=1)
    free = 1 - flags
    text_rank = jnp.cumsum(free) - 1
    pick = (free[:, None] == 1) & (text_rank[:, None] == jnp.arange(text_count, dtype=jnp.int32)[None, :])
    own_text_pos = jnp.sum(jnp.where(pick, place[:, None], 0), axis=0) + here * tok

    heads = vis_qkv.shape[2] // HD
    patches_f = patches.astype(jnp.float32)
    normed = normalize(patches_f, vis_gain, vis_bias).astype(jnp.bfloat16)
    proj = jnp.einsum("pd,sde->spe", normed, vis_qkv, preferred_element_type=jnp.float32).astype(
        jnp.bfloat16
    )
    query = proj[0].reshape(rows, heads, HD)
    swap = [(i, i ^ 1) for i in range(lax.axis_size("gy"))]
    partner_kv, partner_ids = lax.ppermute((proj[1:], patch_image), "gy", swap)
    both_kv = jnp.concatenate([proj[1:], partner_kv], axis=1)
    both_ids = jnp.concatenate([patch_image, partner_ids], axis=0)
    keys = both_kv[0].reshape(2 * rows, heads, HD)
    values = both_kv[1].reshape(2 * rows, heads, HD)
    scores = jnp.einsum("phe,khe->hpk", query, keys, preferred_element_type=jnp.float32) * HD ** (
        -0.5
    )
    same = patch_image[:, None] == both_ids[None, :]
    top = jnp.max(jnp.where(same, scores, -1e30), axis=2, keepdims=True)
    expo = jnp.where(same, jnp.exp(scores - top), 0.0)
    weights = (expo / jnp.sum(expo, axis=2, keepdims=True)).astype(jnp.bfloat16)
    attended = jnp.einsum(
        "hpk,khe->phe", weights, values, preferred_element_type=jnp.float32
    ).astype(jnp.bfloat16)
    attended = attended.reshape(rows, heads * HD)

    nz = lax.axis_size("z")
    ncore = lax.axis_size("core")
    width = patches.shape[1] // (nz * ncore)
    mixed_parts = lax.dot_general(
        vis_out, attended, (((0,), (1,)), ((), ())), preferred_element_type=jnp.float32
    ).astype(jnp.bfloat16)
    mixed_parts = mixed_parts.reshape(nz, ncore, width, rows).transpose(1, 0, 2, 3)
    half = a2a_sum(mixed_parts, "core").astype(jnp.bfloat16)
    mixed = a2a_sum(half, "z")
    own_cols = lax.dynamic_slice_in_dim(patches_f, lax.axis_index(TP) * width, width, 1)
    visual = (mixed + own_cols.T).astype(jnp.bfloat16)
    windows = visual.reshape(width, merged_count, 4)
    partial_rows = jnp.einsum(
        "cmk,kce->me", windows, merge_weight, preferred_element_type=jnp.float32
    ).astype(jnp.bfloat16)
    ntp = nz * ncore
    merged = a2a_gather(
        a2a_sum(partial_rows.reshape(ntp, merged_count // ntp, -1), TP).astype(jnp.bfloat16), TP
    )

    mnorm = normalize(merged.astype(jnp.float32), dec_gain, dec_bias).astype(jnp.bfloat16)
    mproj = jnp.einsum("td,sde->ste", mnorm, dec_qkv, preferred_element_type=jnp.float32).astype(
        jnp.bfloat16
    )
    merged_kv = grp_gather(jnp.concatenate([mproj[1], mproj[2]], axis=1))

    dquery = jnp.concatenate([tproj[0], mproj[0]], axis=0)
    query_pos = jnp.concatenate([own_text_pos, positions], axis=0)
    block = positions // tok
    seen = jnp.sum(
        ((all_pos[None, :] >= (block * tok)[:, None]) & (all_pos[None, :] <= positions[:, None])).astype(
            jnp.int32
        ),
        axis=1,
    )
    merged_limit = block * text_count + (positions - block * tok + 1 - seen)
    text_limit = here * text_count + jnp.arange(text_count, dtype=jnp.int32) + 1
    limit = jnp.concatenate([text_limit, merged_limit], axis=0)
    key_row = jnp.arange(groups * (text_count + pad_rows), dtype=jnp.int32)
    key_grp = key_row // (text_count + pad_rows)
    key_in = key_row % (text_count + pad_rows)
    text_key = jnp.where(key_in < text_count, key_grp * text_count + key_in, groups * tok)
    top_t, total_t, acc_t = attend_part(
        dquery, text_key[None, :] < limit[:, None], text_kv[:, :DH], text_kv[:, DH:]
    )
    top_m, total_m, acc_m = attend_part(
        dquery, all_pos[None, :] <= query_pos[:, None], merged_kv[:, :DH], merged_kv[:, DH:]
    )
    best = jnp.maximum(top_t, top_m)
    scale_t = jnp.exp(top_t - best)
    scale_m = jnp.exp(top_m - best)
    total = total_t * scale_t + total_m * scale_m
    acc = acc_t * scale_t[:, None] + acc_m * scale_m[:, None]
    result = (acc / total[:, None]).astype(jnp.bfloat16)
    text_out = result[:text_count]
    merged_out = result[text_count:]

    target = positions // tok
    member = (target[:, None] == jnp.arange(groups, dtype=jnp.int32)[None, :]).astype(jnp.int32)
    rank = jnp.sum(jnp.cumsum(member, axis=0) * member, axis=1) - 1
    slot = target * cap + rank
    select = slot[None, :] == jnp.arange(groups * cap, dtype=jnp.int32)[:, None]
    packed = jnp.dot(
        select.astype(jnp.bfloat16), merged_out, preferred_element_type=jnp.float32
    ).astype(jnp.bfloat16)
    got = lax.all_to_all(packed, GRP, 0, 0, tiled=True)

    src_pos = all_pos.reshape(groups, merged_count)
    to_me = (src_pos // tok) == here
    src_rank = jnp.cumsum(to_me.astype(jnp.int32), axis=1) - 1
    slot_hit = to_me[:, :, None] & (
        src_rank[:, :, None] == jnp.arange(cap, dtype=jnp.int32)[None, None, :]
    )
    got_pos = jnp.sum(jnp.where(slot_hit, src_pos[:, :, None] + 1, 0), axis=1).reshape(-1) - 1
    local = got_pos - here * tok
    landing = (local[None, :] == place[:, None]) & (got_pos[None, :] >= 0)
    text_land = own_text_pos[None, :] - here * tok == place[:, None]
    out = jnp.dot(landing.astype(jnp.bfloat16), got, preferred_element_type=jnp.float32)
    out = out + jnp.dot(
        text_land.astype(jnp.bfloat16), text_out, preferred_element_type=jnp.float32
    )
    return out.astype(jnp.bfloat16)


def solution(mesh):
    grid = mesh.devices.reshape(4, mesh.devices.shape[0] // 4, mesh.devices.shape[1] // 2, 2)
    mesh4 = Mesh(grid, GRP + TP)
    in_specs = (
        P(GRP, None),
        P(GRP),
        P(),
        P(),
        P(None, None, TP),
        P(TP, None),
        P(None, TP, None),
        P(GRP),
        P(GRP, None),
        P(),
        P(),
        P(None, None, TP),
    )
    out_specs = P(GRP, TP)
    return jax.shard_map(body, mesh=mesh4, in_specs=in_specs, out_specs=out_specs, check_vma=False)
```

```python
import jax
import jax.numpy as jnp
from jax import lax
from jax.sharding import Mesh
from jax.sharding import PartitionSpec as P

HD = 104
DH = 64

layer_eps = 1e-05

GRP = ("gx", "gy")
TP = ("z", "core")


def normalize(values, gain, bias):
    mean = jnp.mean(values, axis=-1, keepdims=True)
    centred = values - mean
    spread = jnp.mean(centred * centred, axis=-1, keepdims=True)
    return centred * lax.rsqrt(spread + layer_eps) * gain + bias


def a2a_gather(value, axis):
    n = lax.axis_size(axis)
    spread = jnp.broadcast_to(value[None], (n,) + value.shape)
    got = lax.all_to_all(spread, axis, 0, 0, tiled=True)
    return got.reshape((n * value.shape[0],) + value.shape[1:])


def grp_gather(value):
    return a2a_gather(a2a_gather(value, "gy"), "gx")


def a2a_sum(parts, axis):
    got = lax.all_to_all(parts, axis, 0, 0, tiled=True)
    return jnp.sum(got.astype(jnp.float32), axis=0)


def attend_part(query, allowed, keys, values):
    score = jnp.dot(query, keys.T, preferred_element_type=jnp.float32) * DH ** (-0.5)
    top = jnp.max(jnp.where(allowed, score, -1e30), axis=1)
    expo = jnp.where(allowed, jnp.exp(score - top[:, None]), 0.0)
    total = jnp.sum(expo, axis=1)
    acc = jnp.dot(expo.astype(jnp.bfloat16), values, preferred_element_type=jnp.float32)
    return top, total, acc


def body(
    patches,
    patch_image,
    vis_gain,
    vis_bias,
    vis_qkv,
    vis_out,
    merge_weight,
    positions,
    text,
    dec_gain,
    dec_bias,
    dec_qkv,
):
    groups = lax.axis_size(GRP)
    here = lax.axis_index(GRP)
    rows = patches.shape[0]
    merged_count = rows // 4
    text_count = text.shape[0]
    tok = text_count + merged_count
    cap = merged_count // min(groups, 16)

    tnorm = normalize(text.astype(jnp.float32), dec_gain, dec_bias).astype(jnp.bfloat16)
    tproj = jnp.einsum("td,sde->ste", tnorm, dec_qkv, preferred_element_type=jnp.float32).astype(
        jnp.bfloat16
    )
    digit = 128
    pad_rows = 8
    lanes = 2 * DH
    pos_rows = jnp.stack([positions // digit, positions % digit]).astype(jnp.bfloat16)
    extra = jnp.zeros((pad_rows, lanes), jnp.bfloat16).at[:2].set(pos_rows.reshape(2, lanes))
    payload = jnp.concatenate([jnp.concatenate([tproj[1], tproj[2]], axis=1), extra], axis=0)
    text_kv = lax.all_gather(payload, GRP, axis=0, tiled=True)
    digits = text_kv.reshape(groups, text_count + pad_rows, lanes)[:, text_count : text_count + 2]
    digits = digits.astype(jnp.int32)
    all_pos = (digits[:, 0] * digit + digits[:, 1]).reshape(-1)

    place = jnp.arange(tok, dtype=jnp.int32)
    flags = jnp.sum((all_pos[None, :] == (here * tok + place)[:, None]).astype(jnp.int32), axis=1)
    free = 1 - flags
    text_rank = jnp.cumsum(free) - 1
    pick = (free[:, None] == 1) & (text_rank[:, None] == jnp.arange(text_count, dtype=jnp.int32)[None, :])
    own_text_pos = jnp.sum(jnp.where(pick, place[:, None], 0), axis=0) + here * tok

    heads = vis_qkv.shape[2] // HD
    patches_f = patches.astype(jnp.float32)
    normed = normalize(patches_f, vis_gain, vis_bias).astype(jnp.bfloat16)
    proj = jnp.einsum("pd,sde->spe", normed, vis_qkv, preferred_element_type=jnp.float32).astype(
        jnp.bfloat16
    )
    query = proj[0].reshape(rows, heads, HD)
    swap = [(i, i ^ 1) for i in range(lax.axis_size("gy"))]
    partner_kv, partner_ids = lax.ppermute((proj[1:], patch_image), "gy", swap)
    both_kv = jnp.concatenate([proj[1:], partner_kv], axis=1)
    both_ids = jnp.concatenate([patch_image, partner_ids], axis=0)
    keys = both_kv[0].reshape(2 * rows, heads, HD)
    values = both_kv[1].reshape(2 * rows, heads, HD)
    scores = jnp.einsum("phe,khe->hpk", query, keys, preferred_element_type=jnp.float32) * HD ** (
        -0.5
    )
    same = patch_image[:, None] == both_ids[None, :]
    top = jnp.max(jnp.where(same, scores, -1e30), axis=2, keepdims=True)
    expo = jnp.where(same, jnp.exp(scores - top), 0.0)
    weights = (expo / jnp.sum(expo, axis=2, keepdims=True)).astype(jnp.bfloat16)
    attended = jnp.einsum(
        "hpk,khe->phe", weights, values, preferred_element_type=jnp.float32
    ).astype(jnp.bfloat16)
    attended = attended.reshape(rows, heads * HD)

    nz = lax.axis_size("z")
    ncore = lax.axis_size("core")
    width = patches.shape[1] // (nz * ncore)
    mixed_parts = lax.dot_general(
        vis_out, attended, (((0,), (1,)), ((), ())), preferred_element_type=jnp.float32
    ).astype(jnp.bfloat16)
    mixed_parts = mixed_parts.reshape(nz, ncore, width, rows).transpose(1, 0, 2, 3)
    half = a2a_sum(mixed_parts, "core").astype(jnp.bfloat16)
    mixed = a2a_sum(half, "z")
    own_cols = lax.dynamic_slice_in_dim(patches_f, lax.axis_index(TP) * width, width, 1)
    visual = (mixed + own_cols.T).astype(jnp.bfloat16)
    windows = visual.reshape(width, merged_count, 4)
    partial_rows = jnp.einsum(
        "cmk,kce->me", windows, merge_weight, preferred_element_type=jnp.float32
    ).astype(jnp.bfloat16)
    ntp = nz * ncore
    merged = a2a_gather(
        a2a_sum(partial_rows.reshape(ntp, merged_count // ntp, -1), TP).astype(jnp.bfloat16), TP
    )

    mnorm = normalize(merged.astype(jnp.float32), dec_gain, dec_bias).astype(jnp.bfloat16)
    mproj = jnp.einsum("td,sde->ste", mnorm, dec_qkv, preferred_element_type=jnp.float32).astype(
        jnp.bfloat16
    )
    merged_kv = grp_gather(jnp.concatenate([mproj[1], mproj[2]], axis=1))

    query_pos = jnp.concatenate([own_text_pos, positions], axis=0)
    block = positions // tok
    seen = jnp.sum(
        ((all_pos[None, :] >= (block * tok)[:, None]) & (all_pos[None, :] <= positions[:, None])).astype(
            jnp.int32
        ),
        axis=1,
    )
    merged_limit = block * text_count + (positions - block * tok + 1 - seen)
    text_limit = here * text_count + jnp.arange(text_count, dtype=jnp.int32) + 1
    key_row = jnp.arange(groups * (text_count + pad_rows), dtype=jnp.int32)
    key_grp = key_row // (text_count + pad_rows)
    key_in = key_row % (text_count + pad_rows)
    text_key = jnp.where(key_in < text_count, key_grp * text_count + key_in, groups * tok)
    text_keys, text_values = text_kv[:, :DH], text_kv[:, DH:]
    part_tt = attend_part(tproj[0], text_key[None, :] < text_limit[:, None], text_keys, text_values)
    part_mt = attend_part(mproj[0], text_key[None, :] < merged_limit[:, None], text_keys, text_values)
    part_t = [jnp.concatenate([a, b], axis=0) for a, b in zip(part_tt, part_mt)]
    top_t, total_t, acc_t = part_t
    dquery = jnp.concatenate([tproj[0], mproj[0]], axis=0)
    top_m, total_m, acc_m = attend_part(
        dquery, all_pos[None, :] <= query_pos[:, None], merged_kv[:, :DH], merged_kv[:, DH:]
    )
    best = jnp.maximum(top_t, top_m)
    scale_t = jnp.exp(top_t - best)
    scale_m = jnp.exp(top_m - best)
    total = total_t * scale_t + total_m * scale_m
    acc = acc_t * scale_t[:, None] + acc_m * scale_m[:, None]
    result = (acc / total[:, None]).astype(jnp.bfloat16)
    text_out = result[:text_count]
    merged_out = result[text_count:]

    target = positions // tok
    member = (target[:, None] == jnp.arange(groups, dtype=jnp.int32)[None, :]).astype(jnp.int32)
    rank = jnp.sum(jnp.cumsum(member, axis=0) * member, axis=1) - 1
    slot = target * cap + rank
    select = slot[None, :] == jnp.arange(groups * cap, dtype=jnp.int32)[:, None]
    packed = jnp.dot(
        select.astype(jnp.bfloat16), merged_out, preferred_element_type=jnp.float32
    ).astype(jnp.bfloat16)
    got = lax.all_to_all(packed, GRP, 0, 0, tiled=True)

    src_pos = all_pos.reshape(groups, merged_count)
    to_me = (src_pos // tok) == here
    src_rank = jnp.cumsum(to_me.astype(jnp.int32), axis=1) - 1
    slot_hit = to_me[:, :, None] & (
        src_rank[:, :, None] == jnp.arange(cap, dtype=jnp.int32)[None, None, :]
    )
    got_pos = jnp.sum(jnp.where(slot_hit, src_pos[:, :, None] + 1, 0), axis=1).reshape(-1) - 1
    local = got_pos - here * tok
    landing = (local[None, :] == place[:, None]) & (got_pos[None, :] >= 0)
    text_land = own_text_pos[None, :] - here * tok == place[:, None]
    out = jnp.dot(landing.astype(jnp.bfloat16), got, preferred_element_type=jnp.float32)
    out = out + jnp.dot(
        text_land.astype(jnp.bfloat16), text_out, preferred_element_type=jnp.float32
    )
    return out.astype(jnp.bfloat16)


def solution(mesh):
    grid = mesh.devices.reshape(4, mesh.devices.shape[0] // 4, mesh.devices.shape[1] // 2, 2)
    mesh4 = Mesh(grid, GRP + TP)
    in_specs = (
        P(GRP, None),
        P(GRP),
        P(),
        P(),
        P(None, None, TP),
        P(TP, None),
        P(None, TP, None),
        P(GRP),
        P(GRP, None),
        P(),
        P(),
        P(None, None, TP),
    )
    out_specs = P(GRP, TP)
    return jax.shard_map(body, mesh=mesh4, in_specs=in_specs, out_specs=out_specs, check_vma=False)
```

```python
import jax
import jax.numpy as jnp
from jax import lax
from jax.sharding import Mesh
from jax.sharding import PartitionSpec as P

HD = 104
DH = 64

layer_eps = 1e-05

GRP = ("gx", "gy")
TP = ("z", "core")


def normalize(values, gain, bias):
    mean = jnp.mean(values, axis=-1, keepdims=True)
    centred = values - mean
    spread = jnp.mean(centred * centred, axis=-1, keepdims=True)
    return centred * lax.rsqrt(spread + layer_eps) * gain + bias


def a2a_gather(value, axis):
    n = lax.axis_size(axis)
    spread = jnp.broadcast_to(value[None], (n,) + value.shape)
    got = lax.all_to_all(spread, axis, 0, 0, tiled=True)
    return got.reshape((n * value.shape[0],) + value.shape[1:])


def grp_gather(value):
    return a2a_gather(a2a_gather(value, "gy"), "gx")


def a2a_sum(parts, axis):
    got = lax.all_to_all(parts, axis, 0, 0, tiled=True)
    return jnp.sum(got.astype(jnp.float32), axis=0)


def attend_part(query, allowed, keys, values):
    score = jnp.dot(query, keys.T, preferred_element_type=jnp.float32) * DH ** (-0.5)
    top = jnp.max(jnp.where(allowed, score, -1e30), axis=1)
    expo = jnp.where(allowed, jnp.exp(score - top[:, None]), 0.0)
    total = jnp.sum(expo, axis=1)
    acc = jnp.dot(expo.astype(jnp.bfloat16), values, preferred_element_type=jnp.float32)
    return top, total, acc


def body(
    patches,
    patch_image,
    vis_gain,
    vis_bias,
    vis_qkv,
    vis_out,
    merge_weight,
    positions,
    text,
    dec_gain,
    dec_bias,
    dec_qkv,
):
    groups = lax.axis_size(GRP)
    here = lax.axis_index(GRP)
    rows = patches.shape[0]
    merged_count = rows // 4
    text_count = text.shape[0]
    tok = text_count + merged_count
    cap = merged_count // min(groups, 16)

    tnorm = normalize(text.astype(jnp.float32), dec_gain, dec_bias).astype(jnp.bfloat16)
    tproj = jnp.einsum("td,sde->ste", tnorm, dec_qkv, preferred_element_type=jnp.float32).astype(
        jnp.bfloat16
    )
    digit = 128
    pad_rows = 8
    lanes = 2 * DH
    pos_rows = jnp.stack([positions // digit, positions % digit]).astype(jnp.bfloat16)
    extra = jnp.zeros((pad_rows, lanes), jnp.bfloat16).at[:2].set(pos_rows.reshape(2, lanes))
    payload = jnp.concatenate([jnp.concatenate([tproj[1], tproj[2]], axis=1), extra], axis=0)
    text_kv = lax.all_gather(payload, GRP, axis=0, tiled=True)
    digits = text_kv.reshape(groups, text_count + pad_rows, lanes)[:, text_count : text_count + 2]
    digits = digits.astype(jnp.int32)
    all_pos = (digits[:, 0] * digit + digits[:, 1]).reshape(-1)

    place = jnp.arange(tok, dtype=jnp.int32)
    flags = jnp.sum((all_pos[None, :] == (here * tok + place)[:, None]).astype(jnp.int32), axis=1)
    free = 1 - flags
    text_rank = jnp.cumsum(free) - 1
    pick = (free[:, None] == 1) & (text_rank[:, None] == jnp.arange(text_count, dtype=jnp.int32)[None, :])
    own_text_pos = jnp.sum(jnp.where(pick, place[:, None], 0), axis=0) + here * tok

    heads = vis_qkv.shape[2] // HD
    patches_f = patches.astype(jnp.float32)
    normed = normalize(patches_f, vis_gain, vis_bias).astype(jnp.bfloat16)
    proj = jnp.einsum("pd,sde->spe", normed, vis_qkv, preferred_element_type=jnp.float32).astype(
        jnp.bfloat16
    )
    query = proj[0].reshape(rows, heads, HD)
    swap = [(i, i ^ 1) for i in range(lax.axis_size("gy"))]
    partner_kv, partner_ids = lax.ppermute((proj[1:], patch_image), "gy", swap)
    both_kv = jnp.concatenate([proj[1:], partner_kv], axis=1)
    both_ids = jnp.concatenate([patch_image, partner_ids], axis=0)
    keys = both_kv[0].reshape(2 * rows, heads, HD)
    values = both_kv[1].reshape(2 * rows, heads, HD)
    scores = jnp.einsum("phe,khe->hpk", query, keys, preferred_element_type=jnp.float32) * HD ** (
        -0.5
    )
    same = patch_image[:, None] == both_ids[None, :]
    top = jnp.max(jnp.where(same, scores, -1e30), axis=2, keepdims=True)
    expo = jnp.where(same, jnp.exp(scores - top), 0.0)
    weights = (expo / jnp.sum(expo, axis=2, keepdims=True)).astype(jnp.bfloat16)
    attended = jnp.einsum(
        "hpk,khe->phe", weights, values, preferred_element_type=jnp.float32
    ).astype(jnp.bfloat16)
    attended = attended.reshape(rows, heads * HD)

    nz = lax.axis_size("z")
    ncore = lax.axis_size("core")
    width = patches.shape[1] // (nz * ncore)
    mixed_parts = lax.dot_general(
        vis_out, attended, (((0,), (1,)), ((), ())), preferred_element_type=jnp.float32
    ).astype(jnp.bfloat16)
    mixed_parts = mixed_parts.reshape(nz, ncore, width, rows)
    core = lax.axis_index("core")
    keep = lax.dynamic_index_in_dim(mixed_parts, core, 1, keepdims=False)
    send = lax.dynamic_index_in_dim(mixed_parts, 1 - core, 1, keepdims=False)
    pair = [(i, i ^ 1) for i in range(ncore)]
    half = (
        keep.astype(jnp.float32) + lax.ppermute(send, "core", pair).astype(jnp.float32)
    ).astype(jnp.bfloat16)
    mixed = a2a_sum(half, "z")
    own_cols = lax.dynamic_slice_in_dim(patches_f, lax.axis_index(TP) * width, width, 1)
    visual = (mixed + own_cols.T).astype(jnp.bfloat16)
    windows = visual.reshape(width, merged_count, 4)
    partial_rows = jnp.einsum(
        "cmk,kce->me", windows, merge_weight, preferred_element_type=jnp.float32
    ).astype(jnp.bfloat16)
    ntp = nz * ncore
    merged = a2a_gather(
        a2a_sum(partial_rows.reshape(ntp, merged_count // ntp, -1), TP).astype(jnp.bfloat16), TP
    )

    mnorm = normalize(merged.astype(jnp.float32), dec_gain, dec_bias).astype(jnp.bfloat16)
    mproj = jnp.einsum("td,sde->ste", mnorm, dec_qkv, preferred_element_type=jnp.float32).astype(
        jnp.bfloat16
    )
    merged_kv = grp_gather(jnp.concatenate([mproj[1], mproj[2]], axis=1))

    query_pos = jnp.concatenate([own_text_pos, positions], axis=0)
    block = positions // tok
    seen = jnp.sum(
        ((all_pos[None, :] >= (block * tok)[:, None]) & (all_pos[None, :] <= positions[:, None])).astype(
            jnp.int32
        ),
        axis=1,
    )
    merged_limit = block * text_count + (positions - block * tok + 1 - seen)
    text_limit = here * text_count + jnp.arange(text_count, dtype=jnp.int32) + 1
    key_row = jnp.arange(groups * (text_count + pad_rows), dtype=jnp.int32)
    key_grp = key_row // (text_count + pad_rows)
    key_in = key_row % (text_count + pad_rows)
    text_key = jnp.where(key_in < text_count, key_grp * text_count + key_in, groups * tok)
    text_keys, text_values = text_kv[:, :DH], text_kv[:, DH:]
    part_tt = attend_part(tproj[0], text_key[None, :] < text_limit[:, None], text_keys, text_values)
    part_mt = attend_part(mproj[0], text_key[None, :] < merged_limit[:, None], text_keys, text_values)
    part_t = [jnp.concatenate([a, b], axis=0) for a, b in zip(part_tt, part_mt)]
    top_t, total_t, acc_t = part_t
    dquery = jnp.concatenate([tproj[0], mproj[0]], axis=0)
    top_m, total_m, acc_m = attend_part(
        dquery, all_pos[None, :] <= query_pos[:, None], merged_kv[:, :DH], merged_kv[:, DH:]
    )
    best = jnp.maximum(top_t, top_m)
    scale_t = jnp.exp(top_t - best)
    scale_m = jnp.exp(top_m - best)
    total = total_t * scale_t + total_m * scale_m
    acc = acc_t * scale_t[:, None] + acc_m * scale_m[:, None]
    result = (acc / total[:, None]).astype(jnp.bfloat16)
    text_out = result[:text_count]
    merged_out = result[text_count:]

    target = positions // tok
    member = (target[:, None] == jnp.arange(groups, dtype=jnp.int32)[None, :]).astype(jnp.int32)
    rank = jnp.sum(jnp.cumsum(member, axis=0) * member, axis=1) - 1
    slot = target * cap + rank
    select = slot[None, :] == jnp.arange(groups * cap, dtype=jnp.int32)[:, None]
    packed = jnp.dot(
        select.astype(jnp.bfloat16), merged_out, preferred_element_type=jnp.float32
    ).astype(jnp.bfloat16)
    got = lax.all_to_all(packed, GRP, 0, 0, tiled=True)

    src_pos = all_pos.reshape(groups, merged_count)
    to_me = (src_pos // tok) == here
    src_rank = jnp.cumsum(to_me.astype(jnp.int32), axis=1) - 1
    slot_hit = to_me[:, :, None] & (
        src_rank[:, :, None] == jnp.arange(cap, dtype=jnp.int32)[None, None, :]
    )
    got_pos = jnp.sum(jnp.where(slot_hit, src_pos[:, :, None] + 1, 0), axis=1).reshape(-1) - 1
    local = got_pos - here * tok
    landing = (local[None, :] == place[:, None]) & (got_pos[None, :] >= 0)
    text_land = own_text_pos[None, :] - here * tok == place[:, None]
    out = jnp.dot(landing.astype(jnp.bfloat16), got, preferred_element_type=jnp.float32)
    out = out + jnp.dot(
        text_land.astype(jnp.bfloat16), text_out, preferred_element_type=jnp.float32
    )
    return out.astype(jnp.bfloat16)


def solution(mesh):
    grid = mesh.devices.reshape(4, mesh.devices.shape[0] // 4, mesh.devices.shape[1] // 2, 2)
    mesh4 = Mesh(grid, GRP + TP)
    in_specs = (
        P(GRP, None),
        P(GRP),
        P(),
        P(),
        P(None, None, TP),
        P(TP, None),
        P(None, TP, None),
        P(GRP),
        P(GRP, None),
        P(),
        P(),
        P(None, None, TP),
    )
    out_specs = P(GRP, TP)
    return jax.shard_map(body, mesh=mesh4, in_specs=in_specs, out_specs=out_specs, check_vma=False)
```

```python
import jax
import jax.numpy as jnp
from jax import lax
from jax.sharding import Mesh
from jax.sharding import PartitionSpec as P

HD = 104
DH = 64

layer_eps = 1e-05

GRP = ("gx", "gy")
TP = ("z", "core")


def normalize(values, gain, bias):
    mean = jnp.mean(values, axis=-1, keepdims=True)
    centred = values - mean
    spread = jnp.mean(centred * centred, axis=-1, keepdims=True)
    return centred * lax.rsqrt(spread + layer_eps) * gain + bias


def a2a_gather(value, axis):
    n = lax.axis_size(axis)
    spread = jnp.broadcast_to(value[None], (n,) + value.shape)
    got = lax.all_to_all(spread, axis, 0, 0, tiled=True)
    return got.reshape((n * value.shape[0],) + value.shape[1:])


def grp_gather(value):
    return a2a_gather(a2a_gather(value, "gy"), "gx")


def a2a_sum(parts, axis):
    got = lax.all_to_all(parts, axis, 0, 0, tiled=True)
    return jnp.sum(got.astype(jnp.float32), axis=0)


def attend_part(query, allowed, keys, values):
    score = jnp.dot(query, keys.T, preferred_element_type=jnp.float32) * DH ** (-0.5)
    top = jnp.max(jnp.where(allowed, score, -1e30), axis=1)
    expo = jnp.where(allowed, jnp.exp(score - top[:, None]), 0.0)
    total = jnp.sum(expo, axis=1)
    acc = jnp.dot(expo.astype(jnp.bfloat16), values, preferred_element_type=jnp.float32)
    return top, total, acc


def body(
    patches,
    patch_image,
    vis_gain,
    vis_bias,
    vis_qkv,
    vis_out,
    merge_weight,
    positions,
    text,
    dec_gain,
    dec_bias,
    dec_qkv,
):
    groups = lax.axis_size(GRP)
    here = lax.axis_index(GRP)
    rows = patches.shape[0]
    merged_count = rows // 4
    text_count = text.shape[0]
    tok = text_count + merged_count
    cap = merged_count // min(groups, 16)

    tnorm = normalize(text.astype(jnp.float32), dec_gain, dec_bias).astype(jnp.bfloat16)
    tproj = jnp.einsum("td,sde->ste", tnorm, dec_qkv, preferred_element_type=jnp.float32).astype(
        jnp.bfloat16
    )
    digit = 128
    pad_rows = 8
    lanes = 2 * DH
    pos_rows = jnp.stack([positions // digit, positions % digit]).astype(jnp.bfloat16)
    extra = jnp.zeros((pad_rows, lanes), jnp.bfloat16).at[:2].set(pos_rows.reshape(2, lanes))
    payload = jnp.concatenate([jnp.concatenate([tproj[1], tproj[2]], axis=1), extra], axis=0)
    text_kv = lax.all_gather(payload, GRP, axis=0, tiled=True)
    digits = text_kv.reshape(groups, text_count + pad_rows, lanes)[:, text_count : text_count + 2]
    digits = digits.astype(jnp.int32)
    all_pos = (digits[:, 0] * digit + digits[:, 1]).reshape(-1)

    place = jnp.arange(tok, dtype=jnp.int32)
    flags = jnp.sum((all_pos[None, :] == (here * tok + place)[:, None]).astype(jnp.int32), axis=1)
    free = 1 - flags
    text_rank = jnp.cumsum(free) - 1
    pick = (free[:, None] == 1) & (text_rank[:, None] == jnp.arange(text_count, dtype=jnp.int32)[None, :])
    own_text_pos = jnp.sum(jnp.where(pick, place[:, None], 0), axis=0) + here * tok

    heads = vis_qkv.shape[2] // HD
    patches_f = patches.astype(jnp.float32)
    normed = normalize(patches_f, vis_gain, vis_bias).astype(jnp.bfloat16)
    proj = jnp.einsum("pd,sde->spe", normed, vis_qkv, preferred_element_type=jnp.float32).astype(
        jnp.bfloat16
    )
    query = proj[0].reshape(rows, heads, HD)
    swap = [(i, i ^ 1) for i in range(lax.axis_size("gy"))]
    partner_kv, partner_ids = lax.ppermute((proj[1:], patch_image), "gy", swap)
    both_kv = jnp.concatenate([proj[1:], partner_kv], axis=1)
    both_ids = jnp.concatenate([patch_image, partner_ids], axis=0)
    keys = both_kv[0].reshape(2 * rows, heads, HD)
    values = both_kv[1].reshape(2 * rows, heads, HD)
    scores = jnp.einsum("phe,khe->hpk", query, keys, preferred_element_type=jnp.float32) * HD ** (
        -0.5
    )
    same = patch_image[:, None] == both_ids[None, :]
    top = jnp.max(jnp.where(same, scores, -1e30), axis=2, keepdims=True)
    expo = jnp.where(same, jnp.exp(scores - top), 0.0)
    weights = (expo / jnp.sum(expo, axis=2, keepdims=True)).astype(jnp.bfloat16)
    attended = jnp.einsum(
        "hpk,khe->phe", weights, values, preferred_element_type=jnp.float32
    ).astype(jnp.bfloat16)
    attended = attended.reshape(rows, heads * HD)

    nz = lax.axis_size("z")
    ncore = lax.axis_size("core")
    width = patches.shape[1] // (nz * ncore)
    core = lax.axis_index("core")
    vo = vis_out.reshape(vis_out.shape[0], nz, ncore, width)
    keep_w = lax.dynamic_index_in_dim(vo, core, 2, keepdims=False)
    send_w = lax.dynamic_index_in_dim(vo, 1 - core, 2, keepdims=False)
    keep = jnp.einsum("pe,ezf->zfp", attended, keep_w, preferred_element_type=jnp.float32)
    send = jnp.einsum("pe,ezf->zfp", attended, send_w, preferred_element_type=jnp.float32)
    pair = [(i, i ^ 1) for i in range(ncore)]
    half = (
        keep.astype(jnp.bfloat16).astype(jnp.float32)
        + lax.ppermute(send.astype(jnp.bfloat16), "core", pair).astype(jnp.float32)
    ).astype(jnp.bfloat16)
    mixed = a2a_sum(half, "z")
    own_cols = lax.dynamic_slice_in_dim(patches, lax.axis_index(TP) * width, width, 1)
    visual = (mixed + own_cols.astype(jnp.float32).T).astype(jnp.bfloat16)
    windows = visual.reshape(width, merged_count, 4)
    partial_rows = jnp.einsum(
        "cmk,kce->me", windows, merge_weight, preferred_element_type=jnp.float32
    ).astype(jnp.bfloat16)
    ntp = nz * ncore
    merged = a2a_gather(
        a2a_sum(partial_rows.reshape(ntp, merged_count // ntp, -1), TP).astype(jnp.bfloat16), TP
    )

    mnorm = normalize(merged.astype(jnp.float32), dec_gain, dec_bias).astype(jnp.bfloat16)
    mproj = jnp.einsum("td,sde->ste", mnorm, dec_qkv, preferred_element_type=jnp.float32).astype(
        jnp.bfloat16
    )
    merged_kv = grp_gather(jnp.concatenate([mproj[1], mproj[2]], axis=1))

    query_pos = jnp.concatenate([own_text_pos, positions], axis=0)
    block = positions // tok
    seen = jnp.sum(
        ((all_pos[None, :] >= (block * tok)[:, None]) & (all_pos[None, :] <= positions[:, None])).astype(
            jnp.int32
        ),
        axis=1,
    )
    merged_limit = block * text_count + (positions - block * tok + 1 - seen)
    text_limit = here * text_count + jnp.arange(text_count, dtype=jnp.int32) + 1
    key_row = jnp.arange(groups * (text_count + pad_rows), dtype=jnp.int32)
    key_grp = key_row // (text_count + pad_rows)
    key_in = key_row % (text_count + pad_rows)
    text_key = jnp.where(key_in < text_count, key_grp * text_count + key_in, groups * tok)
    text_keys, text_values = text_kv[:, :DH], text_kv[:, DH:]
    part_tt = attend_part(tproj[0], text_key[None, :] < text_limit[:, None], text_keys, text_values)
    part_mt = attend_part(mproj[0], text_key[None, :] < merged_limit[:, None], text_keys, text_values)
    part_t = [jnp.concatenate([a, b], axis=0) for a, b in zip(part_tt, part_mt)]
    top_t, total_t, acc_t = part_t
    dquery = jnp.concatenate([tproj[0], mproj[0]], axis=0)
    top_m, total_m, acc_m = attend_part(
        dquery, all_pos[None, :] <= query_pos[:, None], merged_kv[:, :DH], merged_kv[:, DH:]
    )
    best = jnp.maximum(top_t, top_m)
    scale_t = jnp.exp(top_t - best)
    scale_m = jnp.exp(top_m - best)
    total = total_t * scale_t + total_m * scale_m
    acc = acc_t * scale_t[:, None] + acc_m * scale_m[:, None]
    result = (acc / total[:, None]).astype(jnp.bfloat16)
    text_out = result[:text_count]
    merged_out = result[text_count:]

    target = positions // tok
    member = (target[:, None] == jnp.arange(groups, dtype=jnp.int32)[None, :]).astype(jnp.int32)
    rank = jnp.sum(jnp.cumsum(member, axis=0) * member, axis=1) - 1
    slot = target * cap + rank
    select = slot[None, :] == jnp.arange(groups * cap, dtype=jnp.int32)[:, None]
    packed = jnp.dot(
        select.astype(jnp.bfloat16), merged_out, preferred_element_type=jnp.float32
    ).astype(jnp.bfloat16)
    got = lax.all_to_all(packed, GRP, 0, 0, tiled=True)

    src_pos = all_pos.reshape(groups, merged_count)
    to_me = (src_pos // tok) == here
    src_rank = jnp.cumsum(to_me.astype(jnp.int32), axis=1) - 1
    slot_hit = to_me[:, :, None] & (
        src_rank[:, :, None] == jnp.arange(cap, dtype=jnp.int32)[None, None, :]
    )
    got_pos = jnp.sum(jnp.where(slot_hit, src_pos[:, :, None] + 1, 0), axis=1).reshape(-1) - 1
    local = got_pos - here * tok
    landing = (local[None, :] == place[:, None]) & (got_pos[None, :] >= 0)
    text_land = own_text_pos[None, :] - here * tok == place[:, None]
    out = jnp.dot(landing.astype(jnp.bfloat16), got, preferred_element_type=jnp.float32)
    out = out + jnp.dot(
        text_land.astype(jnp.bfloat16), text_out, preferred_element_type=jnp.float32
    )
    return out.astype(jnp.bfloat16)


def solution(mesh):
    grid = mesh.devices.reshape(4, mesh.devices.shape[0] // 4, mesh.devices.shape[1] // 2, 2)
    mesh4 = Mesh(grid, GRP + TP)
    in_specs = (
        P(GRP, None),
        P(GRP),
        P(),
        P(),
        P(None, None, TP),
        P(TP, None),
        P(None, TP, None),
        P(GRP),
        P(GRP, None),
        P(),
        P(),
        P(None, None, TP),
    )
    out_specs = P(GRP, TP)
    return jax.shard_map(body, mesh=mesh4, in_specs=in_specs, out_specs=out_specs, check_vma=False)
```

```python
import jax
import jax.numpy as jnp
from jax import lax
from jax.sharding import Mesh
from jax.sharding import PartitionSpec as P

HD = 104
DH = 64

layer_eps = 1e-05

GRP = ("gx", "gy")
TP = ("z", "core")


def normalize(values, gain, bias):
    mean = jnp.mean(values, axis=-1, keepdims=True)
    centred = values - mean
    spread = jnp.mean(centred * centred, axis=-1, keepdims=True)
    return centred * lax.rsqrt(spread + layer_eps) * gain + bias


def a2a_gather(value, axis):
    n = lax.axis_size(axis)
    spread = jnp.broadcast_to(value[None], (n,) + value.shape)
    got = lax.all_to_all(spread, axis, 0, 0, tiled=True)
    return got.reshape((n * value.shape[0],) + value.shape[1:])


def grp_gather(value):
    return a2a_gather(a2a_gather(value, "gy"), "gx")


def a2a_sum(parts, axis):
    got = lax.all_to_all(parts, axis, 0, 0, tiled=True)
    return jnp.sum(got.astype(jnp.float32), axis=0)


def attend_part(query, allowed, keys, values):
    score = jnp.dot(query, keys.T, preferred_element_type=jnp.float32) * DH ** (-0.5)
    top = jnp.max(jnp.where(allowed, score, -1e30), axis=1)
    expo = jnp.where(allowed, jnp.exp(score - top[:, None]), 0.0)
    total = jnp.sum(expo, axis=1)
    acc = jnp.dot(expo.astype(jnp.bfloat16), values, preferred_element_type=jnp.float32)
    return top, total, acc


def body(
    patches,
    patch_image,
    vis_gain,
    vis_bias,
    vis_qkv,
    vis_out,
    merge_weight,
    positions,
    text,
    dec_gain,
    dec_bias,
    dec_qkv,
):
    groups = lax.axis_size(GRP)
    here = lax.axis_index(GRP)
    rows = patches.shape[0]
    merged_count = rows // 4
    text_count = text.shape[0]
    tok = text_count + merged_count
    cap = merged_count // min(groups, 16)

    tnorm = normalize(text.astype(jnp.float32), dec_gain, dec_bias).astype(jnp.bfloat16)
    tproj = jnp.einsum("td,sde->ste", tnorm, dec_qkv, preferred_element_type=jnp.float32).astype(
        jnp.bfloat16
    )
    digit = 128
    pad_rows = 8
    lanes = 2 * DH
    pos_rows = jnp.stack([positions // digit, positions % digit]).astype(jnp.bfloat16)
    extra = jnp.zeros((pad_rows, lanes), jnp.bfloat16).at[:2].set(pos_rows.reshape(2, lanes))
    payload = jnp.concatenate([jnp.concatenate([tproj[1], tproj[2]], axis=1), extra], axis=0)
    text_kv = lax.all_gather(payload, GRP, axis=0, tiled=True)
    digits = text_kv.reshape(groups, text_count + pad_rows, lanes)[:, text_count : text_count + 2]
    digits = digits.astype(jnp.int32)
    all_pos = (digits[:, 0] * digit + digits[:, 1]).reshape(-1)

    place = jnp.arange(tok, dtype=jnp.int32)
    flags = jnp.sum((all_pos[None, :] == (here * tok + place)[:, None]).astype(jnp.int32), axis=1)
    free = 1 - flags
    text_rank = jnp.cumsum(free) - 1
    pick = (free[:, None] == 1) & (text_rank[:, None] == jnp.arange(text_count, dtype=jnp.int32)[None, :])
    own_text_pos = jnp.sum(jnp.where(pick, place[:, None], 0), axis=0) + here * tok

    heads = vis_qkv.shape[2] // HD
    patches_f = patches.astype(jnp.float32)
    normed = normalize(patches_f, vis_gain, vis_bias).astype(jnp.bfloat16)
    proj = jnp.einsum("pd,sde->spe", normed, vis_qkv, preferred_element_type=jnp.float32).astype(
        jnp.bfloat16
    )
    query = proj[0].reshape(rows, heads, HD)
    swap = [(i, i ^ 1) for i in range(lax.axis_size("gy"))]
    partner_kv, partner_ids = lax.ppermute((proj[1:], patch_image), "gy", swap)
    both_kv = jnp.concatenate([proj[1:], partner_kv], axis=1)
    both_ids = jnp.concatenate([patch_image, partner_ids], axis=0)
    keys = both_kv[0].reshape(2 * rows, heads, HD)
    values = both_kv[1].reshape(2 * rows, heads, HD)
    scores = jnp.einsum("phe,khe->hpk", query, keys, preferred_element_type=jnp.float32) * HD ** (
        -0.5
    )
    same = patch_image[:, None] == both_ids[None, :]
    top = jnp.max(jnp.where(same, scores, -1e30), axis=2, keepdims=True)
    expo = jnp.where(same, jnp.exp(scores - top), 0.0)
    weights = (expo / jnp.sum(expo, axis=2, keepdims=True)).astype(jnp.bfloat16)
    attended = jnp.einsum(
        "hpk,khe->phe", weights, values, preferred_element_type=jnp.float32
    ).astype(jnp.bfloat16)
    attended = attended.reshape(rows, heads * HD)

    nz = lax.axis_size("z")
    ncore = lax.axis_size("core")
    width = patches.shape[1] // (nz * ncore)
    core = lax.axis_index("core")
    vo = vis_out.reshape(vis_out.shape[0], nz, ncore, width)
    keep_w = lax.dynamic_index_in_dim(vo, core, 2, keepdims=False)
    send_w = lax.dynamic_index_in_dim(vo, 1 - core, 2, keepdims=False)
    keep = jnp.einsum("pe,ezf->zfp", attended, keep_w, preferred_element_type=jnp.float32)
    send = jnp.einsum("pe,ezf->zfp", attended, send_w, preferred_element_type=jnp.float32)
    pair = [(i, i ^ 1) for i in range(ncore)]
    half = (
        keep.astype(jnp.bfloat16).astype(jnp.float32)
        + lax.ppermute(send.astype(jnp.bfloat16), "core", pair).astype(jnp.float32)
    ).astype(jnp.bfloat16)
    mixed = a2a_sum(half, "z")
    own_cols = lax.dynamic_slice_in_dim(patches, lax.axis_index(TP) * width, width, 1)
    visual = (mixed + own_cols.astype(jnp.float32).T).astype(jnp.bfloat16)
    windows = visual.reshape(width, merged_count, 4)
    partial_rows = jnp.einsum(
        "cmk,kce->me", windows, merge_weight, preferred_element_type=jnp.float32
    ).astype(jnp.bfloat16)
    ntp = nz * ncore
    chip_rows = (
        partial_rows.astype(jnp.float32)
        + lax.ppermute(partial_rows, "core", pair).astype(jnp.float32)
    ).astype(jnp.bfloat16)
    merged = a2a_gather(
        a2a_sum(chip_rows.reshape(nz, merged_count // nz, -1), "z").astype(jnp.bfloat16), "z"
    )

    mnorm = normalize(merged.astype(jnp.float32), dec_gain, dec_bias).astype(jnp.bfloat16)
    mproj = jnp.einsum("td,sde->ste", mnorm, dec_qkv, preferred_element_type=jnp.float32).astype(
        jnp.bfloat16
    )
    merged_kv = grp_gather(jnp.concatenate([mproj[1], mproj[2]], axis=1))

    query_pos = jnp.concatenate([own_text_pos, positions], axis=0)
    block = positions // tok
    seen = jnp.sum(
        ((all_pos[None, :] >= (block * tok)[:, None]) & (all_pos[None, :] <= positions[:, None])).astype(
            jnp.int32
        ),
        axis=1,
    )
    merged_limit = block * text_count + (positions - block * tok + 1 - seen)
    text_limit = here * text_count + jnp.arange(text_count, dtype=jnp.int32) + 1
    key_row = jnp.arange(groups * (text_count + pad_rows), dtype=jnp.int32)
    key_grp = key_row // (text_count + pad_rows)
    key_in = key_row % (text_count + pad_rows)
    text_key = jnp.where(key_in < text_count, key_grp * text_count + key_in, groups * tok)
    text_keys, text_values = text_kv[:, :DH], text_kv[:, DH:]
    part_tt = attend_part(tproj[0], text_key[None, :] < text_limit[:, None], text_keys, text_values)
    part_mt = attend_part(mproj[0], text_key[None, :] < merged_limit[:, None], text_keys, text_values)
    part_t = [jnp.concatenate([a, b], axis=0) for a, b in zip(part_tt, part_mt)]
    top_t, total_t, acc_t = part_t
    dquery = jnp.concatenate([tproj[0], mproj[0]], axis=0)
    top_m, total_m, acc_m = attend_part(
        dquery, all_pos[None, :] <= query_pos[:, None], merged_kv[:, :DH], merged_kv[:, DH:]
    )
    best = jnp.maximum(top_t, top_m)
    scale_t = jnp.exp(top_t - best)
    scale_m = jnp.exp(top_m - best)
    total = total_t * scale_t + total_m * scale_m
    acc = acc_t * scale_t[:, None] + acc_m * scale_m[:, None]
    result = (acc / total[:, None]).astype(jnp.bfloat16)
    text_out = result[:text_count]
    merged_out = result[text_count:]

    target = positions // tok
    member = (target[:, None] == jnp.arange(groups, dtype=jnp.int32)[None, :]).astype(jnp.int32)
    rank = jnp.sum(jnp.cumsum(member, axis=0) * member, axis=1) - 1
    slot = target * cap + rank
    select = slot[None, :] == jnp.arange(groups * cap, dtype=jnp.int32)[:, None]
    packed = jnp.dot(
        select.astype(jnp.bfloat16), merged_out, preferred_element_type=jnp.float32
    ).astype(jnp.bfloat16)
    got = lax.all_to_all(packed, GRP, 0, 0, tiled=True)

    src_pos = all_pos.reshape(groups, merged_count)
    to_me = (src_pos // tok) == here
    src_rank = jnp.cumsum(to_me.astype(jnp.int32), axis=1) - 1
    slot_hit = to_me[:, :, None] & (
        src_rank[:, :, None] == jnp.arange(cap, dtype=jnp.int32)[None, None, :]
    )
    got_pos = jnp.sum(jnp.where(slot_hit, src_pos[:, :, None] + 1, 0), axis=1).reshape(-1) - 1
    local = got_pos - here * tok
    landing = (local[None, :] == place[:, None]) & (got_pos[None, :] >= 0)
    text_land = own_text_pos[None, :] - here * tok == place[:, None]
    out = jnp.dot(landing.astype(jnp.bfloat16), got, preferred_element_type=jnp.float32)
    out = out + jnp.dot(
        text_land.astype(jnp.bfloat16), text_out, preferred_element_type=jnp.float32
    )
    return out.astype(jnp.bfloat16)


def solution(mesh):
    grid = mesh.devices.reshape(4, mesh.devices.shape[0] // 4, mesh.devices.shape[1] // 2, 2)
    mesh4 = Mesh(grid, GRP + TP)
    in_specs = (
        P(GRP, None),
        P(GRP),
        P(),
        P(),
        P(None, None, TP),
        P(TP, None),
        P(None, TP, None),
        P(GRP),
        P(GRP, None),
        P(),
        P(),
        P(None, None, TP),
    )
    out_specs = P(GRP, TP)
    return jax.shard_map(body, mesh=mesh4, in_specs=in_specs, out_specs=out_specs, check_vma=False)
```

```python
import jax
import jax.numpy as jnp
from jax import lax
from jax.sharding import Mesh
from jax.sharding import PartitionSpec as P

HD = 104
DH = 64

layer_eps = 1e-05

GRP = ("gx", "gy")
TP = ("z", "core")


def normalize(values, gain, bias):
    mean = jnp.mean(values, axis=-1, keepdims=True)
    centred = values - mean
    spread = jnp.mean(centred * centred, axis=-1, keepdims=True)
    return centred * lax.rsqrt(spread + layer_eps) * gain + bias


def a2a_gather(value, axis):
    n = lax.axis_size(axis)
    spread = jnp.broadcast_to(value[None], (n,) + value.shape)
    got = lax.all_to_all(spread, axis, 0, 0, tiled=True)
    return got.reshape((n * value.shape[0],) + value.shape[1:])


def grp_gather(value):
    return a2a_gather(a2a_gather(value, "gy"), "gx")


def a2a_sum(parts, axis):
    got = lax.all_to_all(parts, axis, 0, 0, tiled=True)
    return jnp.sum(got.astype(jnp.float32), axis=0)


def attend_part(query, allowed, keys, values):
    score = jnp.dot(query, keys.T, preferred_element_type=jnp.float32) * DH ** (-0.5)
    top = jnp.max(jnp.where(allowed, score, -1e30), axis=1)
    expo = jnp.where(allowed, jnp.exp(score - top[:, None]), 0.0)
    total = jnp.sum(expo, axis=1)
    acc = jnp.dot(expo.astype(jnp.bfloat16), values, preferred_element_type=jnp.float32)
    return top, total, acc


def body(
    patches,
    patch_image,
    vis_gain,
    vis_bias,
    vis_qkv,
    vis_out,
    merge_weight,
    positions,
    text,
    dec_gain,
    dec_bias,
    dec_qkv,
):
    groups = lax.axis_size(GRP)
    here = lax.axis_index(GRP)
    rows = patches.shape[0]
    merged_count = rows // 4
    text_count = text.shape[0]
    tok = text_count + merged_count
    cap = merged_count // min(groups, 16)

    tnorm = normalize(text.astype(jnp.float32), dec_gain, dec_bias).astype(jnp.bfloat16)
    tproj = jnp.einsum("td,sde->ste", tnorm, dec_qkv, preferred_element_type=jnp.float32).astype(
        jnp.bfloat16
    )
    digit = 128
    pad_rows = 8
    lanes = 2 * DH
    pos_rows = jnp.stack([positions // digit, positions % digit]).astype(jnp.bfloat16)
    extra = jnp.zeros((pad_rows, lanes), jnp.bfloat16).at[:2].set(pos_rows.reshape(2, lanes))
    payload = jnp.concatenate([jnp.concatenate([tproj[1], tproj[2]], axis=1), extra], axis=0)
    text_kv = lax.all_gather(payload, GRP, axis=0, tiled=True)
    digits = text_kv.reshape(groups, text_count + pad_rows, lanes)[:, text_count : text_count + 2]
    digits = digits.astype(jnp.int32)
    all_pos = (digits[:, 0] * digit + digits[:, 1]).reshape(-1)

    place = jnp.arange(tok, dtype=jnp.int32)
    flags = jnp.sum((all_pos[None, :] == (here * tok + place)[:, None]).astype(jnp.int32), axis=1)
    free = 1 - flags
    text_rank = jnp.cumsum(free) - 1
    pick = (free[:, None] == 1) & (text_rank[:, None] == jnp.arange(text_count, dtype=jnp.int32)[None, :])
    own_text_pos = jnp.sum(jnp.where(pick, place[:, None], 0), axis=0) + here * tok

    heads = vis_qkv.shape[2] // HD
    patches_f = patches.astype(jnp.float32)
    normed = normalize(patches_f, vis_gain, vis_bias).astype(jnp.bfloat16)
    proj = jnp.einsum("pd,sde->spe", normed, vis_qkv, preferred_element_type=jnp.float32).astype(
        jnp.bfloat16
    )
    query = proj[0].reshape(rows, heads, HD)
    swap = [(i, i ^ 1) for i in range(lax.axis_size("gy"))]
    partner_kv, partner_ids = lax.ppermute((proj[1:], patch_image), "gy", swap)
    both_kv = jnp.concatenate([proj[1:], partner_kv], axis=1)
    both_ids = jnp.concatenate([patch_image, partner_ids], axis=0)
    keys = both_kv[0].reshape(2 * rows, heads, HD)
    values = both_kv[1].reshape(2 * rows, heads, HD)
    scores = jnp.einsum("phe,khe->hpk", query, keys, preferred_element_type=jnp.float32) * HD ** (
        -0.5
    )
    same = patch_image[:, None] == both_ids[None, :]
    top = jnp.max(jnp.where(same, scores, -1e30), axis=2, keepdims=True)
    expo = jnp.where(same, jnp.exp(scores - top), 0.0)
    weights = (expo / jnp.sum(expo, axis=2, keepdims=True)).astype(jnp.bfloat16)
    attended = jnp.einsum(
        "hpk,khe->phe", weights, values, preferred_element_type=jnp.float32
    ).astype(jnp.bfloat16)
    attended = attended.reshape(rows, heads * HD)

    nz = lax.axis_size("z")
    ncore = lax.axis_size("core")
    width = patches.shape[1] // (nz * ncore)
    core = lax.axis_index("core")
    vo = vis_out.reshape(vis_out.shape[0], nz, ncore, width)
    keep_w = lax.dynamic_index_in_dim(vo, core, 2, keepdims=False)
    send_w = lax.dynamic_index_in_dim(vo, 1 - core, 2, keepdims=False)
    keep = jnp.einsum("pe,ezf->zfp", attended, keep_w, preferred_element_type=jnp.float32)
    send = jnp.einsum("pe,ezf->zfp", attended, send_w, preferred_element_type=jnp.float32)
    pair = [(i, i ^ 1) for i in range(ncore)]
    half = (
        keep.astype(jnp.bfloat16).astype(jnp.float32)
        + lax.ppermute(send.astype(jnp.bfloat16), "core", pair).astype(jnp.float32)
    ).astype(jnp.bfloat16)
    mixed = a2a_sum(half, "z")
    own_cols = lax.dynamic_slice_in_dim(patches, lax.axis_index(TP) * width, width, 1)
    visual = (mixed + own_cols.astype(jnp.float32).T).astype(jnp.bfloat16)
    windows = visual.reshape(width, merged_count, 4)
    partial_rows = jnp.einsum(
        "cmk,kce->me", windows, merge_weight, preferred_element_type=jnp.float32
    ).astype(jnp.bfloat16)
    ntp = nz * ncore
    merged = a2a_gather(
        a2a_sum(partial_rows.reshape(ntp, merged_count // ntp, -1), TP).astype(jnp.bfloat16), TP
    )

    mnorm = normalize(merged.astype(jnp.float32), dec_gain, dec_bias).astype(jnp.bfloat16)
    mproj = jnp.einsum("td,sde->ste", mnorm, dec_qkv, preferred_element_type=jnp.float32).astype(
        jnp.bfloat16
    )
    merged_kv = grp_gather(jnp.concatenate([mproj[1], mproj[2]], axis=1))

    block = positions // tok
    seen = jnp.sum(
        ((all_pos[None, :] >= (block * tok)[:, None]) & (all_pos[None, :] <= positions[:, None])).astype(
            jnp.int32
        ),
        axis=1,
    )
    merged_limit = block * text_count + (positions - block * tok + 1 - seen)
    text_limit = here * text_count + jnp.arange(text_count, dtype=jnp.int32) + 1
    key_row = jnp.arange(groups * (text_count + pad_rows), dtype=jnp.int32)
    key_grp = key_row // (text_count + pad_rows)
    key_in = key_row % (text_count + pad_rows)
    text_key = jnp.where(key_in < text_count, key_grp * text_count + key_in, groups * tok)
    text_keys, text_values = text_kv[:, :DH], text_kv[:, DH:]
    merged_keys, merged_values = merged_kv[:, :DH], merged_kv[:, DH:]

    def finish(part_a, part_b):
        best = jnp.maximum(part_a[0], part_b[0])
        scale_a = jnp.exp(part_a[0] - best)
        scale_b = jnp.exp(part_b[0] - best)
        total = part_a[1] * scale_a + part_b[1] * scale_b
        acc = part_a[2] * scale_a[:, None] + part_b[2] * scale_b[:, None]
        return (acc / total[:, None]).astype(jnp.bfloat16)

    merged_out = finish(
        attend_part(mproj[0], text_key[None, :] < merged_limit[:, None], text_keys, text_values),
        attend_part(mproj[0], all_pos[None, :] <= positions[:, None], merged_keys, merged_values),
    )
    text_out = finish(
        attend_part(tproj[0], text_key[None, :] < text_limit[:, None], text_keys, text_values),
        attend_part(tproj[0], all_pos[None, :] <= own_text_pos[:, None], merged_keys, merged_values),
    )

    target = positions // tok
    member = (target[:, None] == jnp.arange(groups, dtype=jnp.int32)[None, :]).astype(jnp.int32)
    rank = jnp.sum(jnp.cumsum(member, axis=0) * member, axis=1) - 1
    slot = target * cap + rank
    select = slot[None, :] == jnp.arange(groups * cap, dtype=jnp.int32)[:, None]
    packed = jnp.dot(
        select.astype(jnp.bfloat16), merged_out, preferred_element_type=jnp.float32
    ).astype(jnp.bfloat16)
    got = lax.all_to_all(packed, GRP, 0, 0, tiled=True)

    src_pos = all_pos.reshape(groups, merged_count)
    to_me = (src_pos // tok) == here
    src_rank = jnp.cumsum(to_me.astype(jnp.int32), axis=1) - 1
    slot_hit = to_me[:, :, None] & (
        src_rank[:, :, None] == jnp.arange(cap, dtype=jnp.int32)[None, None, :]
    )
    got_pos = jnp.sum(jnp.where(slot_hit, src_pos[:, :, None] + 1, 0), axis=1).reshape(-1) - 1
    local = got_pos - here * tok
    landing = (local[None, :] == place[:, None]) & (got_pos[None, :] >= 0)
    text_land = own_text_pos[None, :] - here * tok == place[:, None]
    out = jnp.dot(landing.astype(jnp.bfloat16), got, preferred_element_type=jnp.float32)
    out = out + jnp.dot(
        text_land.astype(jnp.bfloat16), text_out, preferred_element_type=jnp.float32
    )
    return out.astype(jnp.bfloat16)


def solution(mesh):
    grid = mesh.devices.reshape(4, mesh.devices.shape[0] // 4, mesh.devices.shape[1] // 2, 2)
    mesh4 = Mesh(grid, GRP + TP)
    in_specs = (
        P(GRP, None),
        P(GRP),
        P(),
        P(),
        P(None, None, TP),
        P(TP, None),
        P(None, TP, None),
        P(GRP),
        P(GRP, None),
        P(),
        P(),
        P(None, None, TP),
    )
    out_specs = P(GRP, TP)
    return jax.shard_map(body, mesh=mesh4, in_specs=in_specs, out_specs=out_specs, check_vma=False)
```

```python
import jax
import jax.numpy as jnp
from jax import lax
from jax.experimental import pallas as pl
from jax.sharding import Mesh
from jax.sharding import PartitionSpec as P

HD = 104
DH = 64

layer_eps = 1e-05

GRP = ("gx", "gy")
TP = ("z", "core")


def normalize(values, gain, bias):
    mean = jnp.mean(values, axis=-1, keepdims=True)
    centred = values - mean
    spread = jnp.mean(centred * centred, axis=-1, keepdims=True)
    return centred * lax.rsqrt(spread + layer_eps) * gain + bias


def a2a_gather(value, axis):
    n = lax.axis_size(axis)
    spread = jnp.broadcast_to(value[None], (n,) + value.shape)
    got = lax.all_to_all(spread, axis, 0, 0, tiled=True)
    return got.reshape((n * value.shape[0],) + value.shape[1:])


def grp_gather(value):
    return a2a_gather(a2a_gather(value, "gy"), "gx")


def a2a_sum(parts, axis):
    got = lax.all_to_all(parts, axis, 0, 0, tiled=True)
    return jnp.sum(got.astype(jnp.float32), axis=0)


BLOCK = 256


def text_attend_kernel(q_ref, kv_ref, rank_ref, lim_ref, top_ref, tot_ref, acc_ref):
    q = q_ref[...]
    lim = lim_ref[...]
    rows = q.shape[0]

    def step(i, carry):
        best, total, acc = carry
        start = pl.multiple_of(i * BLOCK, BLOCK)
        kv = kv_ref[pl.ds(start, BLOCK), :]
        keys = kv[:, :DH]
        values = kv[:, DH:]
        score = lax.dot_general(
            q, keys, (((1,), (1,)), ((), ())), preferred_element_type=jnp.float32
        ) * DH ** (-0.5)
        allowed = rank_ref[:, pl.ds(start, BLOCK)] < lim
        new_best = jnp.maximum(best, jnp.max(jnp.where(allowed, score, -1e30), axis=1, keepdims=True))
        expo = jnp.where(allowed, jnp.exp(score - new_best), 0.0)
        scale = jnp.exp(best - new_best)
        total = total * scale + jnp.sum(expo, axis=1, keepdims=True)
        acc = acc * scale + jnp.dot(expo.astype(jnp.bfloat16), values, preferred_element_type=jnp.float32)
        return new_best, total, acc

    init = (
        jnp.full((rows, 1), -1e30, jnp.float32),
        jnp.zeros((rows, 1), jnp.float32),
        jnp.zeros((rows, DH), jnp.float32),
    )
    best, total, acc = lax.fori_loop(0, kv_ref.shape[0] // BLOCK, step, init)
    top_ref[...] = best
    tot_ref[...] = total
    acc_ref[...] = acc


def text_attend(query, kv, rank, limit):
    rows = query.shape[0]
    keys = kv.shape[0]
    cost = pl.CostEstimate(
        flops=4 * rows * keys * DH, transcendentals=rows * keys, bytes_accessed=kv.size * 2 + rows * DH * 6
    )
    top, total, acc = pl.pallas_call(
        text_attend_kernel,
        out_shape=(
            jax.ShapeDtypeStruct((rows, 1), jnp.float32),
            jax.ShapeDtypeStruct((rows, 1), jnp.float32),
            jax.ShapeDtypeStruct((rows, DH), jnp.float32),
        ),
        cost_estimate=cost,
    )(query, kv, rank.reshape(1, -1), limit.reshape(-1, 1))
    return top[:, 0], total[:, 0], acc


def attend_part(query, allowed, keys, values):
    score = jnp.dot(query, keys.T, preferred_element_type=jnp.float32) * DH ** (-0.5)
    top = jnp.max(jnp.where(allowed, score, -1e30), axis=1)
    expo = jnp.where(allowed, jnp.exp(score - top[:, None]), 0.0)
    total = jnp.sum(expo, axis=1)
    acc = jnp.dot(expo.astype(jnp.bfloat16), values, preferred_element_type=jnp.float32)
    return top, total, acc


def body(
    patches,
    patch_image,
    vis_gain,
    vis_bias,
    vis_qkv,
    vis_out,
    merge_weight,
    positions,
    text,
    dec_gain,
    dec_bias,
    dec_qkv,
):
    groups = lax.axis_size(GRP)
    here = lax.axis_index(GRP)
    rows = patches.shape[0]
    merged_count = rows // 4
    text_count = text.shape[0]
    tok = text_count + merged_count
    cap = merged_count // min(groups, 16)

    tnorm = normalize(text.astype(jnp.float32), dec_gain, dec_bias).astype(jnp.bfloat16)
    tproj = jnp.einsum("td,sde->ste", tnorm, dec_qkv, preferred_element_type=jnp.float32).astype(
        jnp.bfloat16
    )
    digit = 128
    pad_rows = 8
    lanes = 2 * DH
    pos_rows = jnp.stack([positions // digit, positions % digit]).astype(jnp.bfloat16)
    extra = jnp.zeros((pad_rows, lanes), jnp.bfloat16).at[:2].set(pos_rows.reshape(2, lanes))
    payload = jnp.concatenate([jnp.concatenate([tproj[1], tproj[2]], axis=1), extra], axis=0)
    text_kv = lax.all_gather(payload, GRP, axis=0, tiled=True)
    digits = text_kv.reshape(groups, text_count + pad_rows, lanes)[:, text_count : text_count + 2]
    digits = digits.astype(jnp.int32)
    all_pos = (digits[:, 0] * digit + digits[:, 1]).reshape(-1)

    place = jnp.arange(tok, dtype=jnp.int32)
    flags = jnp.sum((all_pos[None, :] == (here * tok + place)[:, None]).astype(jnp.int32), axis=1)
    free = 1 - flags
    text_rank = jnp.cumsum(free) - 1
    pick = (free[:, None] == 1) & (text_rank[:, None] == jnp.arange(text_count, dtype=jnp.int32)[None, :])
    own_text_pos = jnp.sum(jnp.where(pick, place[:, None], 0), axis=0) + here * tok

    heads = vis_qkv.shape[2] // HD
    patches_f = patches.astype(jnp.float32)
    normed = normalize(patches_f, vis_gain, vis_bias).astype(jnp.bfloat16)
    proj = jnp.einsum("pd,sde->spe", normed, vis_qkv, preferred_element_type=jnp.float32).astype(
        jnp.bfloat16
    )
    query = proj[0].reshape(rows, heads, HD)
    swap = [(i, i ^ 1) for i in range(lax.axis_size("gy"))]
    partner_kv, partner_ids = lax.ppermute((proj[1:], patch_image), "gy", swap)
    both_kv = jnp.concatenate([proj[1:], partner_kv], axis=1)
    both_ids = jnp.concatenate([patch_image, partner_ids], axis=0)
    keys = both_kv[0].reshape(2 * rows, heads, HD)
    values = both_kv[1].reshape(2 * rows, heads, HD)
    scores = jnp.einsum("phe,khe->hpk", query, keys, preferred_element_type=jnp.float32) * HD ** (
        -0.5
    )
    same = patch_image[:, None] == both_ids[None, :]
    top = jnp.max(jnp.where(same, scores, -1e30), axis=2, keepdims=True)
    expo = jnp.where(same, jnp.exp(scores - top), 0.0)
    weights = (expo / jnp.sum(expo, axis=2, keepdims=True)).astype(jnp.bfloat16)
    attended = jnp.einsum(
        "hpk,khe->phe", weights, values, preferred_element_type=jnp.float32
    ).astype(jnp.bfloat16)
    attended = attended.reshape(rows, heads * HD)

    nz = lax.axis_size("z")
    ncore = lax.axis_size("core")
    width = patches.shape[1] // (nz * ncore)
    core = lax.axis_index("core")
    vo = vis_out.reshape(vis_out.shape[0], nz, ncore, width)
    keep_w = lax.dynamic_index_in_dim(vo, core, 2, keepdims=False)
    send_w = lax.dynamic_index_in_dim(vo, 1 - core, 2, keepdims=False)
    keep = jnp.einsum("pe,ezf->zfp", attended, keep_w, preferred_element_type=jnp.float32)
    send = jnp.einsum("pe,ezf->zfp", attended, send_w, preferred_element_type=jnp.float32)
    pair = [(i, i ^ 1) for i in range(ncore)]
    half = (
        keep.astype(jnp.bfloat16).astype(jnp.float32)
        + lax.ppermute(send.astype(jnp.bfloat16), "core", pair).astype(jnp.float32)
    ).astype(jnp.bfloat16)
    mixed = a2a_sum(half, "z")
    own_cols = lax.dynamic_slice_in_dim(patches, lax.axis_index(TP) * width, width, 1)
    visual = (mixed + own_cols.astype(jnp.float32).T).astype(jnp.bfloat16)
    windows = visual.reshape(width, merged_count, 4)
    partial_rows = jnp.einsum(
        "cmk,kce->me", windows, merge_weight, preferred_element_type=jnp.float32
    ).astype(jnp.bfloat16)
    ntp = nz * ncore
    merged = a2a_gather(
        a2a_sum(partial_rows.reshape(ntp, merged_count // ntp, -1), TP).astype(jnp.bfloat16), TP
    )

    mnorm = normalize(merged.astype(jnp.float32), dec_gain, dec_bias).astype(jnp.bfloat16)
    mproj = jnp.einsum("td,sde->ste", mnorm, dec_qkv, preferred_element_type=jnp.float32).astype(
        jnp.bfloat16
    )
    merged_kv = grp_gather(jnp.concatenate([mproj[1], mproj[2]], axis=1))

    query_pos = jnp.concatenate([own_text_pos, positions], axis=0)
    block = positions // tok
    seen = jnp.sum(
        ((all_pos[None, :] >= (block * tok)[:, None]) & (all_pos[None, :] <= positions[:, None])).astype(
            jnp.int32
        ),
        axis=1,
    )
    merged_limit = block * text_count + (positions - block * tok + 1 - seen)
    text_limit = here * text_count + jnp.arange(text_count, dtype=jnp.int32) + 1
    key_row = jnp.arange(groups * (text_count + pad_rows), dtype=jnp.int32)
    key_grp = key_row // (text_count + pad_rows)
    key_in = key_row % (text_count + pad_rows)
    text_key = jnp.where(key_in < text_count, key_grp * text_count + key_in, groups * tok)
    part_tt = text_attend(tproj[0], text_kv, text_key, text_limit)
    part_mt = text_attend(mproj[0], text_kv, text_key, merged_limit)
    part_t = [jnp.concatenate([a, b], axis=0) for a, b in zip(part_tt, part_mt)]
    top_t, total_t, acc_t = part_t
    dquery = jnp.concatenate([tproj[0], mproj[0]], axis=0)
    top_m, total_m, acc_m = attend_part(
        dquery, all_pos[None, :] <= query_pos[:, None], merged_kv[:, :DH], merged_kv[:, DH:]
    )
    best = jnp.maximum(top_t, top_m)
    scale_t = jnp.exp(top_t - best)
    scale_m = jnp.exp(top_m - best)
    total = total_t * scale_t + total_m * scale_m
    acc = acc_t * scale_t[:, None] + acc_m * scale_m[:, None]
    result = (acc / total[:, None]).astype(jnp.bfloat16)
    text_out = result[:text_count]
    merged_out = result[text_count:]

    target = positions // tok
    member = (target[:, None] == jnp.arange(groups, dtype=jnp.int32)[None, :]).astype(jnp.int32)
    rank = jnp.sum(jnp.cumsum(member, axis=0) * member, axis=1) - 1
    slot = target * cap + rank
    select = slot[None, :] == jnp.arange(groups * cap, dtype=jnp.int32)[:, None]
    packed = jnp.dot(
        select.astype(jnp.bfloat16), merged_out, preferred_element_type=jnp.float32
    ).astype(jnp.bfloat16)
    got = lax.all_to_all(packed, GRP, 0, 0, tiled=True)

    src_pos = all_pos.reshape(groups, merged_count)
    to_me = (src_pos // tok) == here
    src_rank = jnp.cumsum(to_me.astype(jnp.int32), axis=1) - 1
    slot_hit = to_me[:, :, None] & (
        src_rank[:, :, None] == jnp.arange(cap, dtype=jnp.int32)[None, None, :]
    )
    got_pos = jnp.sum(jnp.where(slot_hit, src_pos[:, :, None] + 1, 0), axis=1).reshape(-1) - 1
    local = got_pos - here * tok
    landing = (local[None, :] == place[:, None]) & (got_pos[None, :] >= 0)
    text_land = own_text_pos[None, :] - here * tok == place[:, None]
    out = jnp.dot(landing.astype(jnp.bfloat16), got, preferred_element_type=jnp.float32)
    out = out + jnp.dot(
        text_land.astype(jnp.bfloat16), text_out, preferred_element_type=jnp.float32
    )
    return out.astype(jnp.bfloat16)


def solution(mesh):
    grid = mesh.devices.reshape(4, mesh.devices.shape[0] // 4, mesh.devices.shape[1] // 2, 2)
    mesh4 = Mesh(grid, GRP + TP)
    in_specs = (
        P(GRP, None),
        P(GRP),
        P(),
        P(),
        P(None, None, TP),
        P(TP, None),
        P(None, TP, None),
        P(GRP),
        P(GRP, None),
        P(),
        P(),
        P(None, None, TP),
    )
    out_specs = P(GRP, TP)
    return jax.shard_map(body, mesh=mesh4, in_specs=in_specs, out_specs=out_specs, check_vma=False)
```

```python
import jax
import jax.numpy as jnp
from jax import lax
from jax.experimental import pallas as pl
from jax.sharding import Mesh
from jax.sharding import PartitionSpec as P

HD = 104
DH = 64

layer_eps = 1e-05

GRP = ("gx", "gy")
TP = ("z", "core")


def normalize(values, gain, bias):
    mean = jnp.mean(values, axis=-1, keepdims=True)
    centred = values - mean
    spread = jnp.mean(centred * centred, axis=-1, keepdims=True)
    return centred * lax.rsqrt(spread + layer_eps) * gain + bias


def a2a_gather(value, axis):
    n = lax.axis_size(axis)
    spread = jnp.broadcast_to(value[None], (n,) + value.shape)
    got = lax.all_to_all(spread, axis, 0, 0, tiled=True)
    return got.reshape((n * value.shape[0],) + value.shape[1:])


def grp_gather(value):
    return a2a_gather(a2a_gather(value, "gy"), "gx")


def a2a_sum(parts, axis):
    got = lax.all_to_all(parts, axis, 0, 0, tiled=True)
    return jnp.sum(got.astype(jnp.float32), axis=0)


BLOCK = 1408


def text_attend_kernel(q_ref, kt_ref, v_ref, rank_ref, lim_ref, top_ref, tot_ref, acc_ref):
    q = q_ref[...]
    lim = lim_ref[...]
    rows = q.shape[0]

    def step(i, carry):
        best, total, acc = carry
        start = pl.multiple_of(i * BLOCK, 128)
        score = jnp.dot(q, kt_ref[:, pl.ds(start, BLOCK)], preferred_element_type=jnp.float32) * (
            DH ** (-0.5)
        )
        allowed = rank_ref[:, pl.ds(start, BLOCK)] < lim
        new_best = jnp.maximum(best, jnp.max(jnp.where(allowed, score, -1e30), axis=1, keepdims=True))
        expo = jnp.where(allowed, jnp.exp(score - new_best), 0.0)
        scale = jnp.exp(best - new_best)
        total = total * scale + jnp.sum(expo, axis=1, keepdims=True)
        acc = acc * scale + jnp.dot(
            expo.astype(jnp.bfloat16), v_ref[pl.ds(start, BLOCK), :], preferred_element_type=jnp.float32
        )
        return new_best, total, acc

    init = (
        jnp.full((rows, 1), -1e30, jnp.float32),
        jnp.zeros((rows, 1), jnp.float32),
        jnp.zeros((rows, DH), jnp.float32),
    )
    best, total, acc = lax.fori_loop(0, kt_ref.shape[1] // BLOCK, step, init, unroll=True)
    top_ref[...] = best
    tot_ref[...] = total
    acc_ref[...] = acc


def text_attend(query, keys_t, values, rank, limit):
    rows = query.shape[0]
    keys = keys_t.shape[1]
    cost = pl.CostEstimate(
        flops=4 * rows * keys * DH, transcendentals=rows * keys, bytes_accessed=keys * DH * 4 + rows * DH * 6
    )
    top, total, acc = pl.pallas_call(
        text_attend_kernel,
        out_shape=(
            jax.ShapeDtypeStruct((rows, 1), jnp.float32),
            jax.ShapeDtypeStruct((rows, 1), jnp.float32),
            jax.ShapeDtypeStruct((rows, DH), jnp.float32),
        ),
        cost_estimate=cost,
    )(query, keys_t, values, rank.reshape(1, -1), limit.reshape(-1, 1))
    return top[:, 0], total[:, 0], acc


def attend_part(query, allowed, keys, values):
    score = jnp.dot(query, keys.T, preferred_element_type=jnp.float32) * DH ** (-0.5)
    top = jnp.max(jnp.where(allowed, score, -1e30), axis=1)
    expo = jnp.where(allowed, jnp.exp(score - top[:, None]), 0.0)
    total = jnp.sum(expo, axis=1)
    acc = jnp.dot(expo.astype(jnp.bfloat16), values, preferred_element_type=jnp.float32)
    return top, total, acc


def body(
    patches,
    patch_image,
    vis_gain,
    vis_bias,
    vis_qkv,
    vis_out,
    merge_weight,
    positions,
    text,
    dec_gain,
    dec_bias,
    dec_qkv,
):
    groups = lax.axis_size(GRP)
    here = lax.axis_index(GRP)
    rows = patches.shape[0]
    merged_count = rows // 4
    text_count = text.shape[0]
    tok = text_count + merged_count
    cap = merged_count // min(groups, 16)

    tnorm = normalize(text.astype(jnp.float32), dec_gain, dec_bias).astype(jnp.bfloat16)
    tproj = jnp.einsum("td,sde->ste", tnorm, dec_qkv, preferred_element_type=jnp.float32).astype(
        jnp.bfloat16
    )
    digit = 128
    pad_rows = 8
    lanes = 2 * DH
    pos_rows = jnp.stack([positions // digit, positions % digit]).astype(jnp.bfloat16)
    extra = jnp.zeros((pad_rows, lanes), jnp.bfloat16).at[:2].set(pos_rows.reshape(2, lanes))
    payload = jnp.concatenate([jnp.concatenate([tproj[1], tproj[2]], axis=1), extra], axis=0)
    text_kv = lax.all_gather(payload, GRP, axis=0, tiled=True)
    digits = text_kv.reshape(groups, text_count + pad_rows, lanes)[:, text_count : text_count + 2]
    digits = digits.astype(jnp.int32)
    all_pos = (digits[:, 0] * digit + digits[:, 1]).reshape(-1)

    place = jnp.arange(tok, dtype=jnp.int32)
    flags = jnp.sum((all_pos[None, :] == (here * tok + place)[:, None]).astype(jnp.int32), axis=1)
    free = 1 - flags
    text_rank = jnp.cumsum(free) - 1
    pick = (free[:, None] == 1) & (text_rank[:, None] == jnp.arange(text_count, dtype=jnp.int32)[None, :])
    own_text_pos = jnp.sum(jnp.where(pick, place[:, None], 0), axis=0) + here * tok

    heads = vis_qkv.shape[2] // HD
    patches_f = patches.astype(jnp.float32)
    normed = normalize(patches_f, vis_gain, vis_bias).astype(jnp.bfloat16)
    proj = jnp.einsum("pd,sde->spe", normed, vis_qkv, preferred_element_type=jnp.float32).astype(
        jnp.bfloat16
    )
    query = proj[0].reshape(rows, heads, HD)
    swap = [(i, i ^ 1) for i in range(lax.axis_size("gy"))]
    partner_kv, partner_ids = lax.ppermute((proj[1:], patch_image), "gy", swap)
    both_kv = jnp.concatenate([proj[1:], partner_kv], axis=1)
    both_ids = jnp.concatenate([patch_image, partner_ids], axis=0)
    keys = both_kv[0].reshape(2 * rows, heads, HD)
    values = both_kv[1].reshape(2 * rows, heads, HD)
    scores = jnp.einsum("phe,khe->hpk", query, keys, preferred_element_type=jnp.float32) * HD ** (
        -0.5
    )
    same = patch_image[:, None] == both_ids[None, :]
    top = jnp.max(jnp.where(same, scores, -1e30), axis=2, keepdims=True)
    expo = jnp.where(same, jnp.exp(scores - top), 0.0)
    weights = (expo / jnp.sum(expo, axis=2, keepdims=True)).astype(jnp.bfloat16)
    attended = jnp.einsum(
        "hpk,khe->phe", weights, values, preferred_element_type=jnp.float32
    ).astype(jnp.bfloat16)
    attended = attended.reshape(rows, heads * HD)

    nz = lax.axis_size("z")
    ncore = lax.axis_size("core")
    width = patches.shape[1] // (nz * ncore)
    core = lax.axis_index("core")
    vo = vis_out.reshape(vis_out.shape[0], nz, ncore, width)
    keep_w = lax.dynamic_index_in_dim(vo, core, 2, keepdims=False)
    send_w = lax.dynamic_index_in_dim(vo, 1 - core, 2, keepdims=False)
    keep = jnp.einsum("pe,ezf->zfp", attended, keep_w, preferred_element_type=jnp.float32)
    send = jnp.einsum("pe,ezf->zfp", attended, send_w, preferred_element_type=jnp.float32)
    pair = [(i, i ^ 1) for i in range(ncore)]
    half = (
        keep.astype(jnp.bfloat16).astype(jnp.float32)
        + lax.ppermute(send.astype(jnp.bfloat16), "core", pair).astype(jnp.float32)
    ).astype(jnp.bfloat16)
    mixed = a2a_sum(half, "z")
    own_cols = lax.dynamic_slice_in_dim(patches, lax.axis_index(TP) * width, width, 1)
    visual = (mixed + own_cols.astype(jnp.float32).T).astype(jnp.bfloat16)
    windows = visual.reshape(width, merged_count, 4)
    partial_rows = jnp.einsum(
        "cmk,kce->me", windows, merge_weight, preferred_element_type=jnp.float32
    ).astype(jnp.bfloat16)
    ntp = nz * ncore
    merged = a2a_gather(
        a2a_sum(partial_rows.reshape(ntp, merged_count // ntp, -1), TP).astype(jnp.bfloat16), TP
    )

    mnorm = normalize(merged.astype(jnp.float32), dec_gain, dec_bias).astype(jnp.bfloat16)
    mproj = jnp.einsum("td,sde->ste", mnorm, dec_qkv, preferred_element_type=jnp.float32).astype(
        jnp.bfloat16
    )
    merged_kv = grp_gather(jnp.concatenate([mproj[1], mproj[2]], axis=1))

    query_pos = jnp.concatenate([own_text_pos, positions], axis=0)
    block = positions // tok
    seen = jnp.sum(
        ((all_pos[None, :] >= (block * tok)[:, None]) & (all_pos[None, :] <= positions[:, None])).astype(
            jnp.int32
        ),
        axis=1,
    )
    merged_limit = block * text_count + (positions - block * tok + 1 - seen)
    text_limit = here * text_count + jnp.arange(text_count, dtype=jnp.int32) + 1
    key_row = jnp.arange(groups * (text_count + pad_rows), dtype=jnp.int32)
    key_grp = key_row // (text_count + pad_rows)
    key_in = key_row % (text_count + pad_rows)
    text_key = jnp.where(key_in < text_count, key_grp * text_count + key_in, groups * tok)
    text_keys_t, text_values = text_kv[:, :DH].T, text_kv[:, DH:]
    part_tt = text_attend(tproj[0], text_keys_t, text_values, text_key, text_limit)
    part_mt = text_attend(mproj[0], text_keys_t, text_values, text_key, merged_limit)
    part_t = [jnp.concatenate([a, b], axis=0) for a, b in zip(part_tt, part_mt)]
    top_t, total_t, acc_t = part_t
    dquery = jnp.concatenate([tproj[0], mproj[0]], axis=0)
    top_m, total_m, acc_m = attend_part(
        dquery, all_pos[None, :] <= query_pos[:, None], merged_kv[:, :DH], merged_kv[:, DH:]
    )
    best = jnp.maximum(top_t, top_m)
    scale_t = jnp.exp(top_t - best)
    scale_m = jnp.exp(top_m - best)
    total = total_t * scale_t + total_m * scale_m
    acc = acc_t * scale_t[:, None] + acc_m * scale_m[:, None]
    result = (acc / total[:, None]).astype(jnp.bfloat16)
    text_out = result[:text_count]
    merged_out = result[text_count:]

    target = positions // tok
    member = (target[:, None] == jnp.arange(groups, dtype=jnp.int32)[None, :]).astype(jnp.int32)
    rank = jnp.sum(jnp.cumsum(member, axis=0) * member, axis=1) - 1
    slot = target * cap + rank
    select = slot[None, :] == jnp.arange(groups * cap, dtype=jnp.int32)[:, None]
    packed = jnp.dot(
        select.astype(jnp.bfloat16), merged_out, preferred_element_type=jnp.float32
    ).astype(jnp.bfloat16)
    got = lax.all_to_all(packed, GRP, 0, 0, tiled=True)

    src_pos = all_pos.reshape(groups, merged_count)
    to_me = (src_pos // tok) == here
    src_rank = jnp.cumsum(to_me.astype(jnp.int32), axis=1) - 1
    slot_hit = to_me[:, :, None] & (
        src_rank[:, :, None] == jnp.arange(cap, dtype=jnp.int32)[None, None, :]
    )
    got_pos = jnp.sum(jnp.where(slot_hit, src_pos[:, :, None] + 1, 0), axis=1).reshape(-1) - 1
    local = got_pos - here * tok
    landing = (local[None, :] == place[:, None]) & (got_pos[None, :] >= 0)
    text_land = own_text_pos[None, :] - here * tok == place[:, None]
    out = jnp.dot(landing.astype(jnp.bfloat16), got, preferred_element_type=jnp.float32)
    out = out + jnp.dot(
        text_land.astype(jnp.bfloat16), text_out, preferred_element_type=jnp.float32
    )
    return out.astype(jnp.bfloat16)


def solution(mesh):
    grid = mesh.devices.reshape(4, mesh.devices.shape[0] // 4, mesh.devices.shape[1] // 2, 2)
    mesh4 = Mesh(grid, GRP + TP)
    in_specs = (
        P(GRP, None),
        P(GRP),
        P(),
        P(),
        P(None, None, TP),
        P(TP, None),
        P(None, TP, None),
        P(GRP),
        P(GRP, None),
        P(),
        P(),
        P(None, None, TP),
    )
    out_specs = P(GRP, TP)
    return jax.shard_map(body, mesh=mesh4, in_specs=in_specs, out_specs=out_specs, check_vma=False)
```

```python
import jax
import jax.numpy as jnp
from jax import lax
from jax.sharding import Mesh
from jax.sharding import PartitionSpec as P

HD = 104
DH = 64

layer_eps = 1e-05

GRP = ("gx", "gy")
TP = ("z", "core")


def normalize(values, gain, bias):
    mean = jnp.mean(values, axis=-1, keepdims=True)
    centred = values - mean
    spread = jnp.mean(centred * centred, axis=-1, keepdims=True)
    return centred * lax.rsqrt(spread + layer_eps) * gain + bias


def a2a_gather(value, axis):
    n = lax.axis_size(axis)
    spread = jnp.broadcast_to(value[None], (n,) + value.shape)
    got = lax.all_to_all(spread, axis, 0, 0, tiled=True)
    return got.reshape((n * value.shape[0],) + value.shape[1:])


def grp_gather(value):
    return a2a_gather(a2a_gather(value, "gy"), "gx")


def a2a_sum(parts, axis):
    got = lax.all_to_all(parts, axis, 0, 0, tiled=True)
    return jnp.sum(got.astype(jnp.float32), axis=0)


def attend_part(query, allowed, keys, values):
    score = jnp.dot(query, keys.T, preferred_element_type=jnp.float32) * DH ** (-0.5)
    top = jnp.max(jnp.where(allowed, score, -1e30), axis=1)
    expo = jnp.where(allowed, jnp.exp(score - top[:, None]), 0.0)
    total = jnp.sum(expo, axis=1)
    acc = jnp.dot(expo.astype(jnp.bfloat16), values, preferred_element_type=jnp.float32)
    return top, total, acc


def body(
    patches,
    patch_image,
    vis_gain,
    vis_bias,
    vis_qkv,
    vis_out,
    merge_weight,
    positions,
    text,
    dec_gain,
    dec_bias,
    dec_qkv,
):
    groups = lax.axis_size(GRP)
    here = lax.axis_index(GRP)
    rows = patches.shape[0]
    merged_count = rows // 4
    text_count = text.shape[0]
    tok = text_count + merged_count
    cap = merged_count // min(groups, 16)

    tnorm = normalize(text.astype(jnp.float32), dec_gain, dec_bias).astype(jnp.bfloat16)
    tproj = jnp.einsum("td,sde->ste", tnorm, dec_qkv, preferred_element_type=jnp.float32).astype(
        jnp.bfloat16
    )
    digit = 128
    pad_rows = 8
    lanes = 2 * DH
    pos_rows = jnp.stack([positions // digit, positions % digit]).astype(jnp.bfloat16)
    extra = jnp.zeros((pad_rows, lanes), jnp.bfloat16).at[:2].set(pos_rows.reshape(2, lanes))
    payload = jnp.concatenate([jnp.concatenate([tproj[1], tproj[2]], axis=1), extra], axis=0)
    text_kv = lax.all_gather(payload, GRP, axis=0, tiled=True)
    digits = text_kv.reshape(groups, text_count + pad_rows, lanes)[:, text_count : text_count + 2]
    digits = digits.astype(jnp.int32)
    all_pos = (digits[:, 0] * digit + digits[:, 1]).reshape(-1)

    place = jnp.arange(tok, dtype=jnp.int32)
    flags = jnp.sum((all_pos[None, :] == (here * tok + place)[:, None]).astype(jnp.int32), axis=1)
    free = 1 - flags
    text_rank = jnp.cumsum(free) - 1
    pick = (free[:, None] == 1) & (text_rank[:, None] == jnp.arange(text_count, dtype=jnp.int32)[None, :])
    own_text_pos = jnp.sum(jnp.where(pick, place[:, None], 0), axis=0) + here * tok

    heads = vis_qkv.shape[2] // HD
    patches_f = patches.astype(jnp.float32)
    normed = normalize(patches_f, vis_gain, vis_bias).astype(jnp.bfloat16)
    proj = jnp.einsum("pd,sde->spe", normed, vis_qkv, preferred_element_type=jnp.float32).astype(
        jnp.bfloat16
    )
    query = proj[0].reshape(rows, heads, HD)
    swap = [(i, i ^ 1) for i in range(lax.axis_size("gy"))]
    id_digit = 64
    id_plane = jnp.zeros((1, rows, HD), jnp.bfloat16)
    id_plane = id_plane.at[0, :, 0].set((patch_image // id_digit).astype(jnp.bfloat16))
    id_plane = id_plane.at[0, :, 1].set((patch_image % id_digit).astype(jnp.bfloat16))
    partner_all = lax.ppermute(jnp.concatenate([proj[1:], id_plane], axis=0), "gy", swap)
    partner_kv = partner_all[:2]
    partner_digits = partner_all[2, :, :2].astype(jnp.int32)
    partner_ids = partner_digits[:, 0] * id_digit + partner_digits[:, 1]
    both_kv = jnp.concatenate([proj[1:], partner_kv], axis=1)
    both_ids = jnp.concatenate([patch_image, partner_ids], axis=0)
    keys = both_kv[0].reshape(2 * rows, heads, HD)
    values = both_kv[1].reshape(2 * rows, heads, HD)
    scores = jnp.einsum("phe,khe->hpk", query, keys, preferred_element_type=jnp.float32) * HD ** (
        -0.5
    )
    same = patch_image[:, None] == both_ids[None, :]
    top = jnp.max(jnp.where(same, scores, -1e30), axis=2, keepdims=True)
    expo = jnp.where(same, jnp.exp(scores - top), 0.0)
    weights = (expo / jnp.sum(expo, axis=2, keepdims=True)).astype(jnp.bfloat16)
    attended = jnp.einsum(
        "hpk,khe->phe", weights, values, preferred_element_type=jnp.float32
    ).astype(jnp.bfloat16)
    attended = attended.reshape(rows, heads * HD)

    nz = lax.axis_size("z")
    ncore = lax.axis_size("core")
    width = patches.shape[1] // (nz * ncore)
    core = lax.axis_index("core")
    vo = vis_out.reshape(vis_out.shape[0], nz, ncore, width)
    keep_w = lax.dynamic_index_in_dim(vo, core, 2, keepdims=False)
    send_w = lax.dynamic_index_in_dim(vo, 1 - core, 2, keepdims=False)
    keep = jnp.einsum("pe,ezf->zfp", attended, keep_w, preferred_element_type=jnp.float32)
    send = jnp.einsum("pe,ezf->zfp", attended, send_w, preferred_element_type=jnp.float32)
    pair = [(i, i ^ 1) for i in range(ncore)]
    half = (
        keep.astype(jnp.bfloat16).astype(jnp.float32)
        + lax.ppermute(send.astype(jnp.bfloat16), "core", pair).astype(jnp.float32)
    ).astype(jnp.bfloat16)
    mixed = a2a_sum(half, "z")
    own_cols = lax.dynamic_slice_in_dim(patches, lax.axis_index(TP) * width, width, 1)
    visual = (mixed + own_cols.astype(jnp.float32).T).astype(jnp.bfloat16)
    windows = visual.reshape(width, merged_count, 4)
    partial_rows = jnp.einsum(
        "cmk,kce->me", windows, merge_weight, preferred_element_type=jnp.float32
    ).astype(jnp.bfloat16)
    ntp = nz * ncore
    merged = a2a_gather(
        a2a_sum(partial_rows.reshape(ntp, merged_count // ntp, -1), TP).astype(jnp.bfloat16), TP
    )

    mnorm = normalize(merged.astype(jnp.float32), dec_gain, dec_bias).astype(jnp.bfloat16)
    mproj = jnp.einsum("td,sde->ste", mnorm, dec_qkv, preferred_element_type=jnp.float32).astype(
        jnp.bfloat16
    )
    merged_kv = grp_gather(jnp.concatenate([mproj[1], mproj[2]], axis=1))

    query_pos = jnp.concatenate([own_text_pos, positions], axis=0)
    block = positions // tok
    seen = jnp.sum(
        ((all_pos[None, :] >= (block * tok)[:, None]) & (all_pos[None, :] <= positions[:, None])).astype(
            jnp.int32
        ),
        axis=1,
    )
    merged_limit = block * text_count + (positions - block * tok + 1 - seen)
    text_limit = here * text_count + jnp.arange(text_count, dtype=jnp.int32) + 1
    key_row = jnp.arange(groups * (text_count + pad_rows), dtype=jnp.int32)
    key_grp = key_row // (text_count + pad_rows)
    key_in = key_row % (text_count + pad_rows)
    text_key = jnp.where(key_in < text_count, key_grp * text_count + key_in, groups * tok)
    text_keys, text_values = text_kv[:, :DH], text_kv[:, DH:]
    part_tt = attend_part(tproj[0], text_key[None, :] < text_limit[:, None], text_keys, text_values)
    part_mt = attend_part(mproj[0], text_key[None, :] < merged_limit[:, None], text_keys, text_values)
    part_t = [jnp.concatenate([a, b], axis=0) for a, b in zip(part_tt, part_mt)]
    top_t, total_t, acc_t = part_t
    dquery = jnp.concatenate([tproj[0], mproj[0]], axis=0)
    top_m, total_m, acc_m = attend_part(
        dquery, all_pos[None, :] <= query_pos[:, None], merged_kv[:, :DH], merged_kv[:, DH:]
    )
    best = jnp.maximum(top_t, top_m)
    scale_t = jnp.exp(top_t - best)
    scale_m = jnp.exp(top_m - best)
    total = total_t * scale_t + total_m * scale_m
    acc = acc_t * scale_t[:, None] + acc_m * scale_m[:, None]
    result = (acc / total[:, None]).astype(jnp.bfloat16)
    text_out = result[:text_count]
    merged_out = result[text_count:]

    target = positions // tok
    member = (target[:, None] == jnp.arange(groups, dtype=jnp.int32)[None, :]).astype(jnp.int32)
    rank = jnp.sum(jnp.cumsum(member, axis=0) * member, axis=1) - 1
    slot = target * cap + rank
    select = slot[None, :] == jnp.arange(groups * cap, dtype=jnp.int32)[:, None]
    packed = jnp.dot(
        select.astype(jnp.bfloat16), merged_out, preferred_element_type=jnp.float32
    ).astype(jnp.bfloat16)
    got = lax.all_to_all(packed, GRP, 0, 0, tiled=True)

    src_pos = all_pos.reshape(groups, merged_count)
    to_me = (src_pos // tok) == here
    src_rank = jnp.cumsum(to_me.astype(jnp.int32), axis=1) - 1
    slot_hit = to_me[:, :, None] & (
        src_rank[:, :, None] == jnp.arange(cap, dtype=jnp.int32)[None, None, :]
    )
    got_pos = jnp.sum(jnp.where(slot_hit, src_pos[:, :, None] + 1, 0), axis=1).reshape(-1) - 1
    local = got_pos - here * tok
    landing = (local[None, :] == place[:, None]) & (got_pos[None, :] >= 0)
    text_land = own_text_pos[None, :] - here * tok == place[:, None]
    out = jnp.dot(landing.astype(jnp.bfloat16), got, preferred_element_type=jnp.float32)
    out = out + jnp.dot(
        text_land.astype(jnp.bfloat16), text_out, preferred_element_type=jnp.float32
    )
    return out.astype(jnp.bfloat16)


def solution(mesh):
    grid = mesh.devices.reshape(4, mesh.devices.shape[0] // 4, mesh.devices.shape[1] // 2, 2)
    mesh4 = Mesh(grid, GRP + TP)
    in_specs = (
        P(GRP, None),
        P(GRP),
        P(),
        P(),
        P(None, None, TP),
        P(TP, None),
        P(None, TP, None),
        P(GRP),
        P(GRP, None),
        P(),
        P(),
        P(None, None, TP),
    )
    out_specs = P(GRP, TP)
    return jax.shard_map(body, mesh=mesh4, in_specs=in_specs, out_specs=out_specs, check_vma=False)
```

```python
import jax
import jax.numpy as jnp
from jax import lax
from jax.sharding import Mesh
from jax.sharding import PartitionSpec as P

HD = 104
DH = 64

layer_eps = 1e-05

GRP = ("gx", "gy")
TP = ("z", "core")


def normalize(values, gain, bias):
    mean = jnp.mean(values, axis=-1, keepdims=True)
    centred = values - mean
    spread = jnp.mean(centred * centred, axis=-1, keepdims=True)
    return centred * lax.rsqrt(spread + layer_eps) * gain + bias


def a2a_gather(value, axis):
    n = lax.axis_size(axis)
    spread = jnp.broadcast_to(value[None], (n,) + value.shape)
    got = lax.all_to_all(spread, axis, 0, 0, tiled=True)
    return got.reshape((n * value.shape[0],) + value.shape[1:])


def grp_gather(value):
    return a2a_gather(a2a_gather(value, "gy"), "gx")


def a2a_sum(parts, axis):
    got = lax.all_to_all(parts, axis, 0, 0, tiled=True)
    return jnp.sum(got.astype(jnp.float32), axis=0)


def attend_part(query, allowed, keys, values):
    score = jnp.dot(query, keys.T, preferred_element_type=jnp.float32) * DH ** (-0.5)
    top = jnp.max(jnp.where(allowed, score, -1e30), axis=1)
    expo = jnp.where(allowed, jnp.exp(score - top[:, None]), 0.0).astype(jnp.bfloat16)
    total = jnp.sum(expo.astype(jnp.float32), axis=1)
    acc = jnp.dot(expo, values, preferred_element_type=jnp.float32)
    return top, total, acc


def body(
    patches,
    patch_image,
    vis_gain,
    vis_bias,
    vis_qkv,
    vis_out,
    merge_weight,
    positions,
    text,
    dec_gain,
    dec_bias,
    dec_qkv,
):
    groups = lax.axis_size(GRP)
    here = lax.axis_index(GRP)
    rows = patches.shape[0]
    merged_count = rows // 4
    text_count = text.shape[0]
    tok = text_count + merged_count
    cap = merged_count // min(groups, 16)

    tnorm = normalize(text.astype(jnp.float32), dec_gain, dec_bias).astype(jnp.bfloat16)
    tproj = jnp.einsum("td,sde->ste", tnorm, dec_qkv, preferred_element_type=jnp.float32).astype(
        jnp.bfloat16
    )
    digit = 128
    pad_rows = 8
    lanes = 2 * DH
    pos_rows = jnp.stack([positions // digit, positions % digit]).astype(jnp.bfloat16)
    extra = jnp.zeros((pad_rows, lanes), jnp.bfloat16).at[:2].set(pos_rows.reshape(2, lanes))
    payload = jnp.concatenate([jnp.concatenate([tproj[1], tproj[2]], axis=1), extra], axis=0)
    text_kv = lax.all_gather(payload, GRP, axis=0, tiled=True)
    digits = text_kv.reshape(groups, text_count + pad_rows, lanes)[:, text_count : text_count + 2]
    digits = digits.astype(jnp.int32)
    all_pos = (digits[:, 0] * digit + digits[:, 1]).reshape(-1)

    place = jnp.arange(tok, dtype=jnp.int32)
    flags = jnp.sum((all_pos[None, :] == (here * tok + place)[:, None]).astype(jnp.int32), axis=1)
    free = 1 - flags
    text_rank = jnp.cumsum(free) - 1
    pick = (free[:, None] == 1) & (text_rank[:, None] == jnp.arange(text_count, dtype=jnp.int32)[None, :])
    own_text_pos = jnp.sum(jnp.where(pick, place[:, None], 0), axis=0) + here * tok

    heads = vis_qkv.shape[2] // HD
    patches_f = patches.astype(jnp.float32)
    normed = normalize(patches_f, vis_gain, vis_bias).astype(jnp.bfloat16)
    proj = jnp.einsum("pd,sde->spe", normed, vis_qkv, preferred_element_type=jnp.float32).astype(
        jnp.bfloat16
    )
    query = proj[0].reshape(rows, heads, HD)
    swap = [(i, i ^ 1) for i in range(lax.axis_size("gy"))]
    partner_kv, partner_ids = lax.ppermute((proj[1:], patch_image), "gy", swap)
    both_kv = jnp.concatenate([proj[1:], partner_kv], axis=1)
    both_ids = jnp.concatenate([patch_image, partner_ids], axis=0)
    keys = both_kv[0].reshape(2 * rows, heads, HD)
    values = both_kv[1].reshape(2 * rows, heads, HD)
    scores = jnp.einsum("phe,khe->hpk", query, keys, preferred_element_type=jnp.float32) * HD ** (
        -0.5
    )
    same = patch_image[:, None] == both_ids[None, :]
    top = jnp.max(jnp.where(same, scores, -1e30), axis=2, keepdims=True)
    expo = jnp.where(same, jnp.exp(scores - top), 0.0)
    weights = (expo / jnp.sum(expo, axis=2, keepdims=True)).astype(jnp.bfloat16)
    attended = jnp.einsum(
        "hpk,khe->phe", weights, values, preferred_element_type=jnp.float32
    ).astype(jnp.bfloat16)
    attended = attended.reshape(rows, heads * HD)

    nz = lax.axis_size("z")
    ncore = lax.axis_size("core")
    width = patches.shape[1] // (nz * ncore)
    core = lax.axis_index("core")
    vo = vis_out.reshape(vis_out.shape[0], nz, ncore, width)
    keep_w = lax.dynamic_index_in_dim(vo, core, 2, keepdims=False)
    send_w = lax.dynamic_index_in_dim(vo, 1 - core, 2, keepdims=False)
    keep = jnp.einsum("pe,ezf->zfp", attended, keep_w, preferred_element_type=jnp.float32)
    send = jnp.einsum("pe,ezf->zfp", attended, send_w, preferred_element_type=jnp.float32)
    pair = [(i, i ^ 1) for i in range(ncore)]
    half = (
        keep.astype(jnp.bfloat16).astype(jnp.float32)
        + lax.ppermute(send.astype(jnp.bfloat16), "core", pair).astype(jnp.float32)
    ).astype(jnp.bfloat16)
    mixed = a2a_sum(half, "z")
    own_cols = lax.dynamic_slice_in_dim(patches, lax.axis_index(TP) * width, width, 1)
    visual = (mixed + own_cols.astype(jnp.float32).T).astype(jnp.bfloat16)
    windows = visual.reshape(width, merged_count, 4)
    partial_rows = jnp.einsum(
        "cmk,kce->me", windows, merge_weight, preferred_element_type=jnp.float32
    ).astype(jnp.bfloat16)
    ntp = nz * ncore
    merged = a2a_gather(
        a2a_sum(partial_rows.reshape(ntp, merged_count // ntp, -1), TP).astype(jnp.bfloat16), TP
    )

    mnorm = normalize(merged.astype(jnp.float32), dec_gain, dec_bias).astype(jnp.bfloat16)
    mproj = jnp.einsum("td,sde->ste", mnorm, dec_qkv, preferred_element_type=jnp.float32).astype(
        jnp.bfloat16
    )
    merged_kv = grp_gather(jnp.concatenate([mproj[1], mproj[2]], axis=1))

    query_pos = jnp.concatenate([own_text_pos, positions], axis=0)
    block = positions // tok
    seen = jnp.sum(
        ((all_pos[None, :] >= (block * tok)[:, None]) & (all_pos[None, :] <= positions[:, None])).astype(
            jnp.int32
        ),
        axis=1,
    )
    merged_limit = block * text_count + (positions - block * tok + 1 - seen)
    text_limit = here * text_count + jnp.arange(text_count, dtype=jnp.int32) + 1
    key_row = jnp.arange(groups * (text_count + pad_rows), dtype=jnp.int32)
    key_grp = key_row // (text_count + pad_rows)
    key_in = key_row % (text_count + pad_rows)
    text_key = jnp.where(key_in < text_count, key_grp * text_count + key_in, groups * tok)
    text_keys, text_values = text_kv[:, :DH], text_kv[:, DH:]
    part_tt = attend_part(tproj[0], text_key[None, :] < text_limit[:, None], text_keys, text_values)
    part_mt = attend_part(mproj[0], text_key[None, :] < merged_limit[:, None], text_keys, text_values)
    part_t = [jnp.concatenate([a, b], axis=0) for a, b in zip(part_tt, part_mt)]
    top_t, total_t, acc_t = part_t
    dquery = jnp.concatenate([tproj[0], mproj[0]], axis=0)
    top_m, total_m, acc_m = attend_part(
        dquery, all_pos[None, :] <= query_pos[:, None], merged_kv[:, :DH], merged_kv[:, DH:]
    )
    best = jnp.maximum(top_t, top_m)
    scale_t = jnp.exp(top_t - best)
    scale_m = jnp.exp(top_m - best)
    total = total_t * scale_t + total_m * scale_m
    acc = acc_t * scale_t[:, None] + acc_m * scale_m[:, None]
    result = (acc / total[:, None]).astype(jnp.bfloat16)
    text_out = result[:text_count]
    merged_out = result[text_count:]

    target = positions // tok
    member = (target[:, None] == jnp.arange(groups, dtype=jnp.int32)[None, :]).astype(jnp.int32)
    rank = jnp.sum(jnp.cumsum(member, axis=0) * member, axis=1) - 1
    slot = target * cap + rank
    select = slot[None, :] == jnp.arange(groups * cap, dtype=jnp.int32)[:, None]
    packed = jnp.dot(
        select.astype(jnp.bfloat16), merged_out, preferred_element_type=jnp.float32
    ).astype(jnp.bfloat16)
    got = lax.all_to_all(packed, GRP, 0, 0, tiled=True)

    src_pos = all_pos.reshape(groups, merged_count)
    to_me = (src_pos // tok) == here
    src_rank = jnp.cumsum(to_me.astype(jnp.int32), axis=1) - 1
    slot_hit = to_me[:, :, None] & (
        src_rank[:, :, None] == jnp.arange(cap, dtype=jnp.int32)[None, None, :]
    )
    got_pos = jnp.sum(jnp.where(slot_hit, src_pos[:, :, None] + 1, 0), axis=1).reshape(-1) - 1
    local = got_pos - here * tok
    landing = (local[None, :] == place[:, None]) & (got_pos[None, :] >= 0)
    text_land = own_text_pos[None, :] - here * tok == place[:, None]
    out = jnp.dot(landing.astype(jnp.bfloat16), got, preferred_element_type=jnp.float32)
    out = out + jnp.dot(
        text_land.astype(jnp.bfloat16), text_out, preferred_element_type=jnp.float32
    )
    return out.astype(jnp.bfloat16)


def solution(mesh):
    grid = mesh.devices.reshape(4, mesh.devices.shape[0] // 4, mesh.devices.shape[1] // 2, 2)
    mesh4 = Mesh(grid, GRP + TP)
    in_specs = (
        P(GRP, None),
        P(GRP),
        P(),
        P(),
        P(None, None, TP),
        P(TP, None),
        P(None, TP, None),
        P(GRP),
        P(GRP, None),
        P(),
        P(),
        P(None, None, TP),
    )
    out_specs = P(GRP, TP)
    return jax.shard_map(body, mesh=mesh4, in_specs=in_specs, out_specs=out_specs, check_vma=False)
```

```python
import jax
import jax.numpy as jnp
from jax import lax
from jax.sharding import Mesh
from jax.sharding import PartitionSpec as P

HD = 104
DH = 64

layer_eps = 1e-05

GRP = ("gx", "gy")
TP = ("z", "core")


def normalize(values, gain, bias):
    mean = jnp.mean(values, axis=-1, keepdims=True)
    centred = values - mean
    spread = jnp.mean(centred * centred, axis=-1, keepdims=True)
    return centred * lax.rsqrt(spread + layer_eps) * gain + bias


def a2a_gather(value, axis):
    n = lax.axis_size(axis)
    spread = jnp.broadcast_to(value[None], (n,) + value.shape)
    got = lax.all_to_all(spread, axis, 0, 0, tiled=True)
    return got.reshape((n * value.shape[0],) + value.shape[1:])


def grp_gather(value):
    return a2a_gather(a2a_gather(value, "gy"), "gx")


def a2a_sum(parts, axis):
    got = lax.all_to_all(parts, axis, 0, 0, tiled=True)
    return jnp.sum(got.astype(jnp.float32), axis=0)


def attend_part(query, allowed, keys, values):
    score = jnp.dot(query, keys.T, preferred_element_type=jnp.float32) * DH ** (-0.5)
    top = jnp.max(jnp.where(allowed, score, -1e30), axis=1)
    expo = jnp.where(allowed, jnp.exp(score - top[:, None]), 0.0).astype(jnp.bfloat16)
    total = jnp.sum(expo.astype(jnp.float32), axis=1)
    acc = jnp.dot(expo, values, preferred_element_type=jnp.float32)
    return top, total, acc


def body(
    patches,
    patch_image,
    vis_gain,
    vis_bias,
    vis_qkv,
    vis_out,
    merge_weight,
    positions,
    text,
    dec_gain,
    dec_bias,
    dec_qkv,
):
    groups = lax.axis_size(GRP)
    here = lax.axis_index(GRP)
    rows = patches.shape[0]
    merged_count = rows // 4
    text_count = text.shape[0]
    tok = text_count + merged_count
    cap = merged_count // min(groups, 16)

    tnorm = normalize(text.astype(jnp.float32), dec_gain, dec_bias).astype(jnp.bfloat16)
    tproj = jnp.einsum("td,sde->ste", tnorm, dec_qkv, preferred_element_type=jnp.float32).astype(
        jnp.bfloat16
    )
    digit = 128
    pad_rows = 8
    lanes = 2 * DH
    pos_rows = jnp.stack([positions // digit, positions % digit]).astype(jnp.bfloat16)
    extra = jnp.zeros((pad_rows, lanes), jnp.bfloat16).at[:2].set(pos_rows.reshape(2, lanes))
    payload = jnp.concatenate([jnp.concatenate([tproj[1], tproj[2]], axis=1), extra], axis=0)
    text_kv = lax.all_gather(payload, GRP, axis=0, tiled=True)
    digits = text_kv.reshape(groups, text_count + pad_rows, lanes)[:, text_count : text_count + 2]
    digits = digits.astype(jnp.int32)
    all_pos = (digits[:, 0] * digit + digits[:, 1]).reshape(-1)

    place = jnp.arange(tok, dtype=jnp.int32)
    flags = jnp.sum((all_pos[None, :] == (here * tok + place)[:, None]).astype(jnp.int32), axis=1)
    free = 1 - flags
    text_rank = jnp.cumsum(free) - 1
    pick = (free[:, None] == 1) & (text_rank[:, None] == jnp.arange(text_count, dtype=jnp.int32)[None, :])
    own_text_pos = jnp.sum(jnp.where(pick, place[:, None], 0), axis=0) + here * tok

    heads = vis_qkv.shape[2] // HD
    patches_f = patches.astype(jnp.float32)
    normed = normalize(patches_f, vis_gain, vis_bias).astype(jnp.bfloat16)
    proj = jnp.einsum("pd,sde->spe", normed, vis_qkv, preferred_element_type=jnp.float32).astype(
        jnp.bfloat16
    )
    query = proj[0].reshape(rows, heads, HD)
    swap = [(i, i ^ 1) for i in range(lax.axis_size("gy"))]
    partner_kv, partner_ids = lax.ppermute((proj[1:], patch_image), "gy", swap)
    both_kv = jnp.concatenate([proj[1:], partner_kv], axis=1)
    both_ids = jnp.concatenate([patch_image, partner_ids], axis=0)
    keys = both_kv[0].reshape(2 * rows, heads, HD)
    values = both_kv[1].reshape(2 * rows, heads, HD)
    scores = jnp.einsum("phe,khe->hpk", query, keys, preferred_element_type=jnp.float32) * HD ** (
        -0.5
    )
    same = patch_image[:, None] == both_ids[None, :]
    top = jnp.max(jnp.where(same, scores, -1e30), axis=2, keepdims=True)
    expo = jnp.where(same, jnp.exp(scores - top), 0.0)
    weights = (expo / jnp.sum(expo, axis=2, keepdims=True)).astype(jnp.bfloat16)
    attended = jnp.einsum(
        "hpk,khe->phe", weights, values, preferred_element_type=jnp.float32
    ).astype(jnp.bfloat16)
    attended = attended.reshape(rows, heads * HD)

    nz = lax.axis_size("z")
    ncore = lax.axis_size("core")
    width = patches.shape[1] // (nz * ncore)
    core = lax.axis_index("core")
    vo = vis_out.reshape(vis_out.shape[0], nz, ncore, width)
    keep_w = lax.dynamic_index_in_dim(vo, core, 2, keepdims=False)
    send_w = lax.dynamic_index_in_dim(vo, 1 - core, 2, keepdims=False)
    keep = jnp.einsum("pe,ezf->zfp", attended, keep_w, preferred_element_type=jnp.float32)
    send = jnp.einsum("pe,ezf->zfp", attended, send_w, preferred_element_type=jnp.float32)
    pair = [(i, i ^ 1) for i in range(ncore)]
    half = (
        keep.astype(jnp.bfloat16).astype(jnp.float32)
        + lax.ppermute(send.astype(jnp.bfloat16), "core", pair).astype(jnp.float32)
    ).astype(jnp.bfloat16)
    mixed = a2a_sum(half, "z")
    own_cols = lax.dynamic_slice_in_dim(patches, lax.axis_index(TP) * width, width, 1)
    visual = (mixed + own_cols.astype(jnp.float32).T).astype(jnp.bfloat16)
    windows = visual.reshape(width, merged_count, 4)
    partial_rows = jnp.einsum(
        "cmk,kce->me", windows, merge_weight, preferred_element_type=jnp.float32
    ).astype(jnp.bfloat16)
    ntp = nz * ncore
    merged = a2a_gather(
        a2a_sum(partial_rows.reshape(ntp, merged_count // ntp, -1), TP).astype(jnp.bfloat16), TP
    )

    mnorm = normalize(merged.astype(jnp.float32), dec_gain, dec_bias).astype(jnp.bfloat16)
    mproj = jnp.einsum("td,sde->ste", mnorm, dec_qkv, preferred_element_type=jnp.float32).astype(
        jnp.bfloat16
    )
    merged_kv = grp_gather(jnp.concatenate([mproj[1], mproj[2]], axis=1))

    query_pos = jnp.concatenate([own_text_pos, positions], axis=0)
    block = positions // tok
    seen = jnp.sum(
        ((all_pos[None, :] >= (block * tok)[:, None]) & (all_pos[None, :] <= positions[:, None])).astype(
            jnp.int32
        ),
        axis=1,
    )
    merged_limit = block * text_count + (positions - block * tok + 1 - seen)
    text_limit = here * text_count + jnp.arange(text_count, dtype=jnp.int32) + 1
    key_row = jnp.arange(groups * (text_count + pad_rows), dtype=jnp.int32)
    key_grp = key_row // (text_count + pad_rows)
    key_in = key_row % (text_count + pad_rows)
    text_key = jnp.where(key_in < text_count, key_grp * text_count + key_in, groups * tok)
    text_keys, text_values = text_kv[:, :DH], text_kv[:, DH:]
    part_tt = attend_part(tproj[0], text_key[None, :] < text_limit[:, None], text_keys, text_values)
    part_mt = attend_part(mproj[0], text_key[None, :] < merged_limit[:, None], text_keys, text_values)
    part_t = [jnp.concatenate([a, b], axis=0) for a, b in zip(part_tt, part_mt)]
    top_t, total_t, acc_t = part_t
    dquery = jnp.concatenate([tproj[0], mproj[0]], axis=0)
    top_m, total_m, acc_m = attend_part(
        dquery, all_pos[None, :] <= query_pos[:, None], merged_kv[:, :DH], merged_kv[:, DH:]
    )
    best = jnp.maximum(top_t, top_m)
    scale_t = jnp.exp(top_t - best)
    scale_m = jnp.exp(top_m - best)
    total = total_t * scale_t + total_m * scale_m
    acc = acc_t * scale_t[:, None] + acc_m * scale_m[:, None]
    result = (acc / total[:, None]).astype(jnp.bfloat16)
    text_out = result[:text_count]
    merged_out = result[text_count:]

    target = positions // tok
    member = (target[:, None] == jnp.arange(groups, dtype=jnp.int32)[None, :]).astype(jnp.int32)
    rank = jnp.sum(jnp.cumsum(member, axis=0) * member, axis=1) - 1
    slot = target * cap + rank
    select = slot[None, :] == jnp.arange(groups * cap, dtype=jnp.int32)[:, None]
    packed = jnp.dot(
        select.astype(jnp.bfloat16), merged_out, preferred_element_type=jnp.float32
    ).astype(jnp.bfloat16)
    wide = jnp.concatenate([packed, jnp.zeros_like(packed)], axis=1)
    got = lax.all_to_all(wide.reshape(groups, cap, 2 * DH), GRP, 0, 0, tiled=True)
    got = got.reshape(groups * cap, 2 * DH)[:, :DH]

    src_pos = all_pos.reshape(groups, merged_count)
    to_me = (src_pos // tok) == here
    src_rank = jnp.cumsum(to_me.astype(jnp.int32), axis=1) - 1
    slot_hit = to_me[:, :, None] & (
        src_rank[:, :, None] == jnp.arange(cap, dtype=jnp.int32)[None, None, :]
    )
    got_pos = jnp.sum(jnp.where(slot_hit, src_pos[:, :, None] + 1, 0), axis=1).reshape(-1) - 1
    local = got_pos - here * tok
    landing = (local[None, :] == place[:, None]) & (got_pos[None, :] >= 0)
    text_land = own_text_pos[None, :] - here * tok == place[:, None]
    out = jnp.dot(landing.astype(jnp.bfloat16), got, preferred_element_type=jnp.float32)
    out = out + jnp.dot(
        text_land.astype(jnp.bfloat16), text_out, preferred_element_type=jnp.float32
    )
    return out.astype(jnp.bfloat16)


def solution(mesh):
    grid = mesh.devices.reshape(4, mesh.devices.shape[0] // 4, mesh.devices.shape[1] // 2, 2)
    mesh4 = Mesh(grid, GRP + TP)
    in_specs = (
        P(GRP, None),
        P(GRP),
        P(),
        P(),
        P(None, None, TP),
        P(TP, None),
        P(None, TP, None),
        P(GRP),
        P(GRP, None),
        P(),
        P(),
        P(None, None, TP),
    )
    out_specs = P(GRP, TP)
    return jax.shard_map(body, mesh=mesh4, in_specs=in_specs, out_specs=out_specs, check_vma=False)
```

```python
import jax
import jax.numpy as jnp
from jax import lax
from jax.sharding import Mesh
from jax.sharding import PartitionSpec as P

HD = 104
DH = 64

layer_eps = 1e-05

GRP = ("gx", "gy")
TP = ("z", "core")


def normalize(values, gain, bias):
    mean = jnp.mean(values, axis=-1, keepdims=True)
    centred = values - mean
    spread = jnp.mean(centred * centred, axis=-1, keepdims=True)
    return centred * lax.rsqrt(spread + layer_eps) * gain + bias


def a2a_gather(value, axis):
    n = lax.axis_size(axis)
    spread = jnp.broadcast_to(value[None], (n,) + value.shape)
    got = lax.all_to_all(spread, axis, 0, 0, tiled=True)
    return got.reshape((n * value.shape[0],) + value.shape[1:])


def grp_gather(value):
    return a2a_gather(a2a_gather(value, "gy"), "gx")


def a2a_sum(parts, axis):
    got = lax.all_to_all(parts, axis, 0, 0, tiled=True)
    return jnp.sum(got.astype(jnp.float32), axis=0)


def attend_part(query, allowed, keys, values):
    score = jnp.dot(query, keys.T, preferred_element_type=jnp.float32) * DH ** (-0.5)
    top = jnp.max(jnp.where(allowed, score, -1e30), axis=1)
    expo = jnp.where(allowed, jnp.exp(score - top[:, None]), 0.0).astype(jnp.bfloat16)
    total = jnp.sum(expo.astype(jnp.float32), axis=1)
    acc = jnp.dot(expo, values, preferred_element_type=jnp.float32)
    return top, total, acc


def body(
    patches,
    patch_image,
    vis_gain,
    vis_bias,
    vis_qkv,
    vis_out,
    merge_weight,
    positions,
    text,
    dec_gain,
    dec_bias,
    dec_qkv,
):
    groups = lax.axis_size(GRP)
    here = lax.axis_index(GRP)
    rows = patches.shape[0]
    merged_count = rows // 4
    text_count = text.shape[0]
    tok = text_count + merged_count
    cap = merged_count // min(groups, 16)

    tnorm = normalize(text.astype(jnp.float32), dec_gain, dec_bias).astype(jnp.bfloat16)
    tproj = jnp.einsum("td,sde->ste", tnorm, dec_qkv, preferred_element_type=jnp.float32).astype(
        jnp.bfloat16
    )
    digit = 128
    pad_rows = 8
    lanes = 2 * DH
    pos_rows = jnp.stack([positions // digit, positions % digit]).astype(jnp.bfloat16)
    extra = jnp.zeros((pad_rows, lanes), jnp.bfloat16).at[:2].set(pos_rows.reshape(2, lanes))
    payload = jnp.concatenate([jnp.concatenate([tproj[1], tproj[2]], axis=1), extra], axis=0)
    text_kv = lax.all_gather(payload, GRP, axis=0, tiled=True)
    digits = text_kv.reshape(groups, text_count + pad_rows, lanes)[:, text_count : text_count + 2]
    digits = digits.astype(jnp.int32)
    all_pos = (digits[:, 0] * digit + digits[:, 1]).reshape(-1)

    place = jnp.arange(tok, dtype=jnp.int32)
    flags = jnp.sum((all_pos[None, :] == (here * tok + place)[:, None]).astype(jnp.int32), axis=1)
    free = 1 - flags
    text_rank = jnp.cumsum(free) - 1
    pick = (free[:, None] == 1) & (text_rank[:, None] == jnp.arange(text_count, dtype=jnp.int32)[None, :])
    own_text_pos = jnp.sum(jnp.where(pick, place[:, None], 0), axis=0) + here * tok

    heads = vis_qkv.shape[2] // HD
    patches_f = patches.astype(jnp.float32)
    normed = normalize(patches_f, vis_gain, vis_bias).astype(jnp.bfloat16)
    proj = jnp.einsum("pd,sde->spe", normed, vis_qkv, preferred_element_type=jnp.float32).astype(
        jnp.bfloat16
    )
    query = proj[0].reshape(rows, heads, HD)
    swap = [(i, i ^ 1) for i in range(lax.axis_size("gy"))]
    partner_kv, partner_ids = lax.ppermute((proj[1:], patch_image), "gy", swap)
    both_kv = jnp.concatenate([proj[1:], partner_kv], axis=1)
    both_ids = jnp.concatenate([patch_image, partner_ids], axis=0)
    keys = both_kv[0].reshape(2 * rows, heads, HD)
    values = both_kv[1].reshape(2 * rows, heads, HD)
    scores = jnp.einsum("phe,khe->hpk", query, keys, preferred_element_type=jnp.float32) * HD ** (
        -0.5
    )
    same = patch_image[:, None] == both_ids[None, :]
    top = jnp.max(jnp.where(same, scores, -1e30), axis=2, keepdims=True)
    expo = jnp.where(same, jnp.exp(scores - top), 0.0)
    weights = (expo / jnp.sum(expo, axis=2, keepdims=True)).astype(jnp.bfloat16)
    attended = jnp.einsum(
        "hpk,khe->phe", weights, values, preferred_element_type=jnp.float32
    ).astype(jnp.bfloat16)
    attended = attended.reshape(rows, heads * HD)

    nz = lax.axis_size("z")
    ncore = lax.axis_size("core")
    width = patches.shape[1] // (nz * ncore)
    core = lax.axis_index("core")
    vo = vis_out.reshape(vis_out.shape[0], nz, ncore, width)
    keep_w = lax.dynamic_index_in_dim(vo, core, 2, keepdims=False)
    send_w = lax.dynamic_index_in_dim(vo, 1 - core, 2, keepdims=False)
    keep = jnp.einsum("pe,ezf->zfp", attended, keep_w, preferred_element_type=jnp.float32)
    send = jnp.einsum("pe,ezf->zfp", attended, send_w, preferred_element_type=jnp.float32)
    pair = [(i, i ^ 1) for i in range(ncore)]
    half = (
        keep.astype(jnp.bfloat16).astype(jnp.float32)
        + lax.ppermute(send.astype(jnp.bfloat16), "core", pair).astype(jnp.float32)
    ).astype(jnp.bfloat16)
    mixed = a2a_sum(half, "z")
    own_cols = lax.dynamic_slice_in_dim(patches, lax.axis_index(TP) * width, width, 1)
    visual = (mixed + own_cols.astype(jnp.float32).T).astype(jnp.bfloat16)
    windows = visual.reshape(width, merged_count, 4)
    partial_rows = jnp.einsum(
        "cmk,kce->me", windows, merge_weight, preferred_element_type=jnp.float32
    ).astype(jnp.bfloat16)
    ntp = nz * ncore
    merged = a2a_gather(
        a2a_sum(partial_rows.reshape(ntp, merged_count // ntp, -1), TP).astype(jnp.bfloat16), TP
    )

    mnorm = normalize(merged.astype(jnp.float32), dec_gain, dec_bias).astype(jnp.bfloat16)
    mproj = jnp.einsum("td,sde->ste", mnorm, dec_qkv, preferred_element_type=jnp.float32).astype(
        jnp.bfloat16
    )
    merged_kv = a2a_gather(jnp.concatenate([mproj[1], mproj[2]], axis=1), GRP)

    query_pos = jnp.concatenate([own_text_pos, positions], axis=0)
    block = positions // tok
    seen = jnp.sum(
        ((all_pos[None, :] >= (block * tok)[:, None]) & (all_pos[None, :] <= positions[:, None])).astype(
            jnp.int32
        ),
        axis=1,
    )
    merged_limit = block * text_count + (positions - block * tok + 1 - seen)
    text_limit = here * text_count + jnp.arange(text_count, dtype=jnp.int32) + 1
    key_row = jnp.arange(groups * (text_count + pad_rows), dtype=jnp.int32)
    key_grp = key_row // (text_count + pad_rows)
    key_in = key_row % (text_count + pad_rows)
    text_key = jnp.where(key_in < text_count, key_grp * text_count + key_in, groups * tok)
    text_keys, text_values = text_kv[:, :DH], text_kv[:, DH:]
    part_tt = attend_part(tproj[0], text_key[None, :] < text_limit[:, None], text_keys, text_values)
    part_mt = attend_part(mproj[0], text_key[None, :] < merged_limit[:, None], text_keys, text_values)
    part_t = [jnp.concatenate([a, b], axis=0) for a, b in zip(part_tt, part_mt)]
    top_t, total_t, acc_t = part_t
    dquery = jnp.concatenate([tproj[0], mproj[0]], axis=0)
    top_m, total_m, acc_m = attend_part(
        dquery, all_pos[None, :] <= query_pos[:, None], merged_kv[:, :DH], merged_kv[:, DH:]
    )
    best = jnp.maximum(top_t, top_m)
    scale_t = jnp.exp(top_t - best)
    scale_m = jnp.exp(top_m - best)
    total = total_t * scale_t + total_m * scale_m
    acc = acc_t * scale_t[:, None] + acc_m * scale_m[:, None]
    result = (acc / total[:, None]).astype(jnp.bfloat16)
    text_out = result[:text_count]
    merged_out = result[text_count:]

    target = positions // tok
    member = (target[:, None] == jnp.arange(groups, dtype=jnp.int32)[None, :]).astype(jnp.int32)
    rank = jnp.sum(jnp.cumsum(member, axis=0) * member, axis=1) - 1
    slot = target * cap + rank
    select = slot[None, :] == jnp.arange(groups * cap, dtype=jnp.int32)[:, None]
    packed = jnp.dot(
        select.astype(jnp.bfloat16), merged_out, preferred_element_type=jnp.float32
    ).astype(jnp.bfloat16)
    got = lax.all_to_all(packed, GRP, 0, 0, tiled=True)

    src_pos = all_pos.reshape(groups, merged_count)
    to_me = (src_pos // tok) == here
    src_rank = jnp.cumsum(to_me.astype(jnp.int32), axis=1) - 1
    slot_hit = to_me[:, :, None] & (
        src_rank[:, :, None] == jnp.arange(cap, dtype=jnp.int32)[None, None, :]
    )
    got_pos = jnp.sum(jnp.where(slot_hit, src_pos[:, :, None] + 1, 0), axis=1).reshape(-1) - 1
    local = got_pos - here * tok
    landing = (local[None, :] == place[:, None]) & (got_pos[None, :] >= 0)
    text_land = own_text_pos[None, :] - here * tok == place[:, None]
    out = jnp.dot(landing.astype(jnp.bfloat16), got, preferred_element_type=jnp.float32)
    out = out + jnp.dot(
        text_land.astype(jnp.bfloat16), text_out, preferred_element_type=jnp.float32
    )
    return out.astype(jnp.bfloat16)


def solution(mesh):
    grid = mesh.devices.reshape(4, mesh.devices.shape[0] // 4, mesh.devices.shape[1] // 2, 2)
    mesh4 = Mesh(grid, GRP + TP)
    in_specs = (
        P(GRP, None),
        P(GRP),
        P(),
        P(),
        P(None, None, TP),
        P(TP, None),
        P(None, TP, None),
        P(GRP),
        P(GRP, None),
        P(),
        P(),
        P(None, None, TP),
    )
    out_specs = P(GRP, TP)
    return jax.shard_map(body, mesh=mesh4, in_specs=in_specs, out_specs=out_specs, check_vma=False)
```

```python
import jax
import jax.numpy as jnp
from jax import lax
from jax.sharding import Mesh
from jax.sharding import PartitionSpec as P

HD = 104
DH = 64

layer_eps = 1e-05

GRP = ("gx", "gy")
TP = ("z", "core")


def normalize(values, gain, bias):
    mean = jnp.mean(values, axis=-1, keepdims=True)
    centred = values - mean
    spread = jnp.mean(centred * centred, axis=-1, keepdims=True)
    return centred * lax.rsqrt(spread + layer_eps) * gain + bias


def normalize_shifted(values, gain, bias):
    shift = values[:, :1]
    moved = values - shift
    first = jnp.mean(moved, axis=-1, keepdims=True)
    second = jnp.mean(moved * moved, axis=-1, keepdims=True)
    spread = jnp.maximum(second - first * first, 0.0)
    return (moved - first) * lax.rsqrt(spread + layer_eps) * gain + bias


def a2a_gather(value, axis):
    n = lax.axis_size(axis)
    spread = jnp.broadcast_to(value[None], (n,) + value.shape)
    got = lax.all_to_all(spread, axis, 0, 0, tiled=True)
    return got.reshape((n * value.shape[0],) + value.shape[1:])


def grp_gather(value):
    return a2a_gather(a2a_gather(value, "gy"), "gx")


def a2a_sum(parts, axis):
    got = lax.all_to_all(parts, axis, 0, 0, tiled=True)
    return jnp.sum(got.astype(jnp.float32), axis=0)


def attend_part(query, allowed, keys, values):
    score = jnp.dot(query, keys.T, preferred_element_type=jnp.float32) * DH ** (-0.5)
    top = jnp.max(jnp.where(allowed, score, -1e30), axis=1)
    expo = jnp.where(allowed, jnp.exp(score - top[:, None]), 0.0).astype(jnp.bfloat16)
    total = jnp.sum(expo.astype(jnp.float32), axis=1)
    acc = jnp.dot(expo, values, preferred_element_type=jnp.float32)
    return top, total, acc


def body(
    patches,
    patch_image,
    vis_gain,
    vis_bias,
    vis_qkv,
    vis_out,
    merge_weight,
    positions,
    text,
    dec_gain,
    dec_bias,
    dec_qkv,
):
    groups = lax.axis_size(GRP)
    here = lax.axis_index(GRP)
    rows = patches.shape[0]
    merged_count = rows // 4
    text_count = text.shape[0]
    tok = text_count + merged_count
    cap = merged_count // min(groups, 16)

    tnorm = normalize(text.astype(jnp.float32), dec_gain, dec_bias).astype(jnp.bfloat16)
    tproj = jnp.einsum("td,sde->ste", tnorm, dec_qkv, preferred_element_type=jnp.float32).astype(
        jnp.bfloat16
    )
    digit = 128
    pad_rows = 8
    lanes = 2 * DH
    pos_rows = jnp.stack([positions // digit, positions % digit]).astype(jnp.bfloat16)
    extra = jnp.zeros((pad_rows, lanes), jnp.bfloat16).at[:2].set(pos_rows.reshape(2, lanes))
    payload = jnp.concatenate([jnp.concatenate([tproj[1], tproj[2]], axis=1), extra], axis=0)
    text_kv = lax.all_gather(payload, GRP, axis=0, tiled=True)
    digits = text_kv.reshape(groups, text_count + pad_rows, lanes)[:, text_count : text_count + 2]
    digits = digits.astype(jnp.int32)
    all_pos = (digits[:, 0] * digit + digits[:, 1]).reshape(-1)

    place = jnp.arange(tok, dtype=jnp.int32)
    flags = jnp.sum((all_pos[None, :] == (here * tok + place)[:, None]).astype(jnp.int32), axis=1)
    free = 1 - flags
    text_rank = jnp.cumsum(free) - 1
    pick = (free[:, None] == 1) & (text_rank[:, None] == jnp.arange(text_count, dtype=jnp.int32)[None, :])
    own_text_pos = jnp.sum(jnp.where(pick, place[:, None], 0), axis=0) + here * tok

    heads = vis_qkv.shape[2] // HD
    patches_f = patches.astype(jnp.float32)
    normed = normalize_shifted(patches_f, vis_gain, vis_bias).astype(jnp.bfloat16)
    proj = jnp.einsum("pd,sde->spe", normed, vis_qkv, preferred_element_type=jnp.float32).astype(
        jnp.bfloat16
    )
    query = proj[0].reshape(rows, heads, HD)
    swap = [(i, i ^ 1) for i in range(lax.axis_size("gy"))]
    partner_kv, partner_ids = lax.ppermute((proj[1:], patch_image), "gy", swap)
    both_kv = jnp.concatenate([proj[1:], partner_kv], axis=1)
    both_ids = jnp.concatenate([patch_image, partner_ids], axis=0)
    keys = both_kv[0].reshape(2 * rows, heads, HD)
    values = both_kv[1].reshape(2 * rows, heads, HD)
    scores = jnp.einsum("phe,khe->hpk", query, keys, preferred_element_type=jnp.float32) * HD ** (
        -0.5
    )
    same = patch_image[:, None] == both_ids[None, :]
    top = jnp.max(jnp.where(same, scores, -1e30), axis=2, keepdims=True)
    expo = jnp.where(same, jnp.exp(scores - top), 0.0)
    weights = (expo / jnp.sum(expo, axis=2, keepdims=True)).astype(jnp.bfloat16)
    attended = jnp.einsum(
        "hpk,khe->phe", weights, values, preferred_element_type=jnp.float32
    ).astype(jnp.bfloat16)
    attended = attended.reshape(rows, heads * HD)

    nz = lax.axis_size("z")
    ncore = lax.axis_size("core")
    width = patches.shape[1] // (nz * ncore)
    core = lax.axis_index("core")
    vo = vis_out.reshape(vis_out.shape[0], nz, ncore, width)
    keep_w = lax.dynamic_index_in_dim(vo, core, 2, keepdims=False)
    send_w = lax.dynamic_index_in_dim(vo, 1 - core, 2, keepdims=False)
    keep = jnp.einsum("pe,ezf->zfp", attended, keep_w, preferred_element_type=jnp.float32)
    send = jnp.einsum("pe,ezf->zfp", attended, send_w, preferred_element_type=jnp.float32)
    pair = [(i, i ^ 1) for i in range(ncore)]
    half = (
        keep.astype(jnp.bfloat16).astype(jnp.float32)
        + lax.ppermute(send.astype(jnp.bfloat16), "core", pair).astype(jnp.float32)
    ).astype(jnp.bfloat16)
    mixed = a2a_sum(half, "z")
    own_cols = lax.dynamic_slice_in_dim(patches, lax.axis_index(TP) * width, width, 1)
    visual = (mixed + own_cols.astype(jnp.float32).T).astype(jnp.bfloat16)
    windows = visual.reshape(width, merged_count, 4)
    partial_rows = jnp.einsum(
        "cmk,kce->me", windows, merge_weight, preferred_element_type=jnp.float32
    ).astype(jnp.bfloat16)
    ntp = nz * ncore
    merged = a2a_gather(
        a2a_sum(partial_rows.reshape(ntp, merged_count // ntp, -1), TP).astype(jnp.bfloat16), TP
    )

    mnorm = normalize(merged.astype(jnp.float32), dec_gain, dec_bias).astype(jnp.bfloat16)
    mproj = jnp.einsum("td,sde->ste", mnorm, dec_qkv, preferred_element_type=jnp.float32).astype(
        jnp.bfloat16
    )
    merged_kv = grp_gather(jnp.concatenate([mproj[1], mproj[2]], axis=1))

    query_pos = jnp.concatenate([own_text_pos, positions], axis=0)
    block = positions // tok
    seen = jnp.sum(
        ((all_pos[None, :] >= (block * tok)[:, None]) & (all_pos[None, :] <= positions[:, None])).astype(
            jnp.int32
        ),
        axis=1,
    )
    merged_limit = block * text_count + (positions - block * tok + 1 - seen)
    text_limit = here * text_count + jnp.arange(text_count, dtype=jnp.int32) + 1
    key_row = jnp.arange(groups * (text_count + pad_rows), dtype=jnp.int32)
    key_grp = key_row // (text_count + pad_rows)
    key_in = key_row % (text_count + pad_rows)
    text_key = jnp.where(key_in < text_count, key_grp * text_count + key_in, groups * tok)
    text_keys, text_values = text_kv[:, :DH], text_kv[:, DH:]
    part_tt = attend_part(tproj[0], text_key[None, :] < text_limit[:, None], text_keys, text_values)
    part_mt = attend_part(mproj[0], text_key[None, :] < merged_limit[:, None], text_keys, text_values)
    part_t = [jnp.concatenate([a, b], axis=0) for a, b in zip(part_tt, part_mt)]
    top_t, total_t, acc_t = part_t
    dquery = jnp.concatenate([tproj[0], mproj[0]], axis=0)
    top_m, total_m, acc_m = attend_part(
        dquery, all_pos[None, :] <= query_pos[:, None], merged_kv[:, :DH], merged_kv[:, DH:]
    )
    best = jnp.maximum(top_t, top_m)
    scale_t = jnp.exp(top_t - best)
    scale_m = jnp.exp(top_m - best)
    total = total_t * scale_t + total_m * scale_m
    acc = acc_t * scale_t[:, None] + acc_m * scale_m[:, None]
    result = (acc / total[:, None]).astype(jnp.bfloat16)
    text_out = result[:text_count]
    merged_out = result[text_count:]

    target = positions // tok
    member = (target[:, None] == jnp.arange(groups, dtype=jnp.int32)[None, :]).astype(jnp.int32)
    rank = jnp.sum(jnp.cumsum(member, axis=0) * member, axis=1) - 1
    slot = target * cap + rank
    select = slot[None, :] == jnp.arange(groups * cap, dtype=jnp.int32)[:, None]
    packed = jnp.dot(
        select.astype(jnp.bfloat16), merged_out, preferred_element_type=jnp.float32
    ).astype(jnp.bfloat16)
    got = lax.all_to_all(packed, GRP, 0, 0, tiled=True)

    src_pos = all_pos.reshape(groups, merged_count)
    to_me = (src_pos // tok) == here
    src_rank = jnp.cumsum(to_me.astype(jnp.int32), axis=1) - 1
    slot_hit = to_me[:, :, None] & (
        src_rank[:, :, None] == jnp.arange(cap, dtype=jnp.int32)[None, None, :]
    )
    got_pos = jnp.sum(jnp.where(slot_hit, src_pos[:, :, None] + 1, 0), axis=1).reshape(-1) - 1
    local = got_pos - here * tok
    landing = (local[None, :] == place[:, None]) & (got_pos[None, :] >= 0)
    text_land = own_text_pos[None, :] - here * tok == place[:, None]
    out = jnp.dot(landing.astype(jnp.bfloat16), got, preferred_element_type=jnp.float32)
    out = out + jnp.dot(
        text_land.astype(jnp.bfloat16), text_out, preferred_element_type=jnp.float32
    )
    return out.astype(jnp.bfloat16)


def solution(mesh):
    grid = mesh.devices.reshape(4, mesh.devices.shape[0] // 4, mesh.devices.shape[1] // 2, 2)
    mesh4 = Mesh(grid, GRP + TP)
    in_specs = (
        P(GRP, None),
        P(GRP),
        P(),
        P(),
        P(None, None, TP),
        P(TP, None),
        P(None, TP, None),
        P(GRP),
        P(GRP, None),
        P(),
        P(),
        P(None, None, TP),
    )
    out_specs = P(GRP, TP)
    return jax.shard_map(body, mesh=mesh4, in_specs=in_specs, out_specs=out_specs, check_vma=False)
```

```python
import jax
import jax.numpy as jnp
from jax import lax
from jax.sharding import Mesh
from jax.sharding import PartitionSpec as P

HD = 104
DH = 64

layer_eps = 1e-05

GRP = ("gx", "gy")
TP = ("z", "core")


def normalize(values, gain, bias):
    mean = jnp.mean(values, axis=-1, keepdims=True)
    centred = values - mean
    spread = jnp.mean(centred * centred, axis=-1, keepdims=True)
    return centred * lax.rsqrt(spread + layer_eps) * gain + bias


def normalize_shifted(values, gain, bias):
    shift = values[:, :1]
    moved = values - shift
    first = jnp.mean(moved, axis=-1, keepdims=True)
    second = jnp.mean(moved * moved, axis=-1, keepdims=True)
    spread = jnp.maximum(second - first * first, 0.0)
    return (moved - first) * lax.rsqrt(spread + layer_eps) * gain + bias


def a2a_gather(value, axis):
    n = lax.axis_size(axis)
    spread = jnp.broadcast_to(value[None], (n,) + value.shape)
    got = lax.all_to_all(spread, axis, 0, 0, tiled=True)
    return got.reshape((n * value.shape[0],) + value.shape[1:])


def grp_gather(value):
    return a2a_gather(a2a_gather(value, "gy"), "gx")


def a2a_sum(parts, axis):
    got = lax.all_to_all(parts, axis, 0, 0, tiled=True)
    return jnp.sum(got.astype(jnp.float32), axis=0)


def attend_part(query, allowed, keys, values):
    score = jnp.dot(query, keys.T, preferred_element_type=jnp.float32) * DH ** (-0.5)
    top = jnp.max(jnp.where(allowed, score, -1e30), axis=1)
    expo = jnp.where(allowed, jnp.exp(score - top[:, None]), 0.0).astype(jnp.bfloat16)
    total = jnp.sum(expo.astype(jnp.float32), axis=1)
    acc = jnp.dot(expo, values, preferred_element_type=jnp.float32)
    return top, total, acc


def body(
    patches,
    patch_image,
    vis_gain,
    vis_bias,
    vis_qkv,
    vis_out,
    merge_weight,
    positions,
    text,
    dec_gain,
    dec_bias,
    dec_qkv,
):
    groups = lax.axis_size(GRP)
    here = lax.axis_index(GRP)
    rows = patches.shape[0]
    merged_count = rows // 4
    text_count = text.shape[0]
    tok = text_count + merged_count
    cap = merged_count // min(groups, 16)

    tnorm = normalize(text.astype(jnp.float32), dec_gain, dec_bias).astype(jnp.bfloat16)
    tproj = jnp.einsum("td,sde->ste", tnorm, dec_qkv, preferred_element_type=jnp.float32).astype(
        jnp.bfloat16
    )
    digit = 128
    pad_rows = 8
    lanes = 2 * DH
    pos_rows = jnp.stack([positions // digit, positions % digit]).astype(jnp.bfloat16)
    extra = jnp.zeros((pad_rows, lanes), jnp.bfloat16).at[:2].set(pos_rows.reshape(2, lanes))
    payload = jnp.concatenate([jnp.concatenate([tproj[1], tproj[2]], axis=1), extra], axis=0)
    text_kv = lax.all_gather(payload, GRP, axis=0, tiled=True)
    digits = text_kv.reshape(groups, text_count + pad_rows, lanes)[:, text_count : text_count + 2]
    digits = digits.astype(jnp.int32)
    all_pos = (digits[:, 0] * digit + digits[:, 1]).reshape(-1)

    place = jnp.arange(tok, dtype=jnp.int32)
    flags = jnp.sum((all_pos[None, :] == (here * tok + place)[:, None]).astype(jnp.int32), axis=1)
    free = 1 - flags
    text_rank = jnp.cumsum(free) - 1
    pick = (free[:, None] == 1) & (text_rank[:, None] == jnp.arange(text_count, dtype=jnp.int32)[None, :])
    own_text_pos = jnp.sum(jnp.where(pick, place[:, None], 0), axis=0) + here * tok

    heads = vis_qkv.shape[2] // HD
    patches_f = patches.astype(jnp.float32)
    normed = normalize_shifted(patches_f, vis_gain, vis_bias).astype(jnp.bfloat16)
    proj = jnp.einsum("pd,sde->spe", normed, vis_qkv, preferred_element_type=jnp.float32).astype(
        jnp.bfloat16
    )
    query = proj[0].reshape(rows, heads, HD)
    swap = [(i, i ^ 1) for i in range(lax.axis_size("gy"))]
    partner_kv, partner_ids = lax.ppermute((proj[1:], patch_image), "gy", swap)
    both_kv = jnp.concatenate([proj[1:], partner_kv], axis=1)
    both_ids = jnp.concatenate([patch_image, partner_ids], axis=0)
    keys = both_kv[0].reshape(2 * rows, heads, HD)
    values = both_kv[1].reshape(2 * rows, heads, HD)
    scores = jnp.einsum("phe,khe->hpk", query, keys, preferred_element_type=jnp.float32) * HD ** (
        -0.5
    )
    same = patch_image[:, None] == both_ids[None, :]
    top = jnp.max(jnp.where(same, scores, -1e30), axis=2, keepdims=True)
    expo = jnp.where(same, jnp.exp(scores - top), 0.0)
    weights = (expo / jnp.sum(expo, axis=2, keepdims=True)).astype(jnp.bfloat16)
    attended = jnp.einsum(
        "hpk,khe->phe", weights, values, preferred_element_type=jnp.float32
    ).astype(jnp.bfloat16)
    attended = attended.reshape(rows, heads * HD)

    nz = lax.axis_size("z")
    ncore = lax.axis_size("core")
    width = patches.shape[1] // (nz * ncore)
    core = lax.axis_index("core")
    vo = vis_out.reshape(vis_out.shape[0], nz, ncore, width)
    keep_w = lax.dynamic_index_in_dim(vo, core, 2, keepdims=False)
    send_w = lax.dynamic_index_in_dim(vo, 1 - core, 2, keepdims=False)
    keep = jnp.einsum("pe,ezf->zfp", attended, keep_w, preferred_element_type=jnp.float32)
    send = jnp.einsum("pe,ezf->zfp", attended, send_w, preferred_element_type=jnp.float32)
    pair = [(i, i ^ 1) for i in range(ncore)]
    half = (
        keep.astype(jnp.bfloat16).astype(jnp.float32)
        + lax.ppermute(send.astype(jnp.bfloat16), "core", pair).astype(jnp.float32)
    ).astype(jnp.bfloat16)
    mixed = a2a_sum(half, "z")
    own_cols = lax.dynamic_slice_in_dim(patches, lax.axis_index(TP) * width, width, 1)
    visual = (mixed + own_cols.astype(jnp.float32).T).astype(jnp.bfloat16)
    windows = visual.reshape(width, merged_count, 4)
    partial_rows = jnp.einsum(
        "cmk,kce->me", windows, merge_weight, preferred_element_type=jnp.float32
    ).astype(jnp.bfloat16)
    ntp = nz * ncore
    merged = a2a_gather(
        a2a_sum(partial_rows.reshape(ntp, merged_count // ntp, -1), TP).astype(jnp.bfloat16), TP
    )

    mnorm = normalize_shifted(merged.astype(jnp.float32), dec_gain, dec_bias).astype(jnp.bfloat16)
    mproj = jnp.einsum("td,sde->ste", mnorm, dec_qkv, preferred_element_type=jnp.float32).astype(
        jnp.bfloat16
    )
    merged_kv = grp_gather(jnp.concatenate([mproj[1], mproj[2]], axis=1))

    query_pos = jnp.concatenate([own_text_pos, positions], axis=0)
    block = positions // tok
    seen = jnp.sum(
        ((all_pos[None, :] >= (block * tok)[:, None]) & (all_pos[None, :] <= positions[:, None])).astype(
            jnp.int32
        ),
        axis=1,
    )
    merged_limit = block * text_count + (positions - block * tok + 1 - seen)
    text_limit = here * text_count + jnp.arange(text_count, dtype=jnp.int32) + 1
    key_row = jnp.arange(groups * (text_count + pad_rows), dtype=jnp.int32)
    key_grp = key_row // (text_count + pad_rows)
    key_in = key_row % (text_count + pad_rows)
    text_key = jnp.where(key_in < text_count, key_grp * text_count + key_in, groups * tok)
    text_keys, text_values = text_kv[:, :DH], text_kv[:, DH:]
    part_tt = attend_part(tproj[0], text_key[None, :] < text_limit[:, None], text_keys, text_values)
    part_mt = attend_part(mproj[0], text_key[None, :] < merged_limit[:, None], text_keys, text_values)
    part_t = [jnp.concatenate([a, b], axis=0) for a, b in zip(part_tt, part_mt)]
    top_t, total_t, acc_t = part_t
    dquery = jnp.concatenate([tproj[0], mproj[0]], axis=0)
    top_m, total_m, acc_m = attend_part(
        dquery, all_pos[None, :] <= query_pos[:, None], merged_kv[:, :DH], merged_kv[:, DH:]
    )
    best = jnp.maximum(top_t, top_m)
    scale_t = jnp.exp(top_t - best)
    scale_m = jnp.exp(top_m - best)
    total = total_t * scale_t + total_m * scale_m
    acc = acc_t * scale_t[:, None] + acc_m * scale_m[:, None]
    result = (acc / total[:, None]).astype(jnp.bfloat16)
    text_out = result[:text_count]
    merged_out = result[text_count:]

    target = positions // tok
    member = (target[:, None] == jnp.arange(groups, dtype=jnp.int32)[None, :]).astype(jnp.int32)
    rank = jnp.sum(jnp.cumsum(member, axis=0) * member, axis=1) - 1
    slot = target * cap + rank
    select = slot[None, :] == jnp.arange(groups * cap, dtype=jnp.int32)[:, None]
    packed = jnp.dot(
        select.astype(jnp.bfloat16), merged_out, preferred_element_type=jnp.float32
    ).astype(jnp.bfloat16)
    got = lax.all_to_all(packed, GRP, 0, 0, tiled=True)

    src_pos = all_pos.reshape(groups, merged_count)
    to_me = (src_pos // tok) == here
    src_rank = jnp.cumsum(to_me.astype(jnp.int32), axis=1) - 1
    slot_hit = to_me[:, :, None] & (
        src_rank[:, :, None] == jnp.arange(cap, dtype=jnp.int32)[None, None, :]
    )
    got_pos = jnp.sum(jnp.where(slot_hit, src_pos[:, :, None] + 1, 0), axis=1).reshape(-1) - 1
    local = got_pos - here * tok
    landing = (local[None, :] == place[:, None]) & (got_pos[None, :] >= 0)
    text_land = own_text_pos[None, :] - here * tok == place[:, None]
    out = jnp.dot(landing.astype(jnp.bfloat16), got, preferred_element_type=jnp.float32)
    out = out + jnp.dot(
        text_land.astype(jnp.bfloat16), text_out, preferred_element_type=jnp.float32
    )
    return out.astype(jnp.bfloat16)


def solution(mesh):
    grid = mesh.devices.reshape(4, mesh.devices.shape[0] // 4, mesh.devices.shape[1] // 2, 2)
    mesh4 = Mesh(grid, GRP + TP)
    in_specs = (
        P(GRP, None),
        P(GRP),
        P(),
        P(),
        P(None, None, TP),
        P(TP, None),
        P(None, TP, None),
        P(GRP),
        P(GRP, None),
        P(),
        P(),
        P(None, None, TP),
    )
    out_specs = P(GRP, TP)
    return jax.shard_map(body, mesh=mesh4, in_specs=in_specs, out_specs=out_specs, check_vma=False)
```

```python
import jax
import jax.numpy as jnp
from jax import lax
from jax.sharding import Mesh
from jax.sharding import PartitionSpec as P

HD = 104
DH = 64

layer_eps = 1e-05

GRP = ("gx", "gy")
TP = ("z", "core")


def normalize(values, gain, bias):
    mean = jnp.mean(values, axis=-1, keepdims=True)
    centred = values - mean
    spread = jnp.mean(centred * centred, axis=-1, keepdims=True)
    return centred * lax.rsqrt(spread + layer_eps) * gain + bias


def normalize_shifted(values, gain, bias):
    shift = values[:, :1]
    moved = values - shift
    first = jnp.mean(moved, axis=-1, keepdims=True)
    second = jnp.mean(moved * moved, axis=-1, keepdims=True)
    spread = jnp.maximum(second - first * first, 0.0)
    return (moved - first) * lax.rsqrt(spread + layer_eps) * gain + bias


def a2a_gather(value, axis):
    n = lax.axis_size(axis)
    spread = jnp.broadcast_to(value[None], (n,) + value.shape)
    got = lax.all_to_all(spread, axis, 0, 0, tiled=True)
    return got.reshape((n * value.shape[0],) + value.shape[1:])


def grp_gather(value):
    return a2a_gather(a2a_gather(value, "gy"), "gx")


def a2a_sum(parts, axis):
    got = lax.all_to_all(parts, axis, 0, 0, tiled=True)
    return jnp.sum(got.astype(jnp.float32), axis=0)


def attend_part(query, allowed, keys, values):
    score = jnp.dot(query, keys.T, preferred_element_type=jnp.float32) * DH ** (-0.5)
    top = jnp.max(jnp.where(allowed, score, -1e30), axis=1)
    expo = jnp.where(allowed, jnp.exp(score - top[:, None]), 0.0).astype(jnp.bfloat16)
    total = jnp.sum(expo.astype(jnp.float32), axis=1)
    acc = jnp.dot(expo, values, preferred_element_type=jnp.float32)
    return top, total, acc


def body(
    patches,
    patch_image,
    vis_gain,
    vis_bias,
    vis_qkv,
    vis_out,
    merge_weight,
    positions,
    text,
    dec_gain,
    dec_bias,
    dec_qkv,
):
    groups = lax.axis_size(GRP)
    here = lax.axis_index(GRP)
    rows = patches.shape[0]
    merged_count = rows // 4
    text_count = text.shape[0]
    tok = text_count + merged_count
    cap = merged_count // min(groups, 16)

    tnorm = normalize_shifted(text.astype(jnp.float32), dec_gain, dec_bias).astype(jnp.bfloat16)
    tproj = jnp.einsum("td,sde->ste", tnorm, dec_qkv, preferred_element_type=jnp.float32).astype(
        jnp.bfloat16
    )
    digit = 128
    pad_rows = 8
    lanes = 2 * DH
    pos_rows = jnp.stack([positions // digit, positions % digit]).astype(jnp.bfloat16)
    extra = jnp.zeros((pad_rows, lanes), jnp.bfloat16).at[:2].set(pos_rows.reshape(2, lanes))
    payload = jnp.concatenate([jnp.concatenate([tproj[1], tproj[2]], axis=1), extra], axis=0)
    text_kv = lax.all_gather(payload, GRP, axis=0, tiled=True)
    digits = text_kv.reshape(groups, text_count + pad_rows, lanes)[:, text_count : text_count + 2]
    digits = digits.astype(jnp.int32)
    all_pos = (digits[:, 0] * digit + digits[:, 1]).reshape(-1)

    place = jnp.arange(tok, dtype=jnp.int32)
    flags = jnp.sum((all_pos[None, :] == (here * tok + place)[:, None]).astype(jnp.int32), axis=1)
    free = 1 - flags
    text_rank = jnp.cumsum(free) - 1
    pick = (free[:, None] == 1) & (text_rank[:, None] == jnp.arange(text_count, dtype=jnp.int32)[None, :])
    own_text_pos = jnp.sum(jnp.where(pick, place[:, None], 0), axis=0) + here * tok

    heads = vis_qkv.shape[2] // HD
    patches_f = patches.astype(jnp.float32)
    normed = normalize_shifted(patches_f, vis_gain, vis_bias).astype(jnp.bfloat16)
    proj = jnp.einsum("pd,sde->spe", normed, vis_qkv, preferred_element_type=jnp.float32).astype(
        jnp.bfloat16
    )
    query = proj[0].reshape(rows, heads, HD)
    swap = [(i, i ^ 1) for i in range(lax.axis_size("gy"))]
    partner_kv, partner_ids = lax.ppermute((proj[1:], patch_image), "gy", swap)
    both_kv = jnp.concatenate([proj[1:], partner_kv], axis=1)
    both_ids = jnp.concatenate([patch_image, partner_ids], axis=0)
    keys = both_kv[0].reshape(2 * rows, heads, HD)
    values = both_kv[1].reshape(2 * rows, heads, HD)
    scores = jnp.einsum("phe,khe->hpk", query, keys, preferred_element_type=jnp.float32) * HD ** (
        -0.5
    )
    same = patch_image[:, None] == both_ids[None, :]
    top = jnp.max(jnp.where(same, scores, -1e30), axis=2, keepdims=True)
    expo = jnp.where(same, jnp.exp(scores - top), 0.0)
    weights = (expo / jnp.sum(expo, axis=2, keepdims=True)).astype(jnp.bfloat16)
    attended = jnp.einsum(
        "hpk,khe->phe", weights, values, preferred_element_type=jnp.float32
    ).astype(jnp.bfloat16)
    attended = attended.reshape(rows, heads * HD)

    nz = lax.axis_size("z")
    ncore = lax.axis_size("core")
    width = patches.shape[1] // (nz * ncore)
    core = lax.axis_index("core")
    vo = vis_out.reshape(vis_out.shape[0], nz, ncore, width)
    keep_w = lax.dynamic_index_in_dim(vo, core, 2, keepdims=False)
    send_w = lax.dynamic_index_in_dim(vo, 1 - core, 2, keepdims=False)
    keep = jnp.einsum("pe,ezf->zfp", attended, keep_w, preferred_element_type=jnp.float32)
    send = jnp.einsum("pe,ezf->zfp", attended, send_w, preferred_element_type=jnp.float32)
    pair = [(i, i ^ 1) for i in range(ncore)]
    half = (
        keep.astype(jnp.bfloat16).astype(jnp.float32)
        + lax.ppermute(send.astype(jnp.bfloat16), "core", pair).astype(jnp.float32)
    ).astype(jnp.bfloat16)
    mixed = a2a_sum(half, "z")
    own_cols = lax.dynamic_slice_in_dim(patches, lax.axis_index(TP) * width, width, 1)
    visual = (mixed + own_cols.astype(jnp.float32).T).astype(jnp.bfloat16)
    windows = visual.reshape(width, merged_count, 4)
    partial_rows = jnp.einsum(
        "cmk,kce->me", windows, merge_weight, preferred_element_type=jnp.float32
    ).astype(jnp.bfloat16)
    ntp = nz * ncore
    merged = a2a_gather(
        a2a_sum(partial_rows.reshape(ntp, merged_count // ntp, -1), TP).astype(jnp.bfloat16), TP
    )

    mnorm = normalize_shifted(merged.astype(jnp.float32), dec_gain, dec_bias).astype(jnp.bfloat16)
    mproj = jnp.einsum("td,sde->ste", mnorm, dec_qkv, preferred_element_type=jnp.float32).astype(
        jnp.bfloat16
    )
    merged_kv = grp_gather(jnp.concatenate([mproj[1], mproj[2]], axis=1))

    query_pos = jnp.concatenate([own_text_pos, positions], axis=0)
    block = positions // tok
    seen = jnp.sum(
        ((all_pos[None, :] >= (block * tok)[:, None]) & (all_pos[None, :] <= positions[:, None])).astype(
            jnp.int32
        ),
        axis=1,
    )
    merged_limit = block * text_count + (positions - block * tok + 1 - seen)
    text_limit = here * text_count + jnp.arange(text_count, dtype=jnp.int32) + 1
    key_row = jnp.arange(groups * (text_count + pad_rows), dtype=jnp.int32)
    key_grp = key_row // (text_count + pad_rows)
    key_in = key_row % (text_count + pad_rows)
    text_key = jnp.where(key_in < text_count, key_grp * text_count + key_in, groups * tok)
    text_keys, text_values = text_kv[:, :DH], text_kv[:, DH:]
    part_tt = attend_part(tproj[0], text_key[None, :] < text_limit[:, None], text_keys, text_values)
    part_mt = attend_part(mproj[0], text_key[None, :] < merged_limit[:, None], text_keys, text_values)
    part_t = [jnp.concatenate([a, b], axis=0) for a, b in zip(part_tt, part_mt)]
    top_t, total_t, acc_t = part_t
    dquery = jnp.concatenate([tproj[0], mproj[0]], axis=0)
    top_m, total_m, acc_m = attend_part(
        dquery, all_pos[None, :] <= query_pos[:, None], merged_kv[:, :DH], merged_kv[:, DH:]
    )
    best = jnp.maximum(top_t, top_m)
    scale_t = jnp.exp(top_t - best)
    scale_m = jnp.exp(top_m - best)
    total = total_t * scale_t + total_m * scale_m
    acc = acc_t * scale_t[:, None] + acc_m * scale_m[:, None]
    result = (acc / total[:, None]).astype(jnp.bfloat16)
    text_out = result[:text_count]
    merged_out = result[text_count:]

    target = positions // tok
    member = (target[:, None] == jnp.arange(groups, dtype=jnp.int32)[None, :]).astype(jnp.int32)
    rank = jnp.sum(jnp.cumsum(member, axis=0) * member, axis=1) - 1
    slot = target * cap + rank
    select = slot[None, :] == jnp.arange(groups * cap, dtype=jnp.int32)[:, None]
    packed = jnp.dot(
        select.astype(jnp.bfloat16), merged_out, preferred_element_type=jnp.float32
    ).astype(jnp.bfloat16)
    got = lax.all_to_all(packed, GRP, 0, 0, tiled=True)

    src_pos = all_pos.reshape(groups, merged_count)
    to_me = (src_pos // tok) == here
    src_rank = jnp.cumsum(to_me.astype(jnp.int32), axis=1) - 1
    slot_hit = to_me[:, :, None] & (
        src_rank[:, :, None] == jnp.arange(cap, dtype=jnp.int32)[None, None, :]
    )
    got_pos = jnp.sum(jnp.where(slot_hit, src_pos[:, :, None] + 1, 0), axis=1).reshape(-1) - 1
    local = got_pos - here * tok
    landing = (local[None, :] == place[:, None]) & (got_pos[None, :] >= 0)
    text_land = own_text_pos[None, :] - here * tok == place[:, None]
    out = jnp.dot(landing.astype(jnp.bfloat16), got, preferred_element_type=jnp.float32)
    out = out + jnp.dot(
        text_land.astype(jnp.bfloat16), text_out, preferred_element_type=jnp.float32
    )
    return out.astype(jnp.bfloat16)


def solution(mesh):
    grid = mesh.devices.reshape(4, mesh.devices.shape[0] // 4, mesh.devices.shape[1] // 2, 2)
    mesh4 = Mesh(grid, GRP + TP)
    in_specs = (
        P(GRP, None),
        P(GRP),
        P(),
        P(),
        P(None, None, TP),
        P(TP, None),
        P(None, TP, None),
        P(GRP),
        P(GRP, None),
        P(),
        P(),
        P(None, None, TP),
    )
    out_specs = P(GRP, TP)
    return jax.shard_map(body, mesh=mesh4, in_specs=in_specs, out_specs=out_specs, check_vma=False)
```
